32 devices in a mesh: node: 8 (over z, y), head: 4 (over x, core).
Axes of the slice: x: 2, y: 2, z: 4, core: 2. Of those that a mesh axis runs over, the one named last changes fastest.
Arguments:
- node_states: bfloat16 [3072, 1024], P('node'), may hold values from -12 to 12
- w_qkv: bfloat16 [1024, 3, 1024], P(None, None, 'head'), may hold values from -1 to 1
- w_out: bfloat16 [1024, 1024], P('head'), may hold values from -4 to 4
- ln_gain: float32 [1024], P('head'), may hold values from 0.5 to 1.5
- ln_bias: float32 [1024], P('head'), may hold values from -4 to 4
- local_mask: int32 [24, 7], P('node'), may hold values 0 or 1
- matchings: int32 [4, 24], P(None, 'node'), may hold values from 0 to 23, as said below
Outputs:
- layer_out: bfloat16 [3072, 1024], P('node', 'head')
The draws below stay inside these ranges and needn't reach their ends.
Inputs may be any that keep to these rules, and one draw needn't show every extreme that they name: Each row of matchings is a perfect matching of the 24 blocks: matchings[m, matchings[m, b]] = b and matchings[m, b] differs from b. The blocks fall into groups of 3 consecutive blocks, and the number of groups is a power of two; for each m there is one number s_m, 1 <= s_m < 8, such that every block of group g is matched with a block of group g XOR s_m.
All inputs are finite; a program needn't handle non-finite values. No bound on the sum of `local_mask` on one device may be relied on, other than what follows from the above.
Results may differ from the reference program's by a relative error of at most 0.0077.
Values may be sent and summed in bfloat16 or wider, within the bound.
No kernel may reach another device: no remote copies, remote signals or barrier semaphores. Data moves between devices by JAX's collectives and lax.ppermute only.
A program may use at most 64 MiB of HBM per device.

```python
import math
import jax
import jax.numpy as jnp
from jax import lax

D = 1024
HEADS = 16
HEAD_DIM = 64
ROWS = 128
REACH = 3
MATCHES = 4
BLK_DEV = 3
WIN = 7
BLOCKS = 24
NODES = 3072


def draw_node_states(key, part):
    shape = (NODES, D)
    value = jax.random.truncated_normal(jax.random.fold_in(key, 1), -5.0, 5.0, shape, jnp.float32)
    return value.astype(jnp.bfloat16)


def draw_w_qkv(key, part):
    shape = (D, HEADS * HEAD_DIM)
    query_part = jax.random.truncated_normal(jax.random.fold_in(key, 1), -5.0, 5.0, shape, jnp.float32)
    noise_part = jax.random.truncated_normal(jax.random.fold_in(key, 2), -5.0, 5.0, shape, jnp.float32)
    value_part = jax.random.truncated_normal(jax.random.fold_in(key, 3), -5.0, 5.0, shape, jnp.float32)
    key_part = noise_part
    stacked = jnp.stack([query_part, key_part, value_part], axis=1) * D ** (-0.5)
    return stacked.astype(jnp.bfloat16)


def one_matching(sub_key):
    groups = BLOCKS // BLK_DEV
    shift_key = jax.random.fold_in(sub_key, 1)
    perm_key = jax.random.fold_in(sub_key, 2)
    shift_val = jax.random.randint(shift_key, (), 1, groups)
    perms = jax.vmap(lambda one_key: jax.random.permutation(one_key, BLK_DEV))(jax.random.split(perm_key, groups))
    inverse = jnp.argsort(perms, axis=1)
    group_ids = jnp.arange(groups)[:, None]
    other = jnp.bitwise_xor(group_ids, shift_val)
    lower = group_ids < other
    local_pos = jnp.where(lower, perms, jnp.take(inverse, other[:, 0], axis=0))
    return (other * BLK_DEV + local_pos).reshape(BLOCKS).astype(jnp.int32)


def draw_matchings(key, part):
    rows_list = [one_matching(jax.random.fold_in(key, 10 + match_pos)) for match_pos in range(MATCHES)]
    return jnp.stack(rows_list, axis=0)


def set_ends(values, key, low, high):
    longest = values.shape.index(max(values.shape))
    spots = []
    for shift in (0, 1):
        where = [jax.random.randint(jax.random.fold_in(key, axis), (), 0, length) for axis, length in enumerate(values.shape)]
        where[longest] = (where[longest] + shift) % values.shape[longest]
        spots.append(tuple(where))
    return values.at[spots[0]].set(low).at[spots[1]].set(high)


def steps_of(stream_key, shape, cuts, least, high):
    loudness, own = 1.0, jax.random.fold_in(stream_key, 6)
    for position, blocks in cuts:
        draws = jnp.exp(jax.random.uniform(jax.random.fold_in(own, position), (blocks,), jnp.float32, least / len(cuts), high / len(cuts)))
        loudness = loudness * jnp.repeat(draws, shape[position] // blocks).reshape([-1 if axis == position else 1 for axis in range(len(shape))])
    return loudness


def centred(stream_key, shape, scale, limit, pieces=(), held_as=jnp.bfloat16):
    drawn = scale * jax.random.normal(stream_key, shape, jnp.float32)
    if pieces:
        drawn = drawn * steps_of(stream_key, shape, pieces, -0.22, 0.18)
    return jnp.clip(drawn, -limit, limit).astype(held_as)


def setup_inputs(seed: int = 0) -> dict:
    key_of = jax.random.split(jax.random.key(seed), 8)
    return {
        "node_states": draw_node_states(jax.random.fold_in(key_of[7], 71), 0),
        "w_qkv": draw_w_qkv(jax.random.fold_in(key_of[7], 71), 0),
        "w_out": centred(key_of[2], (HEADS * HEAD_DIM, D), 0.3, 4.0, ((0, 4),)),
        "ln_gain": jnp.clip(1.0 + 0.1 * jax.random.normal(key_of[3], (D,), jnp.float32), 0.5, 1.5),
        "ln_bias": centred(key_of[4], (D,), 0.5, 4.0, ((0, 4),), jnp.float32),
        "local_mask": set_ends((jax.random.randint(key_of[5], (BLOCKS, WIN), 0, 2) < 1).astype(jnp.int32), jax.random.fold_in(key_of[5], 1), 0, 1),
        "matchings": draw_matchings(jax.random.fold_in(key_of[7], 71), 0),
    }


def reference(node_states, w_qkv, w_out, ln_gain, ln_bias, local_mask, matchings):
    inv_root = 1.0 / math.sqrt(HEAD_DIM)
    model_width = node_states.shape[1]
    head_feats = HEADS * HEAD_DIM
    projected = jnp.dot(node_states, w_qkv.reshape(model_width, 3 * head_feats), preferred_element_type=jnp.float32).astype(jnp.bfloat16)
    projected = projected.reshape(BLOCKS, ROWS, 3, head_feats)
    query_blocks = projected[:, :, 0]
    key_blocks = projected[:, :, 1]
    value_blocks = projected[:, :, 2]
    offsets = jnp.arange(2 * REACH + 1, dtype=jnp.int32) - REACH

    def one_block(block_id):
        neighbour = block_id + offsets
        local_ok = (neighbour >= 0) & (neighbour < BLOCKS) & ((offsets == 0) | (local_mask[block_id] == 1))
        chosen = jnp.concatenate([jnp.clip(neighbour, 0, BLOCKS - 1).astype(jnp.int32), matchings[:, block_id].astype(jnp.int32)])
        block_ok = jnp.concatenate([local_ok, jnp.ones((MATCHES,), dtype=bool)])
        row_ok = jnp.repeat(block_ok, ROWS)
        key_part = jnp.take(key_blocks, chosen, axis=0).reshape(-1, HEADS, HEAD_DIM).astype(jnp.float32)
        value_part = jnp.take(value_blocks, chosen, axis=0).reshape(-1, HEADS, HEAD_DIM).astype(jnp.float32)
        query_part = query_blocks[block_id].reshape(ROWS, HEADS, HEAD_DIM).astype(jnp.float32)
        scores = jnp.einsum('qhd,khd->hqk', query_part, key_part) * inv_root
        scores = jnp.where(row_ok[None, None, :], scores, -jnp.inf)
        highest = lax.optimization_barrier(jnp.max(scores, axis=-1, keepdims=True))
        weights = jnp.exp(scores - highest)
        weights = (weights / lax.optimization_barrier(jnp.sum(weights, axis=-1, keepdims=True))).astype(jnp.bfloat16)
        context = jnp.einsum('hqk,khd->qhd', weights.astype(jnp.float32), value_part)
        return context.astype(jnp.bfloat16).reshape(ROWS, head_feats)
    context = lax.map(one_block, jnp.arange(BLOCKS, dtype=jnp.int32)).reshape(NODES, head_feats)
    mixed_rows = node_states.astype(jnp.float32) + jnp.dot(context, w_out, preferred_element_type=jnp.float32)
    centre = lax.optimization_barrier(jnp.mean(mixed_rows, axis=1, keepdims=True))
    deviation = mixed_rows - centre
    spread = lax.optimization_barrier(jnp.mean(jnp.square(deviation), axis=1, keepdims=True))
    normed = deviation * lax.rsqrt(spread + 1e-05)
    return (normed * ln_gain + ln_bias).astype(jnp.bfloat16)
```

```python
import math

import jax
import jax.numpy as jnp
from jax import lax
from jax.sharding import PartitionSpec as P

HEAD_DIM = 64
ROWS = 128
REACH = 3
GATHER_GROUPS = 16


NORM_EPS = 1e-05


def partner(array, axis, bit):
    return lax.ppermute(array, axis, [(i, i ^ 1 << bit) for i in range(lax.axis_size(axis))])


def with_halo(array, sides, width):
    for axis, dim in sides:
        devices, length = (lax.axis_size(axis), array.shape[dim])
        up = [(i, (i + 1) % devices) for i in range(devices - 1)]
        down = [(j, i) for i, j in up]
        last = lax.slice_in_dim(array, length - width, length, axis=dim)
        first = lax.slice_in_dim(array, 0, width, axis=dim)
        before = lax.ppermute(last, axis, up)
        after = lax.ppermute(first, axis, down)
        array = jnp.concatenate([before, array, after], axis=dim)
    return array


def keep_same(current):
    return current


def route_direct(payload, shift_val, digits):
    for bit_pos in range(digits):

        def moved(current, bit_pos=bit_pos):
            return partner(current, "node", bit_pos)

        taken = jnp.bitwise_and(jnp.right_shift(shift_val, bit_pos), 1) == 1
        payload = lax.cond(taken, moved, keep_same, payload)
    return payload


def select_partner(received, matchings, blocks_here, pair_feats):
    matches = matchings.shape[0]
    received = received.reshape(matches, blocks_here, ROWS, pair_feats)
    sources = matchings % blocks_here
    selector = (sources[:, :, None] == jnp.arange(blocks_here)[None, None, :]).astype(jnp.bfloat16)
    picked = jnp.einsum("mjs,msrf->mjrf", selector, received, preferred_element_type=jnp.float32)
    return picked.astype(jnp.bfloat16)


def routed_keys(keyvals, matchings, my_index, groups, blocks_here, window):
    total_rows, pair_feats = keyvals.shape
    matches = matchings.shape[0]
    digits = groups.bit_length() - 1
    padded = with_halo(keyvals, (("node", 0),), REACH * ROWS)
    windows = jnp.stack(
        [padded[block_pos * ROWS : (block_pos + window) * ROWS] for block_pos in range(blocks_here)]
    )
    targets = jnp.bitwise_xor(matchings[:, 0] // blocks_here, my_index)
    received = jnp.stack(
        [route_direct(keyvals, targets[match_pos], digits) for match_pos in range(matches)]
    )
    partner_blocks = select_partner(received, matchings, blocks_here, pair_feats)
    partner_rows = jnp.transpose(partner_blocks, (1, 0, 2, 3)).reshape(
        blocks_here, matches * ROWS, pair_feats
    )
    return jnp.concatenate([windows, partner_rows], axis=1)


def gathered_keys(keyvals, chosen):
    total_rows, pair_feats = keyvals.shape
    blocks_here, key_blocks = chosen.shape
    everyone = lax.all_gather(keyvals, "node", axis=0, tiled=True)
    everyone = everyone.reshape(-1, ROWS, pair_feats)
    picked = jnp.take(everyone, chosen.reshape(-1), axis=0, mode="clip")
    return picked.reshape(blocks_here, key_blocks * ROWS, pair_feats)


def local(node_states, w_qkv, w_out, ln_gain, ln_bias, local_mask, matchings):
    total_rows, model_width = node_states.shape
    blocks_here = total_rows // ROWS
    head_feats = w_qkv.shape[2]
    heads_here = head_feats // HEAD_DIM
    window = 2 * REACH + 1
    matches = matchings.shape[0]
    inv_root = 1.0 / math.sqrt(HEAD_DIM)
    my_index = lax.axis_index("node")
    groups = lax.axis_size("node")
    all_blocks = groups * blocks_here
    w_full = lax.all_gather(w_out, "head", axis=0, tiled=True)
    projected = jnp.einsum(
        "nd,dtf->ntf", node_states, w_qkv, preferred_element_type=jnp.float32
    ).astype(jnp.bfloat16)
    queries = projected[:, 0]
    keyvals = projected[:, 1:].reshape(total_rows, 2 * head_feats)
    global_blocks = my_index * blocks_here + jnp.arange(blocks_here, dtype=jnp.int32)
    offsets = jnp.arange(window, dtype=jnp.int32) - REACH
    neighbour = global_blocks[:, None] + offsets[None, :]
    if groups <= GATHER_GROUPS:
        chosen = jnp.concatenate(
            [jnp.clip(neighbour, 0, all_blocks - 1), jnp.transpose(matchings)], axis=1
        )
        key_rows = gathered_keys(keyvals, chosen)
    else:
        key_rows = routed_keys(keyvals, matchings, my_index, groups, blocks_here, window)
    key_count = key_rows.shape[1]
    key_part = key_rows[:, :, :head_feats].reshape(blocks_here, key_count, heads_here, HEAD_DIM)
    value_part = key_rows[:, :, head_feats:].reshape(blocks_here, key_count, heads_here, HEAD_DIM)
    query_blocks = queries.reshape(blocks_here, ROWS, heads_here, HEAD_DIM)
    local_ok = (
        (neighbour >= 0) & (neighbour < all_blocks) & ((offsets[None, :] == 0) | (local_mask == 1))
    )
    block_ok = jnp.concatenate([local_ok, jnp.ones((blocks_here, matches), dtype=bool)], axis=1)
    row_ok = jnp.repeat(block_ok, ROWS, axis=1)
    scores = (
        jnp.einsum("bqhd,bkhd->bhqk", query_blocks, key_part, preferred_element_type=jnp.float32)
        * inv_root
    )
    scores = jnp.where(row_ok[:, None, None, :], scores, -jnp.inf)
    highest = jnp.max(scores, axis=-1, keepdims=True)
    weights = jnp.exp(scores - highest)
    weights = (weights / jnp.sum(weights, axis=-1, keepdims=True)).astype(jnp.bfloat16)
    context = jnp.einsum("bhqk,bkhd->bqhd", weights, value_part, preferred_element_type=jnp.float32)
    context = context.astype(jnp.bfloat16).reshape(total_rows, head_feats)
    context_full = lax.all_gather(context, "head", axis=1, tiled=True)
    mixed_rows = node_states.astype(jnp.float32) + jnp.dot(
        context_full, w_full, preferred_element_type=jnp.float32
    )
    centre = jnp.mean(mixed_rows, axis=1, keepdims=True)
    deviation = mixed_rows - centre
    spread = jnp.mean(jnp.square(deviation), axis=1, keepdims=True)
    normed = deviation * lax.rsqrt(spread + NORM_EPS)
    out_cols = ln_gain.shape[0]
    col_start = lax.axis_index("head") * out_cols
    own_rows = lax.dynamic_slice_in_dim(normed, col_start, out_cols, 1)
    return (own_rows * ln_gain + ln_bias).astype(jnp.bfloat16)


def solution(mesh):
    placed = (
        P("node", None),
        P(None, None, "head"),
        P("head", None),
        P("head"),
        P("head"),
        P("node", None),
        P(None, "node"),
    )
    return jax.shard_map(
        local, mesh=mesh, in_specs=placed, out_specs=P("node", "head"), check_vma=False
    )
```

```python
import math

import jax
import jax.numpy as jnp
from jax import lax
from jax.sharding import PartitionSpec as P

HEAD_DIM = 64
ROWS = 128
REACH = 3
GATHER_GROUPS = 16


NORM_EPS = 1e-05


def partner(array, axis, bit):
    return lax.ppermute(array, axis, [(i, i ^ 1 << bit) for i in range(lax.axis_size(axis))])


def with_halo(array, sides, width):
    for axis, dim in sides:
        devices, length = (lax.axis_size(axis), array.shape[dim])
        up = [(i, (i + 1) % devices) for i in range(devices - 1)]
        down = [(j, i) for i, j in up]
        last = lax.slice_in_dim(array, length - width, length, axis=dim)
        first = lax.slice_in_dim(array, 0, width, axis=dim)
        before = lax.ppermute(last, axis, up)
        after = lax.ppermute(first, axis, down)
        array = jnp.concatenate([before, array, after], axis=dim)
    return array


def keep_same(current):
    return current


def route_direct(payload, shift_val, digits):
    for bit_pos in range(digits):

        def moved(current, bit_pos=bit_pos):
            return partner(current, "node", bit_pos)

        taken = jnp.bitwise_and(jnp.right_shift(shift_val, bit_pos), 1) == 1
        payload = lax.cond(taken, moved, keep_same, payload)
    return payload


def select_partner(received, matchings, blocks_here, pair_feats):
    matches = matchings.shape[0]
    received = received.reshape(matches, blocks_here, ROWS, pair_feats)
    sources = matchings % blocks_here
    selector = (sources[:, :, None] == jnp.arange(blocks_here)[None, None, :]).astype(jnp.bfloat16)
    picked = jnp.einsum("mjs,msrf->mjrf", selector, received, preferred_element_type=jnp.float32)
    return picked.astype(jnp.bfloat16)


def routed_keys(keyvals, matchings, my_index, groups, blocks_here, window):
    total_rows, pair_feats = keyvals.shape
    matches = matchings.shape[0]
    digits = groups.bit_length() - 1
    padded = with_halo(keyvals, (("node", 0),), REACH * ROWS)
    windows = jnp.stack(
        [padded[block_pos * ROWS : (block_pos + window) * ROWS] for block_pos in range(blocks_here)]
    )
    targets = jnp.bitwise_xor(matchings[:, 0] // blocks_here, my_index)
    received = jnp.stack(
        [route_direct(keyvals, targets[match_pos], digits) for match_pos in range(matches)]
    )
    partner_blocks = select_partner(received, matchings, blocks_here, pair_feats)
    partner_rows = jnp.transpose(partner_blocks, (1, 0, 2, 3)).reshape(
        blocks_here, matches * ROWS, pair_feats
    )
    return jnp.concatenate([windows, partner_rows], axis=1)


def switched_send(payload, shift_val, groups):
    def branch(shift):
        def moved(current):
            return lax.ppermute(current, "node", [(i, i ^ shift) for i in range(groups)])

        return moved

    branches = [branch(shift) for shift in range(1, groups)]
    return lax.switch(jnp.clip(shift_val - 1, 0, groups - 2), branches, payload)


def switched_keys(keyvals, matchings, my_index, groups, blocks_here, window):
    total_rows, pair_feats = keyvals.shape
    matches = matchings.shape[0]
    padded = with_halo(keyvals, (("node", 0),), REACH * ROWS)
    windows = jnp.stack(
        [padded[block_pos * ROWS : (block_pos + window) * ROWS] for block_pos in range(blocks_here)]
    )
    targets = jnp.bitwise_xor(matchings[:, 0] // blocks_here, my_index)
    picked = []
    for match_pos in range(matches):
        received = switched_send(keyvals, targets[match_pos], groups)
        received = received.reshape(blocks_here, ROWS, pair_feats)
        picked.append(jnp.take(received, matchings[match_pos] % blocks_here, axis=0, mode="clip"))
    partner_rows = jnp.stack(picked, axis=1).reshape(blocks_here, matches * ROWS, pair_feats)
    return jnp.concatenate([windows, partner_rows], axis=1)


def gathered_keys(keyvals, chosen):
    total_rows, pair_feats = keyvals.shape
    blocks_here, key_blocks = chosen.shape
    everyone = lax.all_gather(keyvals, "node", axis=0, tiled=True)
    everyone = everyone.reshape(-1, ROWS, pair_feats)
    picked = jnp.take(everyone, chosen.reshape(-1), axis=0, mode="clip")
    return picked.reshape(blocks_here, key_blocks * ROWS, pair_feats)


def local(node_states, w_qkv, w_out, ln_gain, ln_bias, local_mask, matchings):
    total_rows, model_width = node_states.shape
    blocks_here = total_rows // ROWS
    head_feats = w_qkv.shape[2]
    heads_here = head_feats // HEAD_DIM
    window = 2 * REACH + 1
    matches = matchings.shape[0]
    inv_root = 1.0 / math.sqrt(HEAD_DIM)
    my_index = lax.axis_index("node")
    groups = lax.axis_size("node")
    all_blocks = groups * blocks_here
    w_full = lax.all_gather(w_out, "head", axis=0, tiled=True)
    projected = jnp.einsum(
        "nd,dtf->ntf", node_states, w_qkv, preferred_element_type=jnp.float32
    ).astype(jnp.bfloat16)
    queries = projected[:, 0]
    keyvals = projected[:, 1:].reshape(total_rows, 2 * head_feats)
    global_blocks = my_index * blocks_here + jnp.arange(blocks_here, dtype=jnp.int32)
    offsets = jnp.arange(window, dtype=jnp.int32) - REACH
    neighbour = global_blocks[:, None] + offsets[None, :]
    if groups <= GATHER_GROUPS:
        key_rows = switched_keys(keyvals, matchings, my_index, groups, blocks_here, window)
    else:
        key_rows = routed_keys(keyvals, matchings, my_index, groups, blocks_here, window)
    key_count = key_rows.shape[1]
    key_part = key_rows[:, :, :head_feats].reshape(blocks_here, key_count, heads_here, HEAD_DIM)
    value_part = key_rows[:, :, head_feats:].reshape(blocks_here, key_count, heads_here, HEAD_DIM)
    query_blocks = queries.reshape(blocks_here, ROWS, heads_here, HEAD_DIM)
    local_ok = (
        (neighbour >= 0) & (neighbour < all_blocks) & ((offsets[None, :] == 0) | (local_mask == 1))
    )
    block_ok = jnp.concatenate([local_ok, jnp.ones((blocks_here, matches), dtype=bool)], axis=1)
    row_ok = jnp.repeat(block_ok, ROWS, axis=1)
    scores = (
        jnp.einsum("bqhd,bkhd->bhqk", query_blocks, key_part, preferred_element_type=jnp.float32)
        * inv_root
    )
    scores = jnp.where(row_ok[:, None, None, :], scores, -jnp.inf)
    highest = jnp.max(scores, axis=-1, keepdims=True)
    weights = jnp.exp(scores - highest)
    weights = (weights / jnp.sum(weights, axis=-1, keepdims=True)).astype(jnp.bfloat16)
    context = jnp.einsum("bhqk,bkhd->bqhd", weights, value_part, preferred_element_type=jnp.float32)
    context = context.astype(jnp.bfloat16).reshape(total_rows, head_feats)
    context_full = lax.all_gather(context, "head", axis=1, tiled=True)
    mixed_rows = node_states.astype(jnp.float32) + jnp.dot(
        context_full, w_full, preferred_element_type=jnp.float32
    )
    centre = jnp.mean(mixed_rows, axis=1, keepdims=True)
    deviation = mixed_rows - centre
    spread = jnp.mean(jnp.square(deviation), axis=1, keepdims=True)
    normed = deviation * lax.rsqrt(spread + NORM_EPS)
    out_cols = ln_gain.shape[0]
    col_start = lax.axis_index("head") * out_cols
    own_rows = lax.dynamic_slice_in_dim(normed, col_start, out_cols, 1)
    return (own_rows * ln_gain + ln_bias).astype(jnp.bfloat16)


def solution(mesh):
    placed = (
        P("node", None),
        P(None, None, "head"),
        P("head", None),
        P("head"),
        P("head"),
        P("node", None),
        P(None, "node"),
    )
    return jax.shard_map(
        local, mesh=mesh, in_specs=placed, out_specs=P("node", "head"), check_vma=False
    )
```

```python
import math

import jax
import jax.numpy as jnp
from jax import lax
from jax.sharding import PartitionSpec as P

HEAD_DIM = 64
ROWS = 128
REACH = 3
GATHER_GROUPS = 16


NORM_EPS = 1e-05


def partner(array, axis, bit):
    return lax.ppermute(array, axis, [(i, i ^ 1 << bit) for i in range(lax.axis_size(axis))])


def with_halo(array, sides, width):
    for axis, dim in sides:
        devices, length = (lax.axis_size(axis), array.shape[dim])
        up = [(i, (i + 1) % devices) for i in range(devices - 1)]
        down = [(j, i) for i, j in up]
        last = lax.slice_in_dim(array, length - width, length, axis=dim)
        first = lax.slice_in_dim(array, 0, width, axis=dim)
        before = lax.ppermute(last, axis, up)
        after = lax.ppermute(first, axis, down)
        array = jnp.concatenate([before, array, after], axis=dim)
    return array


def shift_heads(array, step, devices):
    return lax.ppermute(array, "head", [(i, (i + step) % devices) for i in range(devices)])


def keep_same(current):
    return current


def route_direct(payload, shift_val, digits):
    for bit_pos in range(digits):

        def moved(current, bit_pos=bit_pos):
            return partner(current, "node", bit_pos)

        taken = jnp.bitwise_and(jnp.right_shift(shift_val, bit_pos), 1) == 1
        payload = lax.cond(taken, moved, keep_same, payload)
    return payload


def select_partner(received, matchings, blocks_here, pair_feats):
    matches = matchings.shape[0]
    received = received.reshape(matches, blocks_here, ROWS, pair_feats)
    sources = matchings % blocks_here
    selector = (sources[:, :, None] == jnp.arange(blocks_here)[None, None, :]).astype(jnp.bfloat16)
    picked = jnp.einsum("mjs,msrf->mjrf", selector, received, preferred_element_type=jnp.float32)
    return picked.astype(jnp.bfloat16)


def routed_keys(keyvals, matchings, my_index, groups, blocks_here, window):
    total_rows, pair_feats = keyvals.shape
    matches = matchings.shape[0]
    digits = groups.bit_length() - 1
    padded = with_halo(keyvals, (("node", 0),), REACH * ROWS)
    windows = jnp.stack(
        [padded[block_pos * ROWS : (block_pos + window) * ROWS] for block_pos in range(blocks_here)]
    )
    targets = jnp.bitwise_xor(matchings[:, 0] // blocks_here, my_index)
    received = jnp.stack(
        [route_direct(keyvals, targets[match_pos], digits) for match_pos in range(matches)]
    )
    partner_blocks = select_partner(received, matchings, blocks_here, pair_feats)
    partner_rows = jnp.transpose(partner_blocks, (1, 0, 2, 3)).reshape(
        blocks_here, matches * ROWS, pair_feats
    )
    return jnp.concatenate([windows, partner_rows], axis=1)


def switched_send(payload, shift_val, groups):
    def branch(shift):
        def moved(current):
            return lax.ppermute(current, "node", [(i, i ^ shift) for i in range(groups)])

        return moved

    branches = [branch(shift) for shift in range(1, groups)]
    return lax.switch(jnp.clip(shift_val - 1, 0, groups - 2), branches, payload)


def switched_keys(keyvals, matchings, my_index, groups, blocks_here, window):
    total_rows, pair_feats = keyvals.shape
    matches = matchings.shape[0]
    padded = with_halo(keyvals, (("node", 0),), REACH * ROWS)
    windows = jnp.stack(
        [padded[block_pos * ROWS : (block_pos + window) * ROWS] for block_pos in range(blocks_here)]
    )
    targets = jnp.bitwise_xor(matchings[:, 0] // blocks_here, my_index)
    picked = []
    for match_pos in range(matches):
        received = switched_send(keyvals, targets[match_pos], groups)
        received = received.reshape(blocks_here, ROWS, pair_feats)
        picked.append(jnp.take(received, matchings[match_pos] % blocks_here, axis=0, mode="clip"))
    partner_rows = jnp.stack(picked, axis=1).reshape(blocks_here, matches * ROWS, pair_feats)
    return jnp.concatenate([windows, partner_rows], axis=1)


def gathered_keys(keyvals, chosen):
    total_rows, pair_feats = keyvals.shape
    blocks_here, key_blocks = chosen.shape
    everyone = lax.all_gather(keyvals, "node", axis=0, tiled=True)
    everyone = everyone.reshape(-1, ROWS, pair_feats)
    picked = jnp.take(everyone, chosen.reshape(-1), axis=0, mode="clip")
    return picked.reshape(blocks_here, key_blocks * ROWS, pair_feats)


def local(node_states, w_qkv, w_out, ln_gain, ln_bias, local_mask, matchings):
    total_rows, model_width = node_states.shape
    blocks_here = total_rows // ROWS
    head_feats = w_qkv.shape[2]
    heads_here = head_feats // HEAD_DIM
    window = 2 * REACH + 1
    matches = matchings.shape[0]
    inv_root = 1.0 / math.sqrt(HEAD_DIM)
    my_index = lax.axis_index("node")
    groups = lax.axis_size("node")
    all_blocks = groups * blocks_here
    heads_axis = lax.axis_size("head")
    w_parts = [w_out] + [shift_heads(w_out, step, heads_axis) for step in range(1, heads_axis)]
    projected = jnp.einsum(
        "nd,dtf->ntf", node_states, w_qkv, preferred_element_type=jnp.float32
    ).astype(jnp.bfloat16)
    queries = projected[:, 0]
    keyvals = projected[:, 1:].reshape(total_rows, 2 * head_feats)
    global_blocks = my_index * blocks_here + jnp.arange(blocks_here, dtype=jnp.int32)
    offsets = jnp.arange(window, dtype=jnp.int32) - REACH
    neighbour = global_blocks[:, None] + offsets[None, :]
    if groups <= GATHER_GROUPS:
        key_rows = switched_keys(keyvals, matchings, my_index, groups, blocks_here, window)
    else:
        key_rows = routed_keys(keyvals, matchings, my_index, groups, blocks_here, window)
    key_count = key_rows.shape[1]
    key_part = key_rows[:, :, :head_feats].reshape(blocks_here, key_count, heads_here, HEAD_DIM)
    value_part = key_rows[:, :, head_feats:].reshape(blocks_here, key_count, heads_here, HEAD_DIM)
    query_blocks = queries.reshape(blocks_here, ROWS, heads_here, HEAD_DIM)
    local_ok = (
        (neighbour >= 0) & (neighbour < all_blocks) & ((offsets[None, :] == 0) | (local_mask == 1))
    )
    block_ok = jnp.concatenate([local_ok, jnp.ones((blocks_here, matches), dtype=bool)], axis=1)
    row_ok = jnp.repeat(block_ok, ROWS, axis=1)
    scores = (
        jnp.einsum("bqhd,bkhd->bhqk", query_blocks, key_part, preferred_element_type=jnp.float32)
        * inv_root
    )
    scores = jnp.where(row_ok[:, None, None, :], scores, -jnp.inf)
    highest = jnp.max(scores, axis=-1, keepdims=True)
    weights = jnp.exp(scores - highest)
    weights = (weights / jnp.sum(weights, axis=-1, keepdims=True)).astype(jnp.bfloat16)
    context = jnp.einsum("bhqk,bkhd->bqhd", weights, value_part, preferred_element_type=jnp.float32)
    context = context.astype(jnp.bfloat16).reshape(total_rows, head_feats)
    context_parts = [context] + [
        shift_heads(context, step, heads_axis) for step in range(1, heads_axis)
    ]
    mixed_rows = node_states.astype(jnp.float32) + jnp.einsum(
        "srf,sfo->ro",
        jnp.stack(context_parts),
        jnp.stack(w_parts),
        preferred_element_type=jnp.float32,
    )
    centre = jnp.mean(mixed_rows, axis=1, keepdims=True)
    deviation = mixed_rows - centre
    spread = jnp.mean(jnp.square(deviation), axis=1, keepdims=True)
    normed = deviation * lax.rsqrt(spread + NORM_EPS)
    out_cols = ln_gain.shape[0]
    col_start = lax.axis_index("head") * out_cols
    own_rows = lax.dynamic_slice_in_dim(normed, col_start, out_cols, 1)
    return (own_rows * ln_gain + ln_bias).astype(jnp.bfloat16)


def solution(mesh):
    placed = (
        P("node", None),
        P(None, None, "head"),
        P("head", None),
        P("head"),
        P("head"),
        P("node", None),
        P(None, "node"),
    )
    return jax.shard_map(
        local, mesh=mesh, in_specs=placed, out_specs=P("node", "head"), check_vma=False
    )
```

```python
import math

import jax
import jax.numpy as jnp
from jax import lax
from jax.sharding import PartitionSpec as P

HEAD_DIM = 64
ROWS = 128
REACH = 3
GATHER_GROUPS = 16


NORM_EPS = 1e-05


def partner(array, axis, bit):
    return lax.ppermute(array, axis, [(i, i ^ 1 << bit) for i in range(lax.axis_size(axis))])


def with_halo(array, sides, width):
    for axis, dim in sides:
        devices, length = (lax.axis_size(axis), array.shape[dim])
        up = [(i, (i + 1) % devices) for i in range(devices - 1)]
        down = [(j, i) for i, j in up]
        last = lax.slice_in_dim(array, length - width, length, axis=dim)
        first = lax.slice_in_dim(array, 0, width, axis=dim)
        before = lax.ppermute(last, axis, up)
        after = lax.ppermute(first, axis, down)
        array = jnp.concatenate([before, array, after], axis=dim)
    return array


def shift_heads(array, step, devices):
    return lax.ppermute(array, "head", [(i, (i + step) % devices) for i in range(devices)])


def keep_same(current):
    return current


def route_direct(payload, shift_val, digits):
    for bit_pos in range(digits):

        def moved(current, bit_pos=bit_pos):
            return partner(current, "node", bit_pos)

        taken = jnp.bitwise_and(jnp.right_shift(shift_val, bit_pos), 1) == 1
        payload = lax.cond(taken, moved, keep_same, payload)
    return payload


def select_partner(received, matchings, blocks_here, pair_feats):
    matches = matchings.shape[0]
    received = received.reshape(matches, blocks_here, ROWS, pair_feats)
    sources = matchings % blocks_here
    selector = (sources[:, :, None] == jnp.arange(blocks_here)[None, None, :]).astype(jnp.bfloat16)
    picked = jnp.einsum("mjs,msrf->mjrf", selector, received, preferred_element_type=jnp.float32)
    return picked.astype(jnp.bfloat16)


def routed_keys(keyvals, matchings, my_index, groups, blocks_here, window):
    total_rows, pair_feats = keyvals.shape
    matches = matchings.shape[0]
    digits = groups.bit_length() - 1
    padded = with_halo(keyvals, (("node", 0),), REACH * ROWS)
    windows = jnp.stack(
        [padded[block_pos * ROWS : (block_pos + window) * ROWS] for block_pos in range(blocks_here)]
    )
    targets = jnp.bitwise_xor(matchings[:, 0] // blocks_here, my_index)
    received = jnp.stack(
        [route_direct(keyvals, targets[match_pos], digits) for match_pos in range(matches)]
    )
    partner_blocks = select_partner(received, matchings, blocks_here, pair_feats)
    partner_rows = jnp.transpose(partner_blocks, (1, 0, 2, 3)).reshape(
        blocks_here, matches * ROWS, pair_feats
    )
    return jnp.concatenate([windows, partner_rows], axis=1)


def switched_send(payload, shift_val, groups):
    def branch(shift):
        def moved(current):
            return lax.ppermute(current, "node", [(i, i ^ shift) for i in range(groups)])

        return moved

    branches = [branch(shift) for shift in range(1, groups)]
    return lax.switch(jnp.clip(shift_val - 1, 0, groups - 2), branches, payload)


def switched_keys(keyvals, matchings, my_index, groups, blocks_here, window):
    total_rows, pair_feats = keyvals.shape
    matches = matchings.shape[0]
    padded = with_halo(keyvals, (("node", 0),), REACH * ROWS)
    windows = jnp.stack(
        [padded[block_pos * ROWS : (block_pos + window) * ROWS] for block_pos in range(blocks_here)]
    )
    targets = jnp.bitwise_xor(matchings[:, 0] // blocks_here, my_index)
    picked = []
    for match_pos in range(matches):
        received = switched_send(keyvals, targets[match_pos], groups)
        received = received.reshape(blocks_here, ROWS, pair_feats)
        picked.append(jnp.take(received, matchings[match_pos] % blocks_here, axis=0, mode="clip"))
    partner_rows = jnp.stack(picked, axis=1).reshape(blocks_here, matches * ROWS, pair_feats)
    return jnp.concatenate([windows, partner_rows], axis=1)


def spread_rows(pieces, heads_axis, me):
    slots = {0: pieces}
    for bit in reversed(range(heads_axis.bit_length() - 1)):
        flip = 1 << bit
        held = sorted(slots)
        other = lax.ppermute(
            jnp.stack([slots[k] for k in held]),
            "head",
            [(i, i ^ flip) for i in range(heads_axis)],
        )
        for pos, k in enumerate(held):
            slots[k ^ flip] = other[pos]
    count, part_rows, width = pieces.shape
    rows = jnp.zeros((count, heads_axis * part_rows, width), pieces.dtype)
    for k, part in slots.items():
        rows = lax.dynamic_update_slice_in_dim(rows, part, (me ^ k) * part_rows, axis=1)
    return rows


def quarter_keys(node_states, w_qkv, keyvals, matchings, my_index, groups, blocks_here, window):
    total_rows, pair_feats = keyvals.shape
    matches = matchings.shape[0]
    heads_axis = lax.axis_size("head")
    part_rows = total_rows // heads_axis
    me = lax.axis_index("head")
    mine = lax.dynamic_slice_in_dim(node_states, me * part_rows, part_rows, 0)
    up = [(i, i + 1) for i in range(groups - 1)]
    down = [(i + 1, i) for i in range(groups - 1)]
    before = lax.ppermute(mine, "node", up)
    after = lax.ppermute(mine, "node", down)
    targets = jnp.bitwise_xor(matchings[:, 0] // blocks_here, my_index)
    matched = [switched_send(mine, targets[match_pos], groups) for match_pos in range(matches)]
    rows = jnp.concatenate(
        [spread_rows(piece[None], heads_axis, me) for piece in [before, after] + matched]
    )
    partner_kv = jnp.einsum(
        "prd,dtf->prtf", rows, w_qkv[:, 1:], preferred_element_type=jnp.float32
    ).astype(jnp.bfloat16)
    partner_kv = partner_kv.reshape(rows.shape[0], total_rows, pair_feats)
    padded = jnp.concatenate([partner_kv[0], keyvals, partner_kv[1]], axis=0)
    windows = jnp.stack(
        [padded[block_pos * ROWS : (block_pos + window) * ROWS] for block_pos in range(blocks_here)]
    )
    picked = []
    for match_pos in range(matches):
        received = partner_kv[2 + match_pos].reshape(blocks_here, ROWS, pair_feats)
        picked.append(jnp.take(received, matchings[match_pos] % blocks_here, axis=0, mode="clip"))
    partner_rows = jnp.stack(picked, axis=1).reshape(blocks_here, matches * ROWS, pair_feats)
    return jnp.concatenate([windows, partner_rows], axis=1)


def gathered_keys(keyvals, chosen):
    total_rows, pair_feats = keyvals.shape
    blocks_here, key_blocks = chosen.shape
    everyone = lax.all_gather(keyvals, "node", axis=0, tiled=True)
    everyone = everyone.reshape(-1, ROWS, pair_feats)
    picked = jnp.take(everyone, chosen.reshape(-1), axis=0, mode="clip")
    return picked.reshape(blocks_here, key_blocks * ROWS, pair_feats)


def local(node_states, w_qkv, w_out, ln_gain, ln_bias, local_mask, matchings):
    total_rows, model_width = node_states.shape
    blocks_here = total_rows // ROWS
    head_feats = w_qkv.shape[2]
    heads_here = head_feats // HEAD_DIM
    window = 2 * REACH + 1
    matches = matchings.shape[0]
    inv_root = 1.0 / math.sqrt(HEAD_DIM)
    my_index = lax.axis_index("node")
    groups = lax.axis_size("node")
    all_blocks = groups * blocks_here
    heads_axis = lax.axis_size("head")
    w_parts = [w_out] + [shift_heads(w_out, step, heads_axis) for step in range(1, heads_axis)]
    projected = jnp.einsum(
        "nd,dtf->ntf", node_states, w_qkv, preferred_element_type=jnp.float32
    ).astype(jnp.bfloat16)
    queries = projected[:, 0]
    keyvals = projected[:, 1:].reshape(total_rows, 2 * head_feats)
    global_blocks = my_index * blocks_here + jnp.arange(blocks_here, dtype=jnp.int32)
    offsets = jnp.arange(window, dtype=jnp.int32) - REACH
    neighbour = global_blocks[:, None] + offsets[None, :]
    if groups <= GATHER_GROUPS:
        key_rows = quarter_keys(
            node_states, w_qkv, keyvals, matchings, my_index, groups, blocks_here, window
        )
    else:
        key_rows = routed_keys(keyvals, matchings, my_index, groups, blocks_here, window)
    key_count = key_rows.shape[1]
    key_part = key_rows[:, :, :head_feats].reshape(blocks_here, key_count, heads_here, HEAD_DIM)
    value_part = key_rows[:, :, head_feats:].reshape(blocks_here, key_count, heads_here, HEAD_DIM)
    query_blocks = queries.reshape(blocks_here, ROWS, heads_here, HEAD_DIM)
    local_ok = (
        (neighbour >= 0) & (neighbour < all_blocks) & ((offsets[None, :] == 0) | (local_mask == 1))
    )
    block_ok = jnp.concatenate([local_ok, jnp.ones((blocks_here, matches), dtype=bool)], axis=1)
    row_ok = jnp.repeat(block_ok, ROWS, axis=1)
    scores = (
        jnp.einsum("bqhd,bkhd->bhqk", query_blocks, key_part, preferred_element_type=jnp.float32)
        * inv_root
    )
    scores = jnp.where(row_ok[:, None, None, :], scores, -jnp.inf)
    highest = jnp.max(scores, axis=-1, keepdims=True)
    weights = jnp.exp(scores - highest)
    weights = (weights / jnp.sum(weights, axis=-1, keepdims=True)).astype(jnp.bfloat16)
    context = jnp.einsum("bhqk,bkhd->bqhd", weights, value_part, preferred_element_type=jnp.float32)
    context = context.astype(jnp.bfloat16).reshape(total_rows, head_feats)
    context_parts = [context] + [
        shift_heads(context, step, heads_axis) for step in range(1, heads_axis)
    ]
    mixed_rows = node_states.astype(jnp.float32) + jnp.einsum(
        "srf,sfo->ro",
        jnp.stack(context_parts),
        jnp.stack(w_parts),
        preferred_element_type=jnp.float32,
    )
    centre = jnp.mean(mixed_rows, axis=1, keepdims=True)
    deviation = mixed_rows - centre
    spread = jnp.mean(jnp.square(deviation), axis=1, keepdims=True)
    normed = deviation * lax.rsqrt(spread + NORM_EPS)
    out_cols = ln_gain.shape[0]
    col_start = lax.axis_index("head") * out_cols
    own_rows = lax.dynamic_slice_in_dim(normed, col_start, out_cols, 1)
    return (own_rows * ln_gain + ln_bias).astype(jnp.bfloat16)


def solution(mesh):
    placed = (
        P("node", None),
        P(None, None, "head"),
        P("head", None),
        P("head"),
        P("head"),
        P("node", None),
        P(None, "node"),
    )
    return jax.shard_map(
        local, mesh=mesh, in_specs=placed, out_specs=P("node", "head"), check_vma=False
    )
```

```python
import math

import jax
import jax.numpy as jnp
from jax import lax
from jax.sharding import PartitionSpec as P

HEAD_DIM = 64
ROWS = 128
REACH = 3
GATHER_GROUPS = 16


NORM_EPS = 1e-05


def partner(array, axis, bit):
    return lax.ppermute(array, axis, [(i, i ^ 1 << bit) for i in range(lax.axis_size(axis))])


def with_halo(array, sides, width):
    for axis, dim in sides:
        devices, length = (lax.axis_size(axis), array.shape[dim])
        up = [(i, (i + 1) % devices) for i in range(devices - 1)]
        down = [(j, i) for i, j in up]
        last = lax.slice_in_dim(array, length - width, length, axis=dim)
        first = lax.slice_in_dim(array, 0, width, axis=dim)
        before = lax.ppermute(last, axis, up)
        after = lax.ppermute(first, axis, down)
        array = jnp.concatenate([before, array, after], axis=dim)
    return array


def shift_heads(array, step, devices):
    return lax.ppermute(array, "head", [(i, (i + step) % devices) for i in range(devices)])


def flip_heads(array, flip, devices):
    return lax.ppermute(array, "head", [(i, i ^ flip) for i in range(devices)])


def spread_slots(piece, heads_axis):
    slots = {0: piece}
    for bit in reversed(range(heads_axis.bit_length() - 1)):
        flip = 1 << bit
        held = sorted(slots)
        other = flip_heads(jnp.stack([slots[k] for k in held]), flip, heads_axis)
        for pos, k in enumerate(held):
            slots[k ^ flip] = other[pos]
    return slots


def keep_same(current):
    return current


def route_direct(payload, shift_val, digits):
    for bit_pos in range(digits):

        def moved(current, bit_pos=bit_pos):
            return partner(current, "node", bit_pos)

        taken = jnp.bitwise_and(jnp.right_shift(shift_val, bit_pos), 1) == 1
        payload = lax.cond(taken, moved, keep_same, payload)
    return payload


def select_partner(received, matchings, blocks_here, pair_feats):
    matches = matchings.shape[0]
    received = received.reshape(matches, blocks_here, ROWS, pair_feats)
    sources = matchings % blocks_here
    selector = (sources[:, :, None] == jnp.arange(blocks_here)[None, None, :]).astype(jnp.bfloat16)
    picked = jnp.einsum("mjs,msrf->mjrf", selector, received, preferred_element_type=jnp.float32)
    return picked.astype(jnp.bfloat16)


def routed_keys(keyvals, matchings, my_index, groups, blocks_here, window):
    total_rows, pair_feats = keyvals.shape
    matches = matchings.shape[0]
    digits = groups.bit_length() - 1
    padded = with_halo(keyvals, (("node", 0),), REACH * ROWS)
    windows = jnp.stack(
        [padded[block_pos * ROWS : (block_pos + window) * ROWS] for block_pos in range(blocks_here)]
    )
    targets = jnp.bitwise_xor(matchings[:, 0] // blocks_here, my_index)
    received = jnp.stack(
        [route_direct(keyvals, targets[match_pos], digits) for match_pos in range(matches)]
    )
    partner_blocks = select_partner(received, matchings, blocks_here, pair_feats)
    partner_rows = jnp.transpose(partner_blocks, (1, 0, 2, 3)).reshape(
        blocks_here, matches * ROWS, pair_feats
    )
    return jnp.concatenate([windows, partner_rows], axis=1)


def switched_send(payload, shift_val, groups):
    def branch(shift):
        def moved(current):
            return lax.ppermute(current, "node", [(i, i ^ shift) for i in range(groups)])

        return moved

    branches = [branch(shift) for shift in range(1, groups)]
    return lax.switch(jnp.clip(shift_val - 1, 0, groups - 2), branches, payload)


def switched_keys(keyvals, matchings, my_index, groups, blocks_here, window):
    total_rows, pair_feats = keyvals.shape
    matches = matchings.shape[0]
    padded = with_halo(keyvals, (("node", 0),), REACH * ROWS)
    windows = jnp.stack(
        [padded[block_pos * ROWS : (block_pos + window) * ROWS] for block_pos in range(blocks_here)]
    )
    targets = jnp.bitwise_xor(matchings[:, 0] // blocks_here, my_index)
    picked = []
    for match_pos in range(matches):
        received = switched_send(keyvals, targets[match_pos], groups)
        received = received.reshape(blocks_here, ROWS, pair_feats)
        picked.append(jnp.take(received, matchings[match_pos] % blocks_here, axis=0, mode="clip"))
    partner_rows = jnp.stack(picked, axis=1).reshape(blocks_here, matches * ROWS, pair_feats)
    return jnp.concatenate([windows, partner_rows], axis=1)


def spread_rows(pieces, heads_axis, me):
    slots = spread_slots(pieces, heads_axis)
    count, part_rows, width = pieces.shape
    rows = jnp.zeros((count, heads_axis * part_rows, width), pieces.dtype)
    for k, part in slots.items():
        rows = lax.dynamic_update_slice_in_dim(rows, part, (me ^ k) * part_rows, axis=1)
    return rows


def quarter_keys(node_states, w_qkv, keyvals, matchings, my_index, groups, blocks_here, window):
    total_rows, pair_feats = keyvals.shape
    matches = matchings.shape[0]
    heads_axis = lax.axis_size("head")
    part_rows = total_rows // heads_axis
    me = lax.axis_index("head")
    mine = lax.dynamic_slice_in_dim(node_states, me * part_rows, part_rows, 0)
    up = [(i, i + 1) for i in range(groups - 1)]
    down = [(i + 1, i) for i in range(groups - 1)]
    before = lax.ppermute(mine, "node", up)
    after = lax.ppermute(mine, "node", down)
    targets = jnp.bitwise_xor(matchings[:, 0] // blocks_here, my_index)
    matched = [switched_send(mine, targets[match_pos], groups) for match_pos in range(matches)]
    rows = jnp.concatenate(
        [spread_rows(piece[None], heads_axis, me) for piece in [before, after] + matched]
    )
    partner_kv = jnp.einsum(
        "prd,dtf->prtf", rows, w_qkv[:, 1:], preferred_element_type=jnp.float32
    ).astype(jnp.bfloat16)
    partner_kv = partner_kv.reshape(rows.shape[0], total_rows, pair_feats)
    padded = jnp.concatenate([partner_kv[0], keyvals, partner_kv[1]], axis=0)
    windows = jnp.stack(
        [padded[block_pos * ROWS : (block_pos + window) * ROWS] for block_pos in range(blocks_here)]
    )
    picked = []
    for match_pos in range(matches):
        received = partner_kv[2 + match_pos].reshape(blocks_here, ROWS, pair_feats)
        picked.append(jnp.take(received, matchings[match_pos] % blocks_here, axis=0, mode="clip"))
    partner_rows = jnp.stack(picked, axis=1).reshape(blocks_here, matches * ROWS, pair_feats)
    return jnp.concatenate([windows, partner_rows], axis=1)


def gathered_keys(keyvals, chosen):
    total_rows, pair_feats = keyvals.shape
    blocks_here, key_blocks = chosen.shape
    everyone = lax.all_gather(keyvals, "node", axis=0, tiled=True)
    everyone = everyone.reshape(-1, ROWS, pair_feats)
    picked = jnp.take(everyone, chosen.reshape(-1), axis=0, mode="clip")
    return picked.reshape(blocks_here, key_blocks * ROWS, pair_feats)


def local(node_states, w_qkv, w_out, ln_gain, ln_bias, local_mask, matchings):
    total_rows, model_width = node_states.shape
    blocks_here = total_rows // ROWS
    head_feats = w_qkv.shape[2]
    heads_here = head_feats // HEAD_DIM
    window = 2 * REACH + 1
    matches = matchings.shape[0]
    inv_root = 1.0 / math.sqrt(HEAD_DIM)
    my_index = lax.axis_index("node")
    groups = lax.axis_size("node")
    all_blocks = groups * blocks_here
    heads_axis = lax.axis_size("head")
    head_index = lax.axis_index("head")
    out_cols = ln_gain.shape[0]
    w_parts = [lax.dynamic_slice_in_dim(w_out, head_index * out_cols, out_cols, 1)] + [
        flip_heads(
            lax.dynamic_slice_in_dim(w_out, (head_index ^ flip) * out_cols, out_cols, 1),
            flip,
            heads_axis,
        )
        for flip in range(1, heads_axis)
    ]
    projected = jnp.einsum(
        "nd,dtf->ntf", node_states, w_qkv, preferred_element_type=jnp.float32
    ).astype(jnp.bfloat16)
    queries = projected[:, 0]
    keyvals = projected[:, 1:].reshape(total_rows, 2 * head_feats)
    global_blocks = my_index * blocks_here + jnp.arange(blocks_here, dtype=jnp.int32)
    offsets = jnp.arange(window, dtype=jnp.int32) - REACH
    neighbour = global_blocks[:, None] + offsets[None, :]
    if groups <= GATHER_GROUPS:
        key_rows = quarter_keys(
            node_states, w_qkv, keyvals, matchings, my_index, groups, blocks_here, window
        )
    else:
        key_rows = routed_keys(keyvals, matchings, my_index, groups, blocks_here, window)
    key_count = key_rows.shape[1]
    key_part = key_rows[:, :, :head_feats].reshape(blocks_here, key_count, heads_here, HEAD_DIM)
    value_part = key_rows[:, :, head_feats:].reshape(blocks_here, key_count, heads_here, HEAD_DIM)
    query_blocks = queries.reshape(blocks_here, ROWS, heads_here, HEAD_DIM)
    local_ok = (
        (neighbour >= 0) & (neighbour < all_blocks) & ((offsets[None, :] == 0) | (local_mask == 1))
    )
    block_ok = jnp.concatenate([local_ok, jnp.ones((blocks_here, matches), dtype=bool)], axis=1)
    row_ok = jnp.repeat(block_ok, ROWS, axis=1)
    scores = (
        jnp.einsum("bqhd,bkhd->bhqk", query_blocks, key_part, preferred_element_type=jnp.float32)
        * inv_root
    )
    scores = jnp.where(row_ok[:, None, None, :], scores, -jnp.inf)
    highest = jnp.max(scores, axis=-1, keepdims=True)
    weights = jnp.exp(scores - highest)
    weights = (weights / jnp.sum(weights, axis=-1, keepdims=True)).astype(jnp.bfloat16)
    context = jnp.einsum("bhqk,bkhd->bqhd", weights, value_part, preferred_element_type=jnp.float32)
    context = context.astype(jnp.bfloat16).reshape(total_rows, head_feats)
    context_slots = spread_slots(context, heads_axis)
    own_cols = lax.dynamic_slice_in_dim(node_states, head_index * out_cols, out_cols, 1)
    mixed_rows = own_cols.astype(jnp.float32) + jnp.einsum(
        "srf,sfo->ro",
        jnp.stack([context_slots[flip] for flip in range(heads_axis)]),
        jnp.stack(w_parts),
        preferred_element_type=jnp.float32,
    )
    part_mean = jnp.mean(mixed_rows, axis=1, keepdims=True)
    part_square = jnp.sum(jnp.square(mixed_rows - part_mean), axis=1, keepdims=True)
    stats = jnp.concatenate([part_mean, part_square], axis=1)
    all_stats = jnp.stack(
        [stats] + [flip_heads(stats, flip, heads_axis) for flip in range(1, heads_axis)]
    )
    centre = jnp.mean(all_stats[:, :, 0:1], axis=0)
    spread = (
        jnp.sum(all_stats[:, :, 1:2], axis=0)
        + out_cols * jnp.sum(jnp.square(all_stats[:, :, 0:1] - centre), axis=0)
    ) / (heads_axis * out_cols)
    normed = (mixed_rows - centre) * lax.rsqrt(spread + NORM_EPS)
    return (normed * ln_gain + ln_bias).astype(jnp.bfloat16)


def solution(mesh):
    placed = (
        P("node", None),
        P(None, None, "head"),
        P("head", None),
        P("head"),
        P("head"),
        P("node", None),
        P(None, "node"),
    )
    return jax.shard_map(
        local, mesh=mesh, in_specs=placed, out_specs=P("node", "head"), check_vma=False
    )
```

```python
import math

import jax
import jax.numpy as jnp
from jax import lax
from jax.experimental import pallas as pl
from jax.experimental.pallas import tpu as pltpu
from jax.sharding import PartitionSpec as P

HEAD_DIM = 64
ROWS = 128
REACH = 3
GATHER_GROUPS = 16


NORM_EPS = 1e-05


def partner(array, axis, bit):
    return lax.ppermute(array, axis, [(i, i ^ 1 << bit) for i in range(lax.axis_size(axis))])


def with_halo(array, sides, width):
    for axis, dim in sides:
        devices, length = (lax.axis_size(axis), array.shape[dim])
        up = [(i, (i + 1) % devices) for i in range(devices - 1)]
        down = [(j, i) for i, j in up]
        last = lax.slice_in_dim(array, length - width, length, axis=dim)
        first = lax.slice_in_dim(array, 0, width, axis=dim)
        before = lax.ppermute(last, axis, up)
        after = lax.ppermute(first, axis, down)
        array = jnp.concatenate([before, array, after], axis=dim)
    return array


def shift_heads(array, step, devices):
    return lax.ppermute(array, "head", [(i, (i + step) % devices) for i in range(devices)])


def flip_heads(array, flip, devices):
    return lax.ppermute(array, "head", [(i, i ^ flip) for i in range(devices)])


def spread_slots(piece, heads_axis):
    slots = {0: piece}
    for bit in reversed(range(heads_axis.bit_length() - 1)):
        flip = 1 << bit
        held = sorted(slots)
        other = flip_heads(jnp.stack([slots[k] for k in held]), flip, heads_axis)
        for pos, k in enumerate(held):
            slots[k ^ flip] = other[pos]
    return slots


def keep_same(current):
    return current


def route_direct(payload, shift_val, digits):
    for bit_pos in range(digits):

        def moved(current, bit_pos=bit_pos):
            return partner(current, "node", bit_pos)

        taken = jnp.bitwise_and(jnp.right_shift(shift_val, bit_pos), 1) == 1
        payload = lax.cond(taken, moved, keep_same, payload)
    return payload


def select_partner(received, matchings, blocks_here, pair_feats):
    matches = matchings.shape[0]
    received = received.reshape(matches, blocks_here, ROWS, pair_feats)
    sources = matchings % blocks_here
    selector = (sources[:, :, None] == jnp.arange(blocks_here)[None, None, :]).astype(jnp.bfloat16)
    picked = jnp.einsum("mjs,msrf->mjrf", selector, received, preferred_element_type=jnp.float32)
    return picked.astype(jnp.bfloat16)


def routed_keys(keyvals, matchings, my_index, groups, blocks_here):
    matches = matchings.shape[0]
    digits = groups.bit_length() - 1
    up = [(i, i + 1) for i in range(groups - 1)]
    down = [(i + 1, i) for i in range(groups - 1)]
    before = lax.ppermute(keyvals, "node", up)
    after = lax.ppermute(keyvals, "node", down)
    targets = jnp.bitwise_xor(matchings[:, 0] // blocks_here, my_index)
    received = [route_direct(keyvals, targets[match_pos], digits) for match_pos in range(matches)]
    return jnp.stack([before, after] + received)


def switched_send(payload, shift_val, groups):
    def branch(shift):
        def moved(current):
            return lax.ppermute(current, "node", [(i, i ^ shift) for i in range(groups)])

        return moved

    branches = [branch(shift) for shift in range(1, groups)]
    return lax.switch(jnp.clip(shift_val - 1, 0, groups - 2), branches, payload)


def switched_keys(keyvals, matchings, my_index, groups, blocks_here, window):
    total_rows, pair_feats = keyvals.shape
    matches = matchings.shape[0]
    padded = with_halo(keyvals, (("node", 0),), REACH * ROWS)
    windows = jnp.stack(
        [padded[block_pos * ROWS : (block_pos + window) * ROWS] for block_pos in range(blocks_here)]
    )
    targets = jnp.bitwise_xor(matchings[:, 0] // blocks_here, my_index)
    picked = []
    for match_pos in range(matches):
        received = switched_send(keyvals, targets[match_pos], groups)
        received = received.reshape(blocks_here, ROWS, pair_feats)
        picked.append(jnp.take(received, matchings[match_pos] % blocks_here, axis=0, mode="clip"))
    partner_rows = jnp.stack(picked, axis=1).reshape(blocks_here, matches * ROWS, pair_feats)
    return jnp.concatenate([windows, partner_rows], axis=1)


def quarter_keys(node_states, w_qkv, matchings, my_index, groups, blocks_here):
    total_rows = node_states.shape[0]
    matches = matchings.shape[0]
    heads_axis = lax.axis_size("head")
    part_rows = total_rows // heads_axis
    me = lax.axis_index("head")
    mine = lax.dynamic_slice_in_dim(node_states, me * part_rows, part_rows, 0)
    up = [(i, i + 1) for i in range(groups - 1)]
    down = [(i + 1, i) for i in range(groups - 1)]
    before = lax.ppermute(mine, "node", up)
    after = lax.ppermute(mine, "node", down)
    targets = jnp.bitwise_xor(matchings[:, 0] // blocks_here, my_index)
    matched = [switched_send(mine, targets[match_pos], groups) for match_pos in range(matches)]
    spread = [spread_slots(piece, heads_axis) for piece in [before, after] + matched]
    slots = jnp.stack([jnp.stack([one[k] for one in spread]) for k in range(heads_axis)])
    slot_kv = jnp.einsum(
        "kprd,dtf->kprtf", slots, w_qkv[:, 1:], preferred_element_type=jnp.float32
    ).astype(jnp.bfloat16)
    order = jnp.bitwise_xor(jnp.arange(heads_axis, dtype=jnp.int32), me.astype(jnp.int32))
    ordered = jnp.take(slot_kv, order, axis=0, mode="clip")
    count = len(spread)
    ordered = jnp.transpose(ordered, (1, 0, 2, 3, 4))
    return ordered.reshape(count, total_rows, -1)


def gathered_keys(keyvals, chosen):
    total_rows, pair_feats = keyvals.shape
    blocks_here, key_blocks = chosen.shape
    everyone = lax.all_gather(keyvals, "node", axis=0, tiled=True)
    everyone = everyone.reshape(-1, ROWS, pair_feats)
    picked = jnp.take(everyone, chosen.reshape(-1), axis=0, mode="clip")
    return picked.reshape(blocks_here, key_blocks * ROWS, pair_feats)


def attention_kernel(live_ref, pick_ref, q_ref, own_ref, part_ref, out_ref, score_ref):
    blocks_here = q_ref.shape[0]
    heads_here = q_ref.shape[2] // HEAD_DIM
    head_feats = q_ref.shape[2]
    window = 2 * REACH + 1
    matches = part_ref.shape[0] - 2
    key_blocks = window + matches
    inv_root = 1.0 / math.sqrt(HEAD_DIM)
    for j in range(blocks_here):
        def key_block(t, cols, j=j):
            if t < window:
                pos = j + t - REACH
                if pos < 0:
                    return part_ref[0, pos + blocks_here, :, cols]
                if pos < blocks_here:
                    return own_ref[pos, :, cols]
                return part_ref[1, pos - blocks_here, :, cols]
            match_pos = t - window
            return part_ref[2 + match_pos, pick_ref[match_pos, j], :, cols]
        for h in range(heads_here):
            kcols = pl.ds(h * HEAD_DIM, HEAD_DIM)
            vcols = pl.ds(head_feats + h * HEAD_DIM, HEAD_DIM)
            query = q_ref[j, :, kcols]
            highest = jnp.full((ROWS, 1), -jnp.inf, jnp.float32)
            for t in range(key_blocks):
                scores = lax.dot_general(query, key_block(t, kcols), (((1,), (1,)), ((), ())),
                                         preferred_element_type=jnp.float32) * inv_root
                scores = jnp.where(live_ref[j, t] != 0, scores, -jnp.inf)
                score_ref[t] = scores
                highest = jnp.maximum(highest, jnp.max(scores, axis=1, keepdims=True))
            total = jnp.zeros((ROWS, 1), jnp.float32)
            for t in range(key_blocks):
                weights = jnp.exp(score_ref[t] - highest)
                score_ref[t] = weights
                total = total + jnp.sum(weights, axis=1, keepdims=True)
            context = jnp.zeros((ROWS, HEAD_DIM), jnp.float32)
            for t in range(key_blocks):
                probs = (score_ref[t] / total).astype(jnp.bfloat16)
                context = context + jnp.dot(probs, key_block(t, vcols), preferred_element_type=jnp.float32)
            out_ref[j, :, kcols] = context.astype(jnp.bfloat16)


def attention(live, pick, query, own, part):
    blocks_here, rows, head_feats = query.shape
    key_blocks = live.shape[1]
    vmem = pltpu.VMEM
    flops = 4 * blocks_here * rows * key_blocks * rows * head_feats
    moved = 2 * (query.size * 2 + own.size + part.size)
    return pl.pallas_call(
        attention_kernel,
        out_shape=jax.ShapeDtypeStruct(query.shape, jnp.bfloat16),
        in_specs=[pl.BlockSpec(memory_space=pltpu.SMEM), pl.BlockSpec(memory_space=pltpu.SMEM),
                  pl.BlockSpec(memory_space=vmem), pl.BlockSpec(memory_space=vmem), pl.BlockSpec(memory_space=vmem)],
        out_specs=pl.BlockSpec(memory_space=vmem),
        scratch_shapes=[pltpu.VMEM((key_blocks, ROWS, ROWS), jnp.float32)],
        cost_estimate=pl.CostEstimate(
            flops=flops, transcendentals=blocks_here * rows * key_blocks * rows * 4, bytes_accessed=moved
        ),
    )(live, pick, query, own, part)


def local(node_states, w_qkv, w_out, ln_gain, ln_bias, local_mask, matchings):
    total_rows, model_width = node_states.shape
    blocks_here = total_rows // ROWS
    head_feats = w_qkv.shape[2]
    heads_here = head_feats // HEAD_DIM
    window = 2 * REACH + 1
    matches = matchings.shape[0]
    inv_root = 1.0 / math.sqrt(HEAD_DIM)
    my_index = lax.axis_index("node")
    groups = lax.axis_size("node")
    all_blocks = groups * blocks_here
    heads_axis = lax.axis_size("head")
    head_index = lax.axis_index("head")
    out_cols = ln_gain.shape[0]
    w_parts = [lax.dynamic_slice_in_dim(w_out, head_index * out_cols, out_cols, 1)] + [
        flip_heads(
            lax.dynamic_slice_in_dim(w_out, (head_index ^ flip) * out_cols, out_cols, 1),
            flip,
            heads_axis,
        )
        for flip in range(1, heads_axis)
    ]
    projected = jnp.einsum(
        "nd,dtf->ntf", node_states, w_qkv, preferred_element_type=jnp.float32
    ).astype(jnp.bfloat16)
    queries = projected[:, 0]
    keyvals = projected[:, 1:].reshape(total_rows, 2 * head_feats)
    global_blocks = my_index * blocks_here + jnp.arange(blocks_here, dtype=jnp.int32)
    offsets = jnp.arange(window, dtype=jnp.int32) - REACH
    neighbour = global_blocks[:, None] + offsets[None, :]
    if groups <= GATHER_GROUPS:
        part = quarter_keys(node_states, w_qkv, matchings, my_index, groups, blocks_here)
    else:
        part = routed_keys(keyvals, matchings, my_index, groups, blocks_here)
    local_ok = (
        (neighbour >= 0) & (neighbour < all_blocks) & ((offsets[None, :] == 0) | (local_mask == 1))
    )
    block_ok = jnp.concatenate([local_ok, jnp.ones((blocks_here, matches), dtype=bool)], axis=1)
    context = attention(
        block_ok.astype(jnp.int32),
        (matchings % blocks_here).astype(jnp.int32),
        queries.reshape(blocks_here, ROWS, head_feats),
        keyvals.reshape(blocks_here, ROWS, 2 * head_feats),
        part.reshape(part.shape[0], blocks_here, ROWS, 2 * head_feats),
    ).reshape(total_rows, head_feats)
    context_slots = spread_slots(context, heads_axis)
    own_cols = lax.dynamic_slice_in_dim(node_states, head_index * out_cols, out_cols, 1)
    mixed_rows = own_cols.astype(jnp.float32) + jnp.einsum(
        "srf,sfo->ro",
        jnp.stack([context_slots[flip] for flip in range(heads_axis)]),
        jnp.stack(w_parts),
        preferred_element_type=jnp.float32,
    )
    part_mean = jnp.mean(mixed_rows, axis=1, keepdims=True)
    part_square = jnp.sum(jnp.square(mixed_rows - part_mean), axis=1, keepdims=True)
    stats = jnp.concatenate([part_mean, part_square], axis=1)
    all_stats = jnp.stack(
        [stats] + [flip_heads(stats, flip, heads_axis) for flip in range(1, heads_axis)]
    )
    centre = jnp.mean(all_stats[:, :, 0:1], axis=0)
    spread = (
        jnp.sum(all_stats[:, :, 1:2], axis=0)
        + out_cols * jnp.sum(jnp.square(all_stats[:, :, 0:1] - centre), axis=0)
    ) / (heads_axis * out_cols)
    normed = (mixed_rows - centre) * lax.rsqrt(spread + NORM_EPS)
    return (normed * ln_gain + ln_bias).astype(jnp.bfloat16)


def solution(mesh):
    placed = (
        P("node", None),
        P(None, None, "head"),
        P("head", None),
        P("head"),
        P("head"),
        P("node", None),
        P(None, "node"),
    )
    return jax.shard_map(
        local, mesh=mesh, in_specs=placed, out_specs=P("node", "head"), check_vma=False
    )
```

```python
import math

import jax
import jax.numpy as jnp
from jax import lax
from jax.experimental import pallas as pl
from jax.experimental.pallas import tpu as pltpu
from jax.sharding import PartitionSpec as P

HEAD_DIM = 64
ROWS = 128
REACH = 3
LANES = 128
GATHER_GROUPS = 16


NORM_EPS = 1e-05


def partner(array, axis, bit):
    return lax.ppermute(array, axis, [(i, i ^ 1 << bit) for i in range(lax.axis_size(axis))])


def flip_heads(array, flip, devices):
    return lax.ppermute(array, "head", [(i, i ^ flip) for i in range(devices)])


def spread_slots(piece, heads_axis):
    slots = {0: piece}
    for bit in reversed(range(heads_axis.bit_length() - 1)):
        flip = 1 << bit
        held = sorted(slots)
        other = flip_heads(jnp.stack([slots[k] for k in held]), flip, heads_axis)
        for pos, k in enumerate(held):
            slots[k ^ flip] = other[pos]
    return slots


def keep_same(current):
    return current


def route_direct(payload, shift_val, digits):
    for bit_pos in range(digits):

        def moved(current, bit_pos=bit_pos):
            return partner(current, "node", bit_pos)

        taken = jnp.bitwise_and(jnp.right_shift(shift_val, bit_pos), 1) == 1
        payload = lax.cond(taken, moved, keep_same, payload)
    return payload


def routed_keys(keyvals, matchings, my_index, groups, blocks_here):
    matches = matchings.shape[0]
    digits = groups.bit_length() - 1
    up = [(i, i + 1) for i in range(groups - 1)]
    down = [(i + 1, i) for i in range(groups - 1)]
    before = lax.ppermute(keyvals, "node", up)
    after = lax.ppermute(keyvals, "node", down)
    targets = jnp.bitwise_xor(matchings[:, 0] // blocks_here, my_index)
    received = [route_direct(keyvals, targets[match_pos], digits) for match_pos in range(matches)]
    return jnp.stack([before, after] + received)


def switched_send(payload, shift_val, groups):
    def branch(shift):
        def moved(current):
            return lax.ppermute(current, "node", [(i, i ^ shift) for i in range(groups)])

        return moved

    branches = [branch(shift) for shift in range(1, groups)]
    return lax.switch(jnp.clip(shift_val - 1, 0, groups - 2), branches, payload)


def quarter_keys(node_states, w_kv, w_parts, matchings, my_index, groups, blocks_here):
    total_rows, model_width = node_states.shape
    matches = matchings.shape[0]
    heads_axis = lax.axis_size("head")
    sub_rows = ROWS // heads_axis
    me = lax.axis_index("head")
    mine = node_states.reshape(blocks_here, heads_axis, sub_rows, model_width)
    mine = lax.dynamic_index_in_dim(mine, me, axis=1, keepdims=False)
    mine = mine.reshape(blocks_here * sub_rows, model_width)
    up = [(i, i + 1) for i in range(groups - 1)]
    down = [(i + 1, i) for i in range(groups - 1)]
    before = lax.ppermute(mine, "node", up)
    after = lax.ppermute(mine, "node", down)
    targets = jnp.bitwise_xor(matchings[:, 0] // blocks_here, my_index)
    matched = [switched_send(mine, targets[match_pos], groups) for match_pos in range(matches)]
    w_parts, matched[0] = lax.optimization_barrier((w_parts, matched[0]))
    spread = [spread_slots(piece, heads_axis) for piece in [before, after] + matched]
    rows = jnp.stack(
        [
            jnp.stack(
                [one[k].reshape(blocks_here, sub_rows, model_width) for k in range(heads_axis)],
                axis=1,
            )
            for one in spread
        ]
    )
    count = len(spread)
    rows = rows.reshape(count * total_rows, model_width)
    partner_kv = jnp.dot(rows, w_kv, preferred_element_type=jnp.float32).astype(jnp.bfloat16)
    return partner_kv.reshape(count, total_rows, w_kv.shape[1]), w_parts


def attention_kernel(live_ref, pick_ref, q_ref, own_ref, part_ref, out_ref, score_ref):
    blocks_here = q_ref.shape[0]
    head_feats = q_ref.shape[2]
    pairs = head_feats // LANES
    per_pair = LANES // HEAD_DIM
    window = 2 * REACH + 1
    matches = part_ref.shape[0] - 2
    key_blocks = window + matches
    inv_root = 1.0 / math.sqrt(HEAD_DIM)
    lane = lax.broadcasted_iota(jnp.int32, (ROWS, LANES), 1)
    for j in range(blocks_here):

        def key_block(t, cols, j=j):
            if t < window:
                pos = j + t - REACH
                if pos < 0:
                    return part_ref[0, pos + blocks_here, :, cols]
                if pos < blocks_here:
                    return own_ref[pos, :, cols]
                return part_ref[1, pos - blocks_here, :, cols]
            match_pos = t - window
            return part_ref[2 + match_pos, pick_ref[match_pos, j], :, cols]

        for pair in range(pairs):
            kcols = pl.ds(pair * LANES, LANES)
            vcols = pl.ds(head_feats + pair * LANES, LANES)
            both = q_ref[j, :, kcols]
            merged = jnp.zeros((ROWS, LANES), jnp.float32)
            for half in range(per_pair):
                mine = (lane >= half * HEAD_DIM) & (lane < (half + 1) * HEAD_DIM)
                query = jnp.where(mine, both, jnp.zeros_like(both))
                highest = jnp.full((ROWS, ROWS), -jnp.inf, jnp.float32)
                for t in range(key_blocks):
                    scores = lax.dot_general(
                        query, key_block(t, kcols), (((1,), (1,)), ((), ())),
                        preferred_element_type=jnp.float32,
                    ) * inv_root
                    scores = jnp.where(live_ref[j, t] != 0, scores, -jnp.inf)
                    score_ref[t] = scores
                    highest = jnp.maximum(highest, scores)
                highest = jnp.max(highest, axis=1, keepdims=True)
                total = jnp.zeros((ROWS, ROWS), jnp.float32)
                for t in range(key_blocks):
                    weights = jnp.exp(score_ref[t] - highest)
                    score_ref[t] = weights
                    total = total + weights
                total = jnp.sum(total, axis=1, keepdims=True)
                context = jnp.zeros((ROWS, LANES), jnp.float32)
                for t in range(key_blocks):
                    probs = (score_ref[t] / total).astype(jnp.bfloat16)
                    context = context + jnp.dot(
                        probs, key_block(t, vcols), preferred_element_type=jnp.float32
                    )
                merged = jnp.where(mine, context, merged)
            out_ref[j, :, kcols] = merged.astype(jnp.bfloat16)


def attention(live, pick, query, own, part):
    blocks_here, rows, head_feats = query.shape
    key_blocks = live.shape[1]
    vmem = pltpu.VMEM
    flops = 8 * blocks_here * rows * key_blocks * rows * head_feats
    moved = 2 * (query.size * 2 + own.size + part.size)
    return pl.pallas_call(
        attention_kernel,
        out_shape=jax.ShapeDtypeStruct(query.shape, jnp.bfloat16),
        in_specs=[pl.BlockSpec(memory_space=pltpu.SMEM), pl.BlockSpec(memory_space=pltpu.SMEM),
                  pl.BlockSpec(memory_space=vmem), pl.BlockSpec(memory_space=vmem), pl.BlockSpec(memory_space=vmem)],
        out_specs=pl.BlockSpec(memory_space=vmem),
        scratch_shapes=[pltpu.VMEM((key_blocks, ROWS, ROWS), jnp.float32)],
        cost_estimate=pl.CostEstimate(
            flops=flops, transcendentals=blocks_here * rows * key_blocks * rows * 4, bytes_accessed=moved
        ),
    )(live, pick, query, own, part)

def local(node_states, w_qkv, w_out, ln_gain, ln_bias, local_mask, matchings):
    total_rows, model_width = node_states.shape
    blocks_here = total_rows // ROWS
    head_feats = w_qkv.shape[2]
    heads_here = head_feats // HEAD_DIM
    window = 2 * REACH + 1
    matches = matchings.shape[0]
    inv_root = 1.0 / math.sqrt(HEAD_DIM)
    my_index = lax.axis_index("node")
    groups = lax.axis_size("node")
    all_blocks = groups * blocks_here
    heads_axis = lax.axis_size("head")
    head_index = lax.axis_index("head")
    out_cols = ln_gain.shape[0]
    w_parts = [lax.dynamic_slice_in_dim(w_out, head_index * out_cols, out_cols, 1)] + [
        flip_heads(
            lax.dynamic_slice_in_dim(w_out, (head_index ^ flip) * out_cols, out_cols, 1),
            flip,
            heads_axis,
        )
        for flip in range(1, heads_axis)
    ]
    projected = jnp.einsum(
        "nd,dtf->ntf", node_states, w_qkv, preferred_element_type=jnp.float32
    ).astype(jnp.bfloat16)
    queries = projected[:, 0]
    keyvals = projected[:, 1:].reshape(total_rows, 2 * head_feats)
    global_blocks = my_index * blocks_here + jnp.arange(blocks_here, dtype=jnp.int32)
    offsets = jnp.arange(window, dtype=jnp.int32) - REACH
    neighbour = global_blocks[:, None] + offsets[None, :]
    if groups <= GATHER_GROUPS:
        w_kv = w_qkv[:, 1:].reshape(model_width, 2 * head_feats)
        part, w_parts = quarter_keys(
            node_states, w_kv, w_parts, matchings, my_index, groups, blocks_here
        )
    else:
        part = routed_keys(keyvals, matchings, my_index, groups, blocks_here)
    local_ok = (
        (neighbour >= 0) & (neighbour < all_blocks) & ((offsets[None, :] == 0) | (local_mask == 1))
    )
    block_ok = jnp.concatenate([local_ok, jnp.ones((blocks_here, matches), dtype=bool)], axis=1)
    context = attention(
        block_ok.astype(jnp.int32),
        (matchings % blocks_here).astype(jnp.int32),
        queries.reshape(blocks_here, ROWS, head_feats),
        keyvals.reshape(blocks_here, ROWS, 2 * head_feats),
        part.reshape(part.shape[0], blocks_here, ROWS, 2 * head_feats),
    ).reshape(total_rows, head_feats)
    context_slots = spread_slots(context, heads_axis)
    own_cols = lax.dynamic_slice_in_dim(node_states, head_index * out_cols, out_cols, 1)
    mixed_rows = own_cols.astype(jnp.float32) + jnp.einsum(
        "srf,sfo->ro",
        jnp.stack([context_slots[flip] for flip in range(heads_axis)]),
        jnp.stack(w_parts),
        preferred_element_type=jnp.float32,
    )
    part_mean = jnp.mean(mixed_rows, axis=1, keepdims=True)
    part_square = jnp.sum(jnp.square(mixed_rows - part_mean), axis=1, keepdims=True)
    stats = jnp.concatenate([part_mean, part_square], axis=1)
    all_stats = jnp.stack(
        [stats] + [flip_heads(stats, flip, heads_axis) for flip in range(1, heads_axis)]
    )
    centre = jnp.mean(all_stats[:, :, 0:1], axis=0)
    spread = (
        jnp.sum(all_stats[:, :, 1:2], axis=0)
        + out_cols * jnp.sum(jnp.square(all_stats[:, :, 0:1] - centre), axis=0)
    ) / (heads_axis * out_cols)
    normed = (mixed_rows - centre) * lax.rsqrt(spread + NORM_EPS)
    return (normed * ln_gain + ln_bias).astype(jnp.bfloat16)


def solution(mesh):
    placed = (
        P("node", None),
        P(None, None, "head"),
        P("head", None),
        P("head"),
        P("head"),
        P("node", None),
        P(None, "node"),
    )
    return jax.shard_map(
        local, mesh=mesh, in_specs=placed, out_specs=P("node", "head"), check_vma=False
    )
```

```python
import math

import jax
import jax.numpy as jnp
from jax import lax
from jax.experimental import pallas as pl
from jax.experimental.pallas import tpu as pltpu
from jax.sharding import PartitionSpec as P

HEAD_DIM = 64
ROWS = 128
REACH = 3
LANES = 128
GATHER_GROUPS = 16


NORM_EPS = 1e-05


def partner(array, axis, bit):
    return lax.ppermute(array, axis, [(i, i ^ 1 << bit) for i in range(lax.axis_size(axis))])


def flip_heads(array, flip, devices):
    return lax.ppermute(array, "head", [(i, i ^ flip) for i in range(devices)])


def spread_slots(piece, heads_axis):
    slots = {0: piece}
    for bit in reversed(range(heads_axis.bit_length() - 1)):
        flip = 1 << bit
        held = sorted(slots)
        other = flip_heads(jnp.stack([slots[k] for k in held]), flip, heads_axis)
        for pos, k in enumerate(held):
            slots[k ^ flip] = other[pos]
    return slots


def keep_same(current):
    return current


def route_direct(payload, shift_val, digits):
    for bit_pos in range(digits):

        def moved(current, bit_pos=bit_pos):
            return partner(current, "node", bit_pos)

        taken = jnp.bitwise_and(jnp.right_shift(shift_val, bit_pos), 1) == 1
        payload = lax.cond(taken, moved, keep_same, payload)
    return payload


def routed_keys(keyvals, matchings, my_index, groups, blocks_here):
    matches = matchings.shape[0]
    digits = groups.bit_length() - 1
    up = [(i, i + 1) for i in range(groups - 1)]
    down = [(i + 1, i) for i in range(groups - 1)]
    before = lax.ppermute(keyvals, "node", up)
    after = lax.ppermute(keyvals, "node", down)
    targets = jnp.bitwise_xor(matchings[:, 0] // blocks_here, my_index)
    received = [route_direct(keyvals, targets[match_pos], digits) for match_pos in range(matches)]
    return jnp.stack([before, after] + received)


def switched_send(payload, shift_val, groups, pending=()):
    heads_axis = lax.axis_size("head")

    def branch(shift):
        def moved(operands):
            current, waiting = operands
            sent = lax.ppermute(current, "node", [(i, i ^ shift) for i in range(groups)])
            return sent, [spread_stack(piece, heads_axis) for piece in waiting]

        return moved

    branches = [branch(shift) for shift in range(1, groups)]
    return lax.switch(jnp.clip(shift_val - 1, 0, groups - 2), branches, (payload, list(pending)))


def spread_stack(piece, heads_axis):
    slots = spread_slots(piece, heads_axis)
    return jnp.stack([slots[k] for k in range(heads_axis)])


def quarter_keys(node_states, w_kv, w_parts, matchings, my_index, groups, blocks_here):
    total_rows, model_width = node_states.shape
    matches = matchings.shape[0]
    heads_axis = lax.axis_size("head")
    sub_rows = ROWS // heads_axis
    me = lax.axis_index("head")
    mine = node_states.reshape(blocks_here, heads_axis, sub_rows, model_width)
    mine = lax.dynamic_index_in_dim(mine, me, axis=1, keepdims=False)
    mine = mine.reshape(blocks_here * sub_rows, model_width)
    up = [(i, i + 1) for i in range(groups - 1)]
    down = [(i + 1, i) for i in range(groups - 1)]
    before = lax.ppermute(mine, "node", up)
    after = lax.ppermute(mine, "node", down)
    targets = jnp.bitwise_xor(matchings[:, 0] // blocks_here, my_index)
    waiting = [before, after]
    spread = []
    for match_pos in range(matches):
        take = 1 if match_pos < 2 else 2
        received, done = switched_send(
            mine, targets[match_pos], groups, waiting[:take] if match_pos else ()
        )
        if match_pos:
            waiting = waiting[take:]
        if match_pos == 0:
            w_parts, received = lax.optimization_barrier((w_parts, received))
        spread.extend(done)
        waiting.append(received)
    spread.extend(spread_stack(piece, heads_axis) for piece in waiting)
    rows = jnp.stack(
        [
            jnp.transpose(one.reshape(heads_axis, blocks_here, sub_rows, model_width), (1, 0, 2, 3))
            for one in spread
        ]
    )
    count = len(spread)
    rows = rows.reshape(count * total_rows, model_width)
    partner_kv = jnp.dot(rows, w_kv, preferred_element_type=jnp.float32).astype(jnp.bfloat16)
    return partner_kv.reshape(count, total_rows, w_kv.shape[1]), w_parts


def attention_kernel(live_ref, pick_ref, q_ref, own_ref, part_ref, out_ref, score_ref):
    blocks_here = q_ref.shape[0]
    head_feats = q_ref.shape[2]
    pairs = head_feats // LANES
    per_pair = LANES // HEAD_DIM
    window = 2 * REACH + 1
    matches = part_ref.shape[0] - 2
    key_blocks = window + matches
    inv_root = 1.0 / math.sqrt(HEAD_DIM)
    lane = lax.broadcasted_iota(jnp.int32, (ROWS, LANES), 1)
    for j in range(blocks_here):

        def key_block(t, cols, j=j):
            if t < window:
                pos = j + t - REACH
                if pos < 0:
                    return part_ref[0, pos + blocks_here, :, cols]
                if pos < blocks_here:
                    return own_ref[pos, :, cols]
                return part_ref[1, pos - blocks_here, :, cols]
            match_pos = t - window
            return part_ref[2 + match_pos, pick_ref[match_pos, j], :, cols]

        for pair in range(pairs):
            kcols = pl.ds(pair * LANES, LANES)
            vcols = pl.ds(head_feats + pair * LANES, LANES)
            both = q_ref[j, :, kcols]
            merged = jnp.zeros((ROWS, LANES), jnp.float32)
            for half in range(per_pair):
                mine = (lane >= half * HEAD_DIM) & (lane < (half + 1) * HEAD_DIM)
                query = jnp.where(mine, both, jnp.zeros_like(both))
                highest = jnp.full((ROWS, ROWS), -jnp.inf, jnp.float32)
                for t in range(key_blocks):
                    scores = lax.dot_general(
                        query, key_block(t, kcols), (((1,), (1,)), ((), ())),
                        preferred_element_type=jnp.float32,
                    ) * inv_root
                    scores = jnp.where(live_ref[j, t] != 0, scores, -jnp.inf)
                    score_ref[t] = scores
                    highest = jnp.maximum(highest, scores)
                highest = jnp.max(highest, axis=1, keepdims=True)
                total = jnp.zeros((ROWS, ROWS), jnp.float32)
                for t in range(key_blocks):
                    weights = jnp.exp(score_ref[t] - highest)
                    score_ref[t] = weights
                    total = total + weights
                total = jnp.sum(total, axis=1, keepdims=True)
                context = jnp.zeros((ROWS, LANES), jnp.float32)
                for t in range(key_blocks):
                    probs = (score_ref[t] / total).astype(jnp.bfloat16)
                    context = context + jnp.dot(
                        probs, key_block(t, vcols), preferred_element_type=jnp.float32
                    )
                merged = jnp.where(mine, context, merged)
            out_ref[j, :, kcols] = merged.astype(jnp.bfloat16)


def attention(live, pick, query, own, part):
    blocks_here, rows, head_feats = query.shape
    key_blocks = live.shape[1]
    vmem = pltpu.VMEM
    flops = 8 * blocks_here * rows * key_blocks * rows * head_feats
    moved = 2 * (query.size * 2 + own.size + part.size)
    return pl.pallas_call(
        attention_kernel,
        out_shape=jax.ShapeDtypeStruct(query.shape, jnp.bfloat16),
        in_specs=[pl.BlockSpec(memory_space=pltpu.SMEM), pl.BlockSpec(memory_space=pltpu.SMEM),
                  pl.BlockSpec(memory_space=vmem), pl.BlockSpec(memory_space=vmem), pl.BlockSpec(memory_space=vmem)],
        out_specs=pl.BlockSpec(memory_space=vmem),
        scratch_shapes=[pltpu.VMEM((key_blocks, ROWS, ROWS), jnp.float32)],
        cost_estimate=pl.CostEstimate(
            flops=flops, transcendentals=blocks_here * rows * key_blocks * rows * 4, bytes_accessed=moved
        ),
    )(live, pick, query, own, part)

def local(node_states, w_qkv, w_out, ln_gain, ln_bias, local_mask, matchings):
    total_rows, model_width = node_states.shape
    blocks_here = total_rows // ROWS
    head_feats = w_qkv.shape[2]
    heads_here = head_feats // HEAD_DIM
    window = 2 * REACH + 1
    matches = matchings.shape[0]
    inv_root = 1.0 / math.sqrt(HEAD_DIM)
    my_index = lax.axis_index("node")
    groups = lax.axis_size("node")
    all_blocks = groups * blocks_here
    heads_axis = lax.axis_size("head")
    head_index = lax.axis_index("head")
    out_cols = ln_gain.shape[0]
    w_parts = [lax.dynamic_slice_in_dim(w_out, head_index * out_cols, out_cols, 1)] + [
        flip_heads(
            lax.dynamic_slice_in_dim(w_out, (head_index ^ flip) * out_cols, out_cols, 1),
            flip,
            heads_axis,
        )
        for flip in range(1, heads_axis)
    ]
    projected = jnp.einsum(
        "nd,dtf->ntf", node_states, w_qkv, preferred_element_type=jnp.float32
    ).astype(jnp.bfloat16)
    queries = projected[:, 0]
    keyvals = projected[:, 1:].reshape(total_rows, 2 * head_feats)
    global_blocks = my_index * blocks_here + jnp.arange(blocks_here, dtype=jnp.int32)
    offsets = jnp.arange(window, dtype=jnp.int32) - REACH
    neighbour = global_blocks[:, None] + offsets[None, :]
    if groups <= GATHER_GROUPS:
        w_kv = w_qkv[:, 1:].reshape(model_width, 2 * head_feats)
        part, w_parts = quarter_keys(
            node_states, w_kv, w_parts, matchings, my_index, groups, blocks_here
        )
    else:
        part = routed_keys(keyvals, matchings, my_index, groups, blocks_here)
    local_ok = (
        (neighbour >= 0) & (neighbour < all_blocks) & ((offsets[None, :] == 0) | (local_mask == 1))
    )
    block_ok = jnp.concatenate([local_ok, jnp.ones((blocks_here, matches), dtype=bool)], axis=1)
    context = attention(
        block_ok.astype(jnp.int32),
        (matchings % blocks_here).astype(jnp.int32),
        queries.reshape(blocks_here, ROWS, head_feats),
        keyvals.reshape(blocks_here, ROWS, 2 * head_feats),
        part.reshape(part.shape[0], blocks_here, ROWS, 2 * head_feats),
    ).reshape(total_rows, head_feats)
    context_slots = spread_slots(context, heads_axis)
    own_cols = lax.dynamic_slice_in_dim(node_states, head_index * out_cols, out_cols, 1)
    mixed_rows = own_cols.astype(jnp.float32) + jnp.einsum(
        "srf,sfo->ro",
        jnp.stack([context_slots[flip] for flip in range(heads_axis)]),
        jnp.stack(w_parts),
        preferred_element_type=jnp.float32,
    )
    part_mean = jnp.mean(mixed_rows, axis=1, keepdims=True)
    part_square = jnp.sum(jnp.square(mixed_rows - part_mean), axis=1, keepdims=True)
    stats = jnp.concatenate([part_mean, part_square], axis=1)
    all_stats = jnp.stack(
        [stats] + [flip_heads(stats, flip, heads_axis) for flip in range(1, heads_axis)]
    )
    centre = jnp.mean(all_stats[:, :, 0:1], axis=0)
    spread = (
        jnp.sum(all_stats[:, :, 1:2], axis=0)
        + out_cols * jnp.sum(jnp.square(all_stats[:, :, 0:1] - centre), axis=0)
    ) / (heads_axis * out_cols)
    normed = (mixed_rows - centre) * lax.rsqrt(spread + NORM_EPS)
    return (normed * ln_gain + ln_bias).astype(jnp.bfloat16)


def solution(mesh):
    placed = (
        P("node", None),
        P(None, None, "head"),
        P("head", None),
        P("head"),
        P("head"),
        P("node", None),
        P(None, "node"),
    )
    return jax.shard_map(
        local, mesh=mesh, in_specs=placed, out_specs=P("node", "head"), check_vma=False
    )
```

```python
import math

import jax
import jax.numpy as jnp
from jax import lax
from jax.experimental import pallas as pl
from jax.experimental.pallas import tpu as pltpu
from jax.sharding import PartitionSpec as P

HEAD_DIM = 64
ROWS = 128
REACH = 3
LANES = 128
GATHER_GROUPS = 16
STATIC_GROUPS = 8


NORM_EPS = 1e-05


def partner(array, axis, bit):
    return lax.ppermute(array, axis, [(i, i ^ 1 << bit) for i in range(lax.axis_size(axis))])


def flip_heads(array, flip, devices):
    return lax.ppermute(array, "head", [(i, i ^ flip) for i in range(devices)])


def spread_slots(piece, heads_axis):
    slots = {0: piece}
    for bit in reversed(range(heads_axis.bit_length() - 1)):
        flip = 1 << bit
        held = sorted(slots)
        other = flip_heads(jnp.stack([slots[k] for k in held]), flip, heads_axis)
        for pos, k in enumerate(held):
            slots[k ^ flip] = other[pos]
    return slots


def keep_same(current):
    return current


def route_direct(payload, shift_val, digits):
    for bit_pos in range(digits):

        def moved(current, bit_pos=bit_pos):
            return partner(current, "node", bit_pos)

        taken = jnp.bitwise_and(jnp.right_shift(shift_val, bit_pos), 1) == 1
        payload = lax.cond(taken, moved, keep_same, payload)
    return payload


def routed_keys(keyvals, matchings, my_index, groups, blocks_here):
    matches = matchings.shape[0]
    digits = groups.bit_length() - 1
    up = [(i, i + 1) for i in range(groups - 1)]
    down = [(i + 1, i) for i in range(groups - 1)]
    before = lax.ppermute(keyvals, "node", up)
    after = lax.ppermute(keyvals, "node", down)
    targets = jnp.bitwise_xor(matchings[:, 0] // blocks_here, my_index)
    received = [route_direct(keyvals, targets[match_pos], digits) for match_pos in range(matches)]
    return jnp.stack([before, after] + received)


def switched_send(payload, shift_val, groups):
    def branch(shift):
        def moved(current):
            return lax.ppermute(current, "node", [(i, i ^ shift) for i in range(groups)])

        return moved

    branches = [branch(shift) for shift in range(1, groups)]
    return lax.switch(jnp.clip(shift_val - 1, 0, groups - 2), branches, payload)


def quarter_keys(node_states, w_kv, w_parts, matchings, my_index, groups, blocks_here):
    total_rows, model_width = node_states.shape
    matches = matchings.shape[0]
    heads_axis = lax.axis_size("head")
    sub_rows = ROWS // heads_axis
    me = lax.axis_index("head")
    mine = node_states.reshape(blocks_here, heads_axis, sub_rows, model_width)
    mine = lax.dynamic_index_in_dim(mine, me, axis=1, keepdims=False)
    mine = mine.reshape(blocks_here * sub_rows, model_width)
    up = [(i, i + 1) for i in range(groups - 1)]
    down = [(i + 1, i) for i in range(groups - 1)]
    before = lax.ppermute(mine, "node", up)
    after = lax.ppermute(mine, "node", down)
    targets = jnp.bitwise_xor(matchings[:, 0] // blocks_here, my_index)
    if groups <= STATIC_GROUPS:
        every = jnp.stack(
            [
                lax.ppermute(mine, "node", [(i, i ^ shift) for i in range(groups)])
                for shift in range(1, groups)
            ]
        )
        matched = [
            lax.dynamic_index_in_dim(
                every, jnp.clip(targets[match_pos] - 1, 0, groups - 2), 0, keepdims=False
            )
            for match_pos in range(matches)
        ]
    else:
        matched = [switched_send(mine, targets[match_pos], groups) for match_pos in range(matches)]
    w_parts, matched[0] = lax.optimization_barrier((w_parts, matched[0]))
    spread = [spread_slots(piece, heads_axis) for piece in [before, after] + matched]
    rows = jnp.stack(
        [
            jnp.stack(
                [one[k].reshape(blocks_here, sub_rows, model_width) for k in range(heads_axis)],
                axis=1,
            )
            for one in spread
        ]
    )
    count = len(spread)
    rows = rows.reshape(count * total_rows, model_width)
    partner_kv = jnp.dot(rows, w_kv, preferred_element_type=jnp.float32).astype(jnp.bfloat16)
    return partner_kv.reshape(count, total_rows, w_kv.shape[1]), w_parts


def attention_kernel(live_ref, pick_ref, q_ref, own_ref, part_ref, out_ref, score_ref):
    blocks_here = q_ref.shape[0]
    head_feats = q_ref.shape[2]
    pairs = head_feats // LANES
    per_pair = LANES // HEAD_DIM
    window = 2 * REACH + 1
    matches = part_ref.shape[0] - 2
    key_blocks = window + matches
    inv_root = 1.0 / math.sqrt(HEAD_DIM)
    lane = lax.broadcasted_iota(jnp.int32, (ROWS, LANES), 1)
    for j in range(blocks_here):

        def key_block(t, cols, j=j):
            if t < window:
                pos = j + t - REACH
                if pos < 0:
                    return part_ref[0, pos + blocks_here, :, cols]
                if pos < blocks_here:
                    return own_ref[pos, :, cols]
                return part_ref[1, pos - blocks_here, :, cols]
            match_pos = t - window
            return part_ref[2 + match_pos, pick_ref[match_pos, j], :, cols]

        for pair in range(pairs):
            kcols = pl.ds(pair * LANES, LANES)
            vcols = pl.ds(head_feats + pair * LANES, LANES)
            both = q_ref[j, :, kcols]
            merged = jnp.zeros((ROWS, LANES), jnp.float32)
            for half in range(per_pair):
                mine = (lane >= half * HEAD_DIM) & (lane < (half + 1) * HEAD_DIM)
                query = jnp.where(mine, both, jnp.zeros_like(both))
                highest = jnp.full((ROWS, ROWS), -jnp.inf, jnp.float32)
                for t in range(key_blocks):
                    scores = lax.dot_general(
                        query, key_block(t, kcols), (((1,), (1,)), ((), ())),
                        preferred_element_type=jnp.float32,
                    ) * inv_root
                    scores = jnp.where(live_ref[j, t] != 0, scores, -jnp.inf)
                    score_ref[t] = scores
                    highest = jnp.maximum(highest, scores)
                highest = jnp.max(highest, axis=1, keepdims=True)
                total = jnp.zeros((ROWS, ROWS), jnp.float32)
                for t in range(key_blocks):
                    weights = jnp.exp(score_ref[t] - highest)
                    score_ref[t] = weights
                    total = total + weights
                total = jnp.sum(total, axis=1, keepdims=True)
                context = jnp.zeros((ROWS, LANES), jnp.float32)
                for t in range(key_blocks):
                    probs = (score_ref[t] / total).astype(jnp.bfloat16)
                    context = context + jnp.dot(
                        probs, key_block(t, vcols), preferred_element_type=jnp.float32
                    )
                merged = jnp.where(mine, context, merged)
            out_ref[j, :, kcols] = merged.astype(jnp.bfloat16)


def attention(live, pick, query, own, part):
    blocks_here, rows, head_feats = query.shape
    key_blocks = live.shape[1]
    vmem = pltpu.VMEM
    flops = 8 * blocks_here * rows * key_blocks * rows * head_feats
    moved = 2 * (query.size * 2 + own.size + part.size)
    return pl.pallas_call(
        attention_kernel,
        out_shape=jax.ShapeDtypeStruct(query.shape, jnp.bfloat16),
        in_specs=[pl.BlockSpec(memory_space=pltpu.SMEM), pl.BlockSpec(memory_space=pltpu.SMEM),
                  pl.BlockSpec(memory_space=vmem), pl.BlockSpec(memory_space=vmem), pl.BlockSpec(memory_space=vmem)],
        out_specs=pl.BlockSpec(memory_space=vmem),
        scratch_shapes=[pltpu.VMEM((key_blocks, ROWS, ROWS), jnp.float32)],
        cost_estimate=pl.CostEstimate(
            flops=flops, transcendentals=blocks_here * rows * key_blocks * rows * 4, bytes_accessed=moved
        ),
    )(live, pick, query, own, part)

def local(node_states, w_qkv, w_out, ln_gain, ln_bias, local_mask, matchings):
    total_rows, model_width = node_states.shape
    blocks_here = total_rows // ROWS
    head_feats = w_qkv.shape[2]
    heads_here = head_feats // HEAD_DIM
    window = 2 * REACH + 1
    matches = matchings.shape[0]
    inv_root = 1.0 / math.sqrt(HEAD_DIM)
    my_index = lax.axis_index("node")
    groups = lax.axis_size("node")
    all_blocks = groups * blocks_here
    heads_axis = lax.axis_size("head")
    head_index = lax.axis_index("head")
    out_cols = ln_gain.shape[0]
    w_parts = [lax.dynamic_slice_in_dim(w_out, head_index * out_cols, out_cols, 1)] + [
        flip_heads(
            lax.dynamic_slice_in_dim(w_out, (head_index ^ flip) * out_cols, out_cols, 1),
            flip,
            heads_axis,
        )
        for flip in range(1, heads_axis)
    ]
    projected = jnp.einsum(
        "nd,dtf->ntf", node_states, w_qkv, preferred_element_type=jnp.float32
    ).astype(jnp.bfloat16)
    queries = projected[:, 0]
    keyvals = projected[:, 1:].reshape(total_rows, 2 * head_feats)
    global_blocks = my_index * blocks_here + jnp.arange(blocks_here, dtype=jnp.int32)
    offsets = jnp.arange(window, dtype=jnp.int32) - REACH
    neighbour = global_blocks[:, None] + offsets[None, :]
    if groups <= GATHER_GROUPS:
        w_kv = w_qkv[:, 1:].reshape(model_width, 2 * head_feats)
        part, w_parts = quarter_keys(
            node_states, w_kv, w_parts, matchings, my_index, groups, blocks_here
        )
    else:
        part = routed_keys(keyvals, matchings, my_index, groups, blocks_here)
    local_ok = (
        (neighbour >= 0) & (neighbour < all_blocks) & ((offsets[None, :] == 0) | (local_mask == 1))
    )
    block_ok = jnp.concatenate([local_ok, jnp.ones((blocks_here, matches), dtype=bool)], axis=1)
    context = attention(
        block_ok.astype(jnp.int32),
        (matchings % blocks_here).astype(jnp.int32),
        queries.reshape(blocks_here, ROWS, head_feats),
        keyvals.reshape(blocks_here, ROWS, 2 * head_feats),
        part.reshape(part.shape[0], blocks_here, ROWS, 2 * head_feats),
    ).reshape(total_rows, head_feats)
    context_slots = spread_slots(context, heads_axis)
    own_cols = lax.dynamic_slice_in_dim(node_states, head_index * out_cols, out_cols, 1)
    mixed_rows = own_cols.astype(jnp.float32) + jnp.einsum(
        "srf,sfo->ro",
        jnp.stack([context_slots[flip] for flip in range(heads_axis)]),
        jnp.stack(w_parts),
        preferred_element_type=jnp.float32,
    )
    part_mean = jnp.mean(mixed_rows, axis=1, keepdims=True)
    part_square = jnp.sum(jnp.square(mixed_rows - part_mean), axis=1, keepdims=True)
    stats = jnp.concatenate([part_mean, part_square], axis=1)
    all_stats = jnp.stack(
        [stats] + [flip_heads(stats, flip, heads_axis) for flip in range(1, heads_axis)]
    )
    centre = jnp.mean(all_stats[:, :, 0:1], axis=0)
    spread = (
        jnp.sum(all_stats[:, :, 1:2], axis=0)
        + out_cols * jnp.sum(jnp.square(all_stats[:, :, 0:1] - centre), axis=0)
    ) / (heads_axis * out_cols)
    normed = (mixed_rows - centre) * lax.rsqrt(spread + NORM_EPS)
    return (normed * ln_gain + ln_bias).astype(jnp.bfloat16)


def solution(mesh):
    placed = (
        P("node", None),
        P(None, None, "head"),
        P("head", None),
        P("head"),
        P("head"),
        P("node", None),
        P(None, "node"),
    )
    return jax.shard_map(
        local, mesh=mesh, in_specs=placed, out_specs=P("node", "head"), check_vma=False
    )
```

```python
import math

import jax
import jax.numpy as jnp
from jax import lax
from jax.experimental import pallas as pl
from jax.experimental.pallas import tpu as pltpu
from jax.sharding import PartitionSpec as P

HEAD_DIM = 64
ROWS = 128
REACH = 3
LANES = 128
GATHER_GROUPS = 16
STATIC_GROUPS = 8


NORM_EPS = 1e-05


def partner(array, axis, bit):
    return lax.ppermute(array, axis, [(i, i ^ 1 << bit) for i in range(lax.axis_size(axis))])


def flip_heads(array, flip, devices):
    return lax.ppermute(array, "head", [(i, i ^ flip) for i in range(devices)])


def spread_slots(piece, heads_axis):
    slots = {0: piece}
    for bit in reversed(range(heads_axis.bit_length() - 1)):
        flip = 1 << bit
        held = sorted(slots)
        other = flip_heads(jnp.stack([slots[k] for k in held]), flip, heads_axis)
        for pos, k in enumerate(held):
            slots[k ^ flip] = other[pos]
    return slots


def spread_stack(piece, heads_axis):
    slots = spread_slots(piece, heads_axis)
    return jnp.stack([slots[k] for k in range(heads_axis)])


def keep_same(current):
    return current


def route_direct(payload, shift_val, digits):
    for bit_pos in range(digits):

        def moved(current, bit_pos=bit_pos):
            return partner(current, "node", bit_pos)

        taken = jnp.bitwise_and(jnp.right_shift(shift_val, bit_pos), 1) == 1
        payload = lax.cond(taken, moved, keep_same, payload)
    return payload


def routed_keys(keyvals, matchings, my_index, groups, blocks_here):
    matches = matchings.shape[0]
    digits = groups.bit_length() - 1
    up = [(i, i + 1) for i in range(groups - 1)]
    down = [(i + 1, i) for i in range(groups - 1)]
    before = lax.ppermute(keyvals, "node", up)
    after = lax.ppermute(keyvals, "node", down)
    targets = jnp.bitwise_xor(matchings[:, 0] // blocks_here, my_index)
    received = [route_direct(keyvals, targets[match_pos], digits) for match_pos in range(matches)]
    return jnp.stack([before, after] + received)


def switched_send(payload, shift_val, groups):
    def branch(shift):
        def moved(current):
            return lax.ppermute(current, "node", [(i, i ^ shift) for i in range(groups)])

        return moved

    branches = [branch(shift) for shift in range(1, groups)]
    return lax.switch(jnp.clip(shift_val - 1, 0, groups - 2), branches, payload)


def quarter_keys(node_states, w_kv, w_parts, matchings, my_index, groups, blocks_here):
    total_rows, model_width = node_states.shape
    matches = matchings.shape[0]
    heads_axis = lax.axis_size("head")
    sub_rows = ROWS // heads_axis
    me = lax.axis_index("head")
    mine = node_states.reshape(blocks_here, heads_axis, sub_rows, model_width)
    mine = lax.dynamic_index_in_dim(mine, me, axis=1, keepdims=False)
    mine = mine.reshape(blocks_here * sub_rows, model_width)
    up = [(i, i + 1) for i in range(groups - 1)]
    down = [(i + 1, i) for i in range(groups - 1)]
    before = lax.ppermute(mine, "node", up)
    after = lax.ppermute(mine, "node", down)
    targets = jnp.bitwise_xor(matchings[:, 0] // blocks_here, my_index)
    if groups <= STATIC_GROUPS:
        every = jnp.stack(
            [
                lax.ppermute(mine, "node", [(i, i ^ shift) for i in range(groups)])
                for shift in range(1, groups)
            ]
        )
        used = [jnp.any(targets == shift) for shift in range(1, groups)]
        every = jnp.stack(
            [
                lax.cond(
                    used[pos],
                    lambda piece: spread_stack(piece, heads_axis),
                    lambda piece: idle_stack(piece, heads_axis),
                    every[pos],
                )
                for pos in range(groups - 1)
            ]
        )
        spread_matched = [
            lax.dynamic_index_in_dim(
                every, jnp.clip(targets[match_pos] - 1, 0, groups - 2), 0, keepdims=False
            )
            for match_pos in range(matches)
        ]
        w_parts, spread_matched[0] = lax.optimization_barrier((w_parts, spread_matched[0]))
        spread = [spread_stack(piece, heads_axis) for piece in [before, after]] + spread_matched
        return kv_of_spread(spread, w_kv, blocks_here, sub_rows), w_parts
    else:
        matched = [switched_send(mine, targets[match_pos], groups) for match_pos in range(matches)]
    w_parts, matched[0] = lax.optimization_barrier((w_parts, matched[0]))
    spread = [spread_stack(piece, heads_axis) for piece in [before, after] + matched]
    return kv_of_spread(spread, w_kv, blocks_here, sub_rows), w_parts


def idle_stack(piece, heads_axis):
    return jnp.zeros((heads_axis,) + piece.shape, piece.dtype)


def kv_of_spread(spread, w_kv, blocks_here, sub_rows):
    heads_axis, _, model_width = spread[0].shape
    rows = jnp.stack(
        [
            jnp.transpose(one.reshape(heads_axis, blocks_here, sub_rows, model_width), (1, 0, 2, 3))
            for one in spread
        ]
    )
    count = len(spread)
    total_rows = blocks_here * heads_axis * sub_rows
    rows = rows.reshape(count * total_rows, model_width)
    partner_kv = jnp.dot(rows, w_kv, preferred_element_type=jnp.float32).astype(jnp.bfloat16)
    return partner_kv.reshape(count, total_rows, w_kv.shape[1])


def attention_kernel(live_ref, pick_ref, q_ref, own_ref, part_ref, out_ref, score_ref):
    blocks_here = q_ref.shape[0]
    head_feats = q_ref.shape[2]
    pairs = head_feats // LANES
    per_pair = LANES // HEAD_DIM
    window = 2 * REACH + 1
    matches = part_ref.shape[0] - 2
    key_blocks = window + matches
    inv_root = 1.0 / math.sqrt(HEAD_DIM)
    lane = lax.broadcasted_iota(jnp.int32, (ROWS, LANES), 1)
    for j in range(blocks_here):

        def key_block(t, cols, j=j):
            if t < window:
                pos = j + t - REACH
                if pos < 0:
                    return part_ref[0, pos + blocks_here, :, cols]
                if pos < blocks_here:
                    return own_ref[pos, :, cols]
                return part_ref[1, pos - blocks_here, :, cols]
            match_pos = t - window
            return part_ref[2 + match_pos, pick_ref[match_pos, j], :, cols]

        for pair in range(pairs):
            kcols = pl.ds(pair * LANES, LANES)
            vcols = pl.ds(head_feats + pair * LANES, LANES)
            both = q_ref[j, :, kcols]
            merged = jnp.zeros((ROWS, LANES), jnp.float32)
            for half in range(per_pair):
                mine = (lane >= half * HEAD_DIM) & (lane < (half + 1) * HEAD_DIM)
                query = jnp.where(mine, both, jnp.zeros_like(both))
                highest = jnp.full((ROWS, ROWS), -jnp.inf, jnp.float32)
                for t in range(key_blocks):
                    scores = lax.dot_general(
                        query, key_block(t, kcols), (((1,), (1,)), ((), ())),
                        preferred_element_type=jnp.float32,
                    ) * inv_root
                    scores = jnp.where(live_ref[j, t] != 0, scores, -jnp.inf)
                    score_ref[t] = scores
                    highest = jnp.maximum(highest, scores)
                highest = jnp.max(highest, axis=1, keepdims=True)
                total = jnp.zeros((ROWS, ROWS), jnp.float32)
                for t in range(key_blocks):
                    weights = jnp.exp(score_ref[t] - highest)
                    score_ref[t] = weights
                    total = total + weights
                total = jnp.sum(total, axis=1, keepdims=True)
                context = jnp.zeros((ROWS, LANES), jnp.float32)
                for t in range(key_blocks):
                    probs = (score_ref[t] / total).astype(jnp.bfloat16)
                    context = context + jnp.dot(
                        probs, key_block(t, vcols), preferred_element_type=jnp.float32
                    )
                merged = jnp.where(mine, context, merged)
            out_ref[j, :, kcols] = merged.astype(jnp.bfloat16)


def attention(live, pick, query, own, part):
    blocks_here, rows, head_feats = query.shape
    key_blocks = live.shape[1]
    vmem = pltpu.VMEM
    flops = 8 * blocks_here * rows * key_blocks * rows * head_feats
    moved = 2 * (query.size * 2 + own.size + part.size)
    return pl.pallas_call(
        attention_kernel,
        out_shape=jax.ShapeDtypeStruct(query.shape, jnp.bfloat16),
        in_specs=[pl.BlockSpec(memory_space=pltpu.SMEM), pl.BlockSpec(memory_space=pltpu.SMEM),
                  pl.BlockSpec(memory_space=vmem), pl.BlockSpec(memory_space=vmem), pl.BlockSpec(memory_space=vmem)],
        out_specs=pl.BlockSpec(memory_space=vmem),
        scratch_shapes=[pltpu.VMEM((key_blocks, ROWS, ROWS), jnp.float32)],
        cost_estimate=pl.CostEstimate(
            flops=flops, transcendentals=blocks_here * rows * key_blocks * rows * 4, bytes_accessed=moved
        ),
    )(live, pick, query, own, part)

def local(node_states, w_qkv, w_out, ln_gain, ln_bias, local_mask, matchings):
    total_rows, model_width = node_states.shape
    blocks_here = total_rows // ROWS
    head_feats = w_qkv.shape[2]
    heads_here = head_feats // HEAD_DIM
    window = 2 * REACH + 1
    matches = matchings.shape[0]
    inv_root = 1.0 / math.sqrt(HEAD_DIM)
    my_index = lax.axis_index("node")
    groups = lax.axis_size("node")
    all_blocks = groups * blocks_here
    heads_axis = lax.axis_size("head")
    head_index = lax.axis_index("head")
    out_cols = ln_gain.shape[0]
    w_parts = [lax.dynamic_slice_in_dim(w_out, head_index * out_cols, out_cols, 1)] + [
        flip_heads(
            lax.dynamic_slice_in_dim(w_out, (head_index ^ flip) * out_cols, out_cols, 1),
            flip,
            heads_axis,
        )
        for flip in range(1, heads_axis)
    ]
    projected = jnp.einsum(
        "nd,dtf->ntf", node_states, w_qkv, preferred_element_type=jnp.float32
    ).astype(jnp.bfloat16)
    queries = projected[:, 0]
    keyvals = projected[:, 1:].reshape(total_rows, 2 * head_feats)
    global_blocks = my_index * blocks_here + jnp.arange(blocks_here, dtype=jnp.int32)
    offsets = jnp.arange(window, dtype=jnp.int32) - REACH
    neighbour = global_blocks[:, None] + offsets[None, :]
    if groups <= GATHER_GROUPS:
        w_kv = w_qkv[:, 1:].reshape(model_width, 2 * head_feats)
        part, w_parts = quarter_keys(
            node_states, w_kv, w_parts, matchings, my_index, groups, blocks_here
        )
    else:
        part = routed_keys(keyvals, matchings, my_index, groups, blocks_here)
    local_ok = (
        (neighbour >= 0) & (neighbour < all_blocks) & ((offsets[None, :] == 0) | (local_mask == 1))
    )
    block_ok = jnp.concatenate([local_ok, jnp.ones((blocks_here, matches), dtype=bool)], axis=1)
    context = attention(
        block_ok.astype(jnp.int32),
        (matchings % blocks_here).astype(jnp.int32),
        queries.reshape(blocks_here, ROWS, head_feats),
        keyvals.reshape(blocks_here, ROWS, 2 * head_feats),
        part.reshape(part.shape[0], blocks_here, ROWS, 2 * head_feats),
    ).reshape(total_rows, head_feats)
    context_slots = spread_slots(context, heads_axis)
    own_cols = lax.dynamic_slice_in_dim(node_states, head_index * out_cols, out_cols, 1)
    mixed_rows = own_cols.astype(jnp.float32) + jnp.einsum(
        "srf,sfo->ro",
        jnp.stack([context_slots[flip] for flip in range(heads_axis)]),
        jnp.stack(w_parts),
        preferred_element_type=jnp.float32,
    )
    part_mean = jnp.mean(mixed_rows, axis=1, keepdims=True)
    part_square = jnp.sum(jnp.square(mixed_rows - part_mean), axis=1, keepdims=True)
    stats = jnp.concatenate([part_mean, part_square], axis=1)
    all_stats = jnp.stack(
        [stats] + [flip_heads(stats, flip, heads_axis) for flip in range(1, heads_axis)]
    )
    centre = jnp.mean(all_stats[:, :, 0:1], axis=0)
    spread = (
        jnp.sum(all_stats[:, :, 1:2], axis=0)
        + out_cols * jnp.sum(jnp.square(all_stats[:, :, 0:1] - centre), axis=0)
    ) / (heads_axis * out_cols)
    normed = (mixed_rows - centre) * lax.rsqrt(spread + NORM_EPS)
    return (normed * ln_gain + ln_bias).astype(jnp.bfloat16)


def solution(mesh):
    placed = (
        P("node", None),
        P(None, None, "head"),
        P("head", None),
        P("head"),
        P("head"),
        P("node", None),
        P(None, "node"),
    )
    return jax.shard_map(
        local, mesh=mesh, in_specs=placed, out_specs=P("node", "head"), check_vma=False
    )
```

```python
import math

import jax
import jax.numpy as jnp
from jax import lax
from jax.experimental import pallas as pl
from jax.experimental.pallas import tpu as pltpu
from jax.sharding import PartitionSpec as P

HEAD_DIM = 64
ROWS = 128
REACH = 3
LANES = 128
GATHER_GROUPS = 16
STATIC_GROUPS = 8


NORM_EPS = 1e-05


def partner(array, axis, bit):
    return lax.ppermute(array, axis, [(i, i ^ 1 << bit) for i in range(lax.axis_size(axis))])


def flip_heads(array, flip, devices):
    return lax.ppermute(array, "head", [(i, i ^ flip) for i in range(devices)])


def spread_slots(piece, heads_axis):
    slots = {0: piece}
    for bit in reversed(range(heads_axis.bit_length() - 1)):
        flip = 1 << bit
        held = sorted(slots)
        other = flip_heads(jnp.stack([slots[k] for k in held]), flip, heads_axis)
        for pos, k in enumerate(held):
            slots[k ^ flip] = other[pos]
    return slots


def keep_same(current):
    return current


def route_direct(payload, shift_val, digits):
    for bit_pos in range(digits):

        def moved(current, bit_pos=bit_pos):
            return partner(current, "node", bit_pos)

        taken = jnp.bitwise_and(jnp.right_shift(shift_val, bit_pos), 1) == 1
        payload = lax.cond(taken, moved, keep_same, payload)
    return payload


def routed_keys(keyvals, matchings, my_index, groups, blocks_here):
    matches = matchings.shape[0]
    digits = groups.bit_length() - 1
    up = [(i, i + 1) for i in range(groups - 1)]
    down = [(i + 1, i) for i in range(groups - 1)]
    before = lax.ppermute(keyvals, "node", up)
    after = lax.ppermute(keyvals, "node", down)
    targets = jnp.bitwise_xor(matchings[:, 0] // blocks_here, my_index)
    received = [route_direct(keyvals, targets[match_pos], digits) for match_pos in range(matches)]
    return jnp.stack([before, after] + received)


def switched_send(payload, shift_val, groups):
    def branch(shift):
        def moved(current):
            return lax.ppermute(current, "node", [(i, i ^ shift) for i in range(groups)])

        return moved

    branches = [branch(shift) for shift in range(1, groups)]
    return lax.switch(jnp.clip(shift_val - 1, 0, groups - 2), branches, payload)


def quarter_keys(node_states, w_kv, w_parts, matchings, my_index, groups, blocks_here):
    total_rows, model_width = node_states.shape
    matches = matchings.shape[0]
    heads_axis = lax.axis_size("head")
    sub_rows = ROWS // heads_axis
    me = lax.axis_index("head")
    mine = node_states.reshape(blocks_here, heads_axis, sub_rows, model_width)
    mine = lax.dynamic_index_in_dim(mine, me, axis=1, keepdims=False)
    mine = mine.reshape(blocks_here * sub_rows, model_width)
    targets = jnp.bitwise_xor(matchings[:, 0] // blocks_here, my_index)
    if groups <= STATIC_GROUPS:
        return static_keys(mine, w_kv, w_parts, targets, my_index, groups, blocks_here, sub_rows)
    up = [(i, i + 1) for i in range(groups - 1)]
    down = [(i + 1, i) for i in range(groups - 1)]
    before = lax.ppermute(mine, "node", up)
    after = lax.ppermute(mine, "node", down)
    matched = [switched_send(mine, targets[match_pos], groups) for match_pos in range(matches)]
    w_parts, matched[0] = lax.optimization_barrier((w_parts, matched[0]))
    spread = [spread_stack(piece, heads_axis) for piece in [before, after] + matched]
    return kv_of_spread(spread, w_kv, blocks_here, sub_rows), w_parts


def static_keys(mine, w_kv, w_parts, targets, my_index, groups, blocks_here, sub_rows):
    heads_axis = lax.axis_size("head")
    matches = targets.shape[0]
    far = [(j, j + 1) for j in range(1, groups - 1, 2)] + [(j, j - 1) for j in range(2, groups, 2)]
    other = spread_stack(lax.ppermute(mine, "node", far), heads_axis)
    every = jnp.stack(
        [
            spread_stack(
                lax.ppermute(mine, "node", [(i, i ^ shift) for i in range(groups)]), heads_axis
            )
            for shift in range(1, groups)
        ]
    )
    odd = (my_index % 2) == 1
    before = jnp.where(odd, every[0], other)
    after = jnp.where(odd, other, every[0])
    matched = [
        lax.dynamic_index_in_dim(
            every, jnp.clip(targets[match_pos] - 1, 0, groups - 2), 0, keepdims=False
        )
        for match_pos in range(matches)
    ]
    w_parts, matched[0] = lax.optimization_barrier((w_parts, matched[0]))
    return kv_of_spread([before, after] + matched, w_kv, blocks_here, sub_rows), w_parts


def spread_stack(piece, heads_axis):
    slots = spread_slots(piece, heads_axis)
    return jnp.stack([slots[k] for k in range(heads_axis)])


def kv_of_spread(spread, w_kv, blocks_here, sub_rows):
    heads_axis, _, model_width = spread[0].shape
    rows = jnp.stack(
        [
            jnp.transpose(one.reshape(heads_axis, blocks_here, sub_rows, model_width), (1, 0, 2, 3))
            for one in spread
        ]
    )
    count = len(spread)
    total_rows = blocks_here * heads_axis * sub_rows
    rows = rows.reshape(count * total_rows, model_width)
    partner_kv = jnp.dot(rows, w_kv, preferred_element_type=jnp.float32).astype(jnp.bfloat16)
    return partner_kv.reshape(count, total_rows, w_kv.shape[1])


def attention_kernel(live_ref, pick_ref, q_ref, own_ref, part_ref, out_ref, score_ref):
    blocks_here = q_ref.shape[0]
    head_feats = q_ref.shape[2]
    pairs = head_feats // LANES
    per_pair = LANES // HEAD_DIM
    window = 2 * REACH + 1
    matches = part_ref.shape[0] - 2
    key_blocks = window + matches
    inv_root = 1.0 / math.sqrt(HEAD_DIM)
    lane = lax.broadcasted_iota(jnp.int32, (ROWS, LANES), 1)
    for j in range(blocks_here):

        def key_block(t, cols, j=j):
            if t < window:
                pos = j + t - REACH
                if pos < 0:
                    return part_ref[0, pos + blocks_here, :, cols]
                if pos < blocks_here:
                    return own_ref[pos, :, cols]
                return part_ref[1, pos - blocks_here, :, cols]
            match_pos = t - window
            return part_ref[2 + match_pos, pick_ref[match_pos, j], :, cols]

        for pair in range(pairs):
            kcols = pl.ds(pair * LANES, LANES)
            vcols = pl.ds(head_feats + pair * LANES, LANES)
            both = q_ref[j, :, kcols]
            merged = jnp.zeros((ROWS, LANES), jnp.float32)
            for half in range(per_pair):
                mine = (lane >= half * HEAD_DIM) & (lane < (half + 1) * HEAD_DIM)
                query = jnp.where(mine, both, jnp.zeros_like(both))
                highest = jnp.full((ROWS, ROWS), -jnp.inf, jnp.float32)
                for t in range(key_blocks):
                    scores = lax.dot_general(
                        query, key_block(t, kcols), (((1,), (1,)), ((), ())),
                        preferred_element_type=jnp.float32,
                    ) * inv_root
                    scores = jnp.where(live_ref[j, t] != 0, scores, -jnp.inf)
                    score_ref[t] = scores
                    highest = jnp.maximum(highest, scores)
                highest = jnp.max(highest, axis=1, keepdims=True)
                total = jnp.zeros((ROWS, ROWS), jnp.float32)
                for t in range(key_blocks):
                    weights = jnp.exp(score_ref[t] - highest)
                    score_ref[t] = weights
                    total = total + weights
                total = jnp.sum(total, axis=1, keepdims=True)
                context = jnp.zeros((ROWS, LANES), jnp.float32)
                for t in range(key_blocks):
                    probs = (score_ref[t] / total).astype(jnp.bfloat16)
                    context = context + jnp.dot(
                        probs, key_block(t, vcols), preferred_element_type=jnp.float32
                    )
                merged = jnp.where(mine, context, merged)
            out_ref[j, :, kcols] = merged.astype(jnp.bfloat16)


def attention(live, pick, query, own, part):
    blocks_here, rows, head_feats = query.shape
    key_blocks = live.shape[1]
    vmem = pltpu.VMEM
    flops = 8 * blocks_here * rows * key_blocks * rows * head_feats
    moved = 2 * (query.size * 2 + own.size + part.size)
    return pl.pallas_call(
        attention_kernel,
        out_shape=jax.ShapeDtypeStruct(query.shape, jnp.bfloat16),
        in_specs=[pl.BlockSpec(memory_space=pltpu.SMEM), pl.BlockSpec(memory_space=pltpu.SMEM),
                  pl.BlockSpec(memory_space=vmem), pl.BlockSpec(memory_space=vmem), pl.BlockSpec(memory_space=vmem)],
        out_specs=pl.BlockSpec(memory_space=vmem),
        scratch_shapes=[pltpu.VMEM((key_blocks, ROWS, ROWS), jnp.float32)],
        cost_estimate=pl.CostEstimate(
            flops=flops, transcendentals=blocks_here * rows * key_blocks * rows * 4, bytes_accessed=moved
        ),
    )(live, pick, query, own, part)

def local(node_states, w_qkv, w_out, ln_gain, ln_bias, local_mask, matchings):
    total_rows, model_width = node_states.shape
    blocks_here = total_rows // ROWS
    head_feats = w_qkv.shape[2]
    heads_here = head_feats // HEAD_DIM
    window = 2 * REACH + 1
    matches = matchings.shape[0]
    inv_root = 1.0 / math.sqrt(HEAD_DIM)
    my_index = lax.axis_index("node")
    groups = lax.axis_size("node")
    all_blocks = groups * blocks_here
    heads_axis = lax.axis_size("head")
    head_index = lax.axis_index("head")
    out_cols = ln_gain.shape[0]
    w_parts = [lax.dynamic_slice_in_dim(w_out, head_index * out_cols, out_cols, 1)] + [
        flip_heads(
            lax.dynamic_slice_in_dim(w_out, (head_index ^ flip) * out_cols, out_cols, 1),
            flip,
            heads_axis,
        )
        for flip in range(1, heads_axis)
    ]
    projected = jnp.einsum(
        "nd,dtf->ntf", node_states, w_qkv, preferred_element_type=jnp.float32
    ).astype(jnp.bfloat16)
    queries = projected[:, 0]
    keyvals = projected[:, 1:].reshape(total_rows, 2 * head_feats)
    global_blocks = my_index * blocks_here + jnp.arange(blocks_here, dtype=jnp.int32)
    offsets = jnp.arange(window, dtype=jnp.int32) - REACH
    neighbour = global_blocks[:, None] + offsets[None, :]
    if groups <= GATHER_GROUPS:
        w_kv = w_qkv[:, 1:].reshape(model_width, 2 * head_feats)
        part, w_parts = quarter_keys(
            node_states, w_kv, w_parts, matchings, my_index, groups, blocks_here
        )
    else:
        part = routed_keys(keyvals, matchings, my_index, groups, blocks_here)
    local_ok = (
        (neighbour >= 0) & (neighbour < all_blocks) & ((offsets[None, :] == 0) | (local_mask == 1))
    )
    block_ok = jnp.concatenate([local_ok, jnp.ones((blocks_here, matches), dtype=bool)], axis=1)
    context = attention(
        block_ok.astype(jnp.int32),
        (matchings % blocks_here).astype(jnp.int32),
        queries.reshape(blocks_here, ROWS, head_feats),
        keyvals.reshape(blocks_here, ROWS, 2 * head_feats),
        part.reshape(part.shape[0], blocks_here, ROWS, 2 * head_feats),
    ).reshape(total_rows, head_feats)
    context_slots = spread_slots(context, heads_axis)
    own_cols = lax.dynamic_slice_in_dim(node_states, head_index * out_cols, out_cols, 1)
    mixed_rows = own_cols.astype(jnp.float32) + jnp.einsum(
        "srf,sfo->ro",
        jnp.stack([context_slots[flip] for flip in range(heads_axis)]),
        jnp.stack(w_parts),
        preferred_element_type=jnp.float32,
    )
    part_mean = jnp.mean(mixed_rows, axis=1, keepdims=True)
    part_square = jnp.sum(jnp.square(mixed_rows - part_mean), axis=1, keepdims=True)
    stats = jnp.concatenate([part_mean, part_square], axis=1)
    all_stats = jnp.stack(
        [stats] + [flip_heads(stats, flip, heads_axis) for flip in range(1, heads_axis)]
    )
    centre = jnp.mean(all_stats[:, :, 0:1], axis=0)
    spread = (
        jnp.sum(all_stats[:, :, 1:2], axis=0)
        + out_cols * jnp.sum(jnp.square(all_stats[:, :, 0:1] - centre), axis=0)
    ) / (heads_axis * out_cols)
    normed = (mixed_rows - centre) * lax.rsqrt(spread + NORM_EPS)
    return (normed * ln_gain + ln_bias).astype(jnp.bfloat16)


def solution(mesh):
    placed = (
        P("node", None),
        P(None, None, "head"),
        P("head", None),
        P("head"),
        P("head"),
        P("node", None),
        P(None, "node"),
    )
    return jax.shard_map(
        local, mesh=mesh, in_specs=placed, out_specs=P("node", "head"), check_vma=False
    )
```

```python
import math

import jax
import jax.numpy as jnp
from jax import lax
from jax.experimental import pallas as pl
from jax.experimental.pallas import tpu as pltpu
from jax.sharding import PartitionSpec as P

HEAD_DIM = 64
ROWS = 128
REACH = 3
LANES = 128
GATHER_GROUPS = 16
STATIC_GROUPS = 8


NORM_EPS = 1e-05


def partner(array, axis, bit):
    return lax.ppermute(array, axis, [(i, i ^ 1 << bit) for i in range(lax.axis_size(axis))])


def flip_heads(array, flip, devices):
    return lax.ppermute(array, "head", [(i, i ^ flip) for i in range(devices)])


def spread_slots(piece, heads_axis):
    slots = {0: piece}
    for bit in reversed(range(heads_axis.bit_length() - 1)):
        flip = 1 << bit
        held = sorted(slots)
        other = flip_heads(jnp.stack([slots[k] for k in held]), flip, heads_axis)
        for pos, k in enumerate(held):
            slots[k ^ flip] = other[pos]
    return slots


def keep_same(current):
    return current


def route_direct(payload, shift_val, digits):
    for bit_pos in range(digits):

        def moved(current, bit_pos=bit_pos):
            return partner(current, "node", bit_pos)

        taken = jnp.bitwise_and(jnp.right_shift(shift_val, bit_pos), 1) == 1
        payload = lax.cond(taken, moved, keep_same, payload)
    return payload


def routed_keys(keyvals, matchings, my_index, groups, blocks_here):
    matches = matchings.shape[0]
    digits = groups.bit_length() - 1
    up = [(i, i + 1) for i in range(groups - 1)]
    down = [(i + 1, i) for i in range(groups - 1)]
    before = lax.ppermute(keyvals, "node", up)
    after = lax.ppermute(keyvals, "node", down)
    targets = jnp.bitwise_xor(matchings[:, 0] // blocks_here, my_index)
    received = [route_direct(keyvals, targets[match_pos], digits) for match_pos in range(matches)]
    return jnp.stack([before, after] + received)


def switched_send(payload, shift_val, groups):
    def branch(shift):
        def moved(current):
            return lax.ppermute(current, "node", [(i, i ^ shift) for i in range(groups)])

        return moved

    branches = [branch(shift) for shift in range(1, groups)]
    return lax.switch(jnp.clip(shift_val - 1, 0, groups - 2), branches, payload)


def quarter_keys(node_states, w_kv, w_parts, matchings, my_index, groups, blocks_here):
    total_rows, model_width = node_states.shape
    matches = matchings.shape[0]
    heads_axis = lax.axis_size("head")
    sub_rows = ROWS // heads_axis
    me = lax.axis_index("head")
    mine = node_states.reshape(blocks_here, heads_axis, sub_rows, model_width)
    mine = lax.dynamic_index_in_dim(mine, me, axis=1, keepdims=False)
    mine = mine.reshape(blocks_here * sub_rows, model_width)
    targets = jnp.bitwise_xor(matchings[:, 0] // blocks_here, my_index)
    if groups <= STATIC_GROUPS:
        return static_keys(mine, w_kv, w_parts, targets, my_index, groups, blocks_here, sub_rows)
    up = [(i, i + 1) for i in range(groups - 1)]
    down = [(i + 1, i) for i in range(groups - 1)]
    before = lax.ppermute(mine, "node", up)
    after = lax.ppermute(mine, "node", down)
    matched = [switched_send(mine, targets[match_pos], groups) for match_pos in range(matches)]
    w_parts, matched[0] = lax.optimization_barrier((w_parts, matched[0]))
    spread = [spread_stack(piece, heads_axis) for piece in [before, after] + matched]
    return kv_of_spread(spread, w_kv, blocks_here, sub_rows), w_parts


def static_keys(mine, w_kv, w_parts, targets, my_index, groups, blocks_here, sub_rows):
    heads_axis = lax.axis_size("head")
    matches = targets.shape[0]
    far = [(j, j + 1) for j in range(1, groups - 1, 2)] + [(j, j - 1) for j in range(2, groups, 2)]

    def arrived(piece):
        return kv_of_piece(spread_stack(piece, heads_axis), w_kv, blocks_here, sub_rows)

    other = arrived(lax.ppermute(mine, "node", far))
    every = jnp.stack(
        [
            arrived(lax.ppermute(mine, "node", [(i, i ^ shift) for i in range(groups)]))
            for shift in range(1, groups)
        ]
    )
    odd = (my_index % 2) == 1
    before = jnp.where(odd, every[0], other)
    after = jnp.where(odd, other, every[0])
    matched = [
        lax.dynamic_index_in_dim(
            every, jnp.clip(targets[match_pos] - 1, 0, groups - 2), 0, keepdims=False
        )
        for match_pos in range(matches)
    ]
    w_parts, matched[0] = lax.optimization_barrier((w_parts, matched[0]))
    return jnp.stack([before, after] + matched), w_parts


def kv_of_piece(full, w_kv, blocks_here, sub_rows):
    heads_axis, _, model_width = full.shape
    total_rows = heads_axis * blocks_here * sub_rows
    kv = jnp.dot(full.reshape(total_rows, model_width), w_kv, preferred_element_type=jnp.float32)
    kv = kv.astype(jnp.bfloat16).reshape(heads_axis, blocks_here, sub_rows, -1)
    return jnp.transpose(kv, (1, 0, 2, 3)).reshape(total_rows, -1)


def spread_stack(piece, heads_axis):
    slots = spread_slots(piece, heads_axis)
    return jnp.stack([slots[k] for k in range(heads_axis)])


def kv_of_spread(spread, w_kv, blocks_here, sub_rows):
    heads_axis, _, model_width = spread[0].shape
    rows = jnp.stack(
        [
            jnp.transpose(one.reshape(heads_axis, blocks_here, sub_rows, model_width), (1, 0, 2, 3))
            for one in spread
        ]
    )
    count = len(spread)
    total_rows = blocks_here * heads_axis * sub_rows
    rows = rows.reshape(count * total_rows, model_width)
    partner_kv = jnp.dot(rows, w_kv, preferred_element_type=jnp.float32).astype(jnp.bfloat16)
    return partner_kv.reshape(count, total_rows, w_kv.shape[1])


def attention_kernel(live_ref, pick_ref, q_ref, own_ref, part_ref, out_ref, score_ref):
    blocks_here = q_ref.shape[0]
    head_feats = q_ref.shape[2]
    pairs = head_feats // LANES
    per_pair = LANES // HEAD_DIM
    window = 2 * REACH + 1
    matches = part_ref.shape[0] - 2
    key_blocks = window + matches
    inv_root = 1.0 / math.sqrt(HEAD_DIM)
    lane = lax.broadcasted_iota(jnp.int32, (ROWS, LANES), 1)
    for j in range(blocks_here):

        def key_block(t, cols, j=j):
            if t < window:
                pos = j + t - REACH
                if pos < 0:
                    return part_ref[0, pos + blocks_here, :, cols]
                if pos < blocks_here:
                    return own_ref[pos, :, cols]
                return part_ref[1, pos - blocks_here, :, cols]
            match_pos = t - window
            return part_ref[2 + match_pos, pick_ref[match_pos, j], :, cols]

        for pair in range(pairs):
            kcols = pl.ds(pair * LANES, LANES)
            vcols = pl.ds(head_feats + pair * LANES, LANES)
            both = q_ref[j, :, kcols]
            merged = jnp.zeros((ROWS, LANES), jnp.float32)
            for half in range(per_pair):
                mine = (lane >= half * HEAD_DIM) & (lane < (half + 1) * HEAD_DIM)
                query = jnp.where(mine, both, jnp.zeros_like(both))
                highest = jnp.full((ROWS, ROWS), -jnp.inf, jnp.float32)
                for t in range(key_blocks):
                    scores = lax.dot_general(
                        query, key_block(t, kcols), (((1,), (1,)), ((), ())),
                        preferred_element_type=jnp.float32,
                    ) * inv_root
                    scores = jnp.where(live_ref[j, t] != 0, scores, -jnp.inf)
                    score_ref[t] = scores
                    highest = jnp.maximum(highest, scores)
                highest = jnp.max(highest, axis=1, keepdims=True)
                total = jnp.zeros((ROWS, ROWS), jnp.float32)
                for t in range(key_blocks):
                    weights = jnp.exp(score_ref[t] - highest)
                    score_ref[t] = weights
                    total = total + weights
                total = jnp.sum(total, axis=1, keepdims=True)
                context = jnp.zeros((ROWS, LANES), jnp.float32)
                for t in range(key_blocks):
                    probs = (score_ref[t] / total).astype(jnp.bfloat16)
                    context = context + jnp.dot(
                        probs, key_block(t, vcols), preferred_element_type=jnp.float32
                    )
                merged = jnp.where(mine, context, merged)
            out_ref[j, :, kcols] = merged.astype(jnp.bfloat16)


def attention(live, pick, query, own, part):
    blocks_here, rows, head_feats = query.shape
    key_blocks = live.shape[1]
    vmem = pltpu.VMEM
    flops = 8 * blocks_here * rows * key_blocks * rows * head_feats
    moved = 2 * (query.size * 2 + own.size + part.size)
    return pl.pallas_call(
        attention_kernel,
        out_shape=jax.ShapeDtypeStruct(query.shape, jnp.bfloat16),
        in_specs=[pl.BlockSpec(memory_space=pltpu.SMEM), pl.BlockSpec(memory_space=pltpu.SMEM),
                  pl.BlockSpec(memory_space=vmem), pl.BlockSpec(memory_space=vmem), pl.BlockSpec(memory_space=vmem)],
        out_specs=pl.BlockSpec(memory_space=vmem),
        scratch_shapes=[pltpu.VMEM((key_blocks, ROWS, ROWS), jnp.float32)],
        cost_estimate=pl.CostEstimate(
            flops=flops, transcendentals=blocks_here * rows * key_blocks * rows * 4, bytes_accessed=moved
        ),
    )(live, pick, query, own, part)

def local(node_states, w_qkv, w_out, ln_gain, ln_bias, local_mask, matchings):
    total_rows, model_width = node_states.shape
    blocks_here = total_rows // ROWS
    head_feats = w_qkv.shape[2]
    heads_here = head_feats // HEAD_DIM
    window = 2 * REACH + 1
    matches = matchings.shape[0]
    inv_root = 1.0 / math.sqrt(HEAD_DIM)
    my_index = lax.axis_index("node")
    groups = lax.axis_size("node")
    all_blocks = groups * blocks_here
    heads_axis = lax.axis_size("head")
    head_index = lax.axis_index("head")
    out_cols = ln_gain.shape[0]
    w_parts = [lax.dynamic_slice_in_dim(w_out, head_index * out_cols, out_cols, 1)] + [
        flip_heads(
            lax.dynamic_slice_in_dim(w_out, (head_index ^ flip) * out_cols, out_cols, 1),
            flip,
            heads_axis,
        )
        for flip in range(1, heads_axis)
    ]
    projected = jnp.einsum(
        "nd,dtf->ntf", node_states, w_qkv, preferred_element_type=jnp.float32
    ).astype(jnp.bfloat16)
    queries = projected[:, 0]
    keyvals = projected[:, 1:].reshape(total_rows, 2 * head_feats)
    global_blocks = my_index * blocks_here + jnp.arange(blocks_here, dtype=jnp.int32)
    offsets = jnp.arange(window, dtype=jnp.int32) - REACH
    neighbour = global_blocks[:, None] + offsets[None, :]
    if groups <= GATHER_GROUPS:
        w_kv = w_qkv[:, 1:].reshape(model_width, 2 * head_feats)
        part, w_parts = quarter_keys(
            node_states, w_kv, w_parts, matchings, my_index, groups, blocks_here
        )
    else:
        part = routed_keys(keyvals, matchings, my_index, groups, blocks_here)
    local_ok = (
        (neighbour >= 0) & (neighbour < all_blocks) & ((offsets[None, :] == 0) | (local_mask == 1))
    )
    block_ok = jnp.concatenate([local_ok, jnp.ones((blocks_here, matches), dtype=bool)], axis=1)
    context = attention(
        block_ok.astype(jnp.int32),
        (matchings % blocks_here).astype(jnp.int32),
        queries.reshape(blocks_here, ROWS, head_feats),
        keyvals.reshape(blocks_here, ROWS, 2 * head_feats),
        part.reshape(part.shape[0], blocks_here, ROWS, 2 * head_feats),
    ).reshape(total_rows, head_feats)
    context_slots = spread_slots(context, heads_axis)
    own_cols = lax.dynamic_slice_in_dim(node_states, head_index * out_cols, out_cols, 1)
    mixed_rows = own_cols.astype(jnp.float32) + jnp.einsum(
        "srf,sfo->ro",
        jnp.stack([context_slots[flip] for flip in range(heads_axis)]),
        jnp.stack(w_parts),
        preferred_element_type=jnp.float32,
    )
    part_mean = jnp.mean(mixed_rows, axis=1, keepdims=True)
    part_square = jnp.sum(jnp.square(mixed_rows - part_mean), axis=1, keepdims=True)
    stats = jnp.concatenate([part_mean, part_square], axis=1)
    all_stats = jnp.stack(
        [stats] + [flip_heads(stats, flip, heads_axis) for flip in range(1, heads_axis)]
    )
    centre = jnp.mean(all_stats[:, :, 0:1], axis=0)
    spread = (
        jnp.sum(all_stats[:, :, 1:2], axis=0)
        + out_cols * jnp.sum(jnp.square(all_stats[:, :, 0:1] - centre), axis=0)
    ) / (heads_axis * out_cols)
    normed = (mixed_rows - centre) * lax.rsqrt(spread + NORM_EPS)
    return (normed * ln_gain + ln_bias).astype(jnp.bfloat16)


def solution(mesh):
    placed = (
        P("node", None),
        P(None, None, "head"),
        P("head", None),
        P("head"),
        P("head"),
        P("node", None),
        P(None, "node"),
    )
    return jax.shard_map(
        local, mesh=mesh, in_specs=placed, out_specs=P("node", "head"), check_vma=False
    )
```

```python
import math

import jax
import jax.numpy as jnp
from jax import lax
from jax.experimental import pallas as pl
from jax.experimental.pallas import tpu as pltpu
from jax.sharding import PartitionSpec as P

HEAD_DIM = 64
ROWS = 128
REACH = 3
LANES = 128
GATHER_GROUPS = 16
STATIC_GROUPS = 8


NORM_EPS = 1e-05


def partner(array, axis, bit):
    return lax.ppermute(array, axis, [(i, i ^ 1 << bit) for i in range(lax.axis_size(axis))])


def flip_heads(array, flip, devices):
    return lax.ppermute(array, "head", [(i, i ^ flip) for i in range(devices)])


def spread_slots(piece, heads_axis):
    slots = {0: piece}
    for bit in reversed(range(heads_axis.bit_length() - 1)):
        flip = 1 << bit
        held = sorted(slots)
        other = flip_heads(jnp.stack([slots[k] for k in held]), flip, heads_axis)
        for pos, k in enumerate(held):
            slots[k ^ flip] = other[pos]
    return slots


def keep_same(current):
    return current


def route_direct(payload, shift_val, digits):
    for bit_pos in range(digits):

        def moved(current, bit_pos=bit_pos):
            return partner(current, "node", bit_pos)

        taken = jnp.bitwise_and(jnp.right_shift(shift_val, bit_pos), 1) == 1
        payload = lax.cond(taken, moved, keep_same, payload)
    return payload


def routed_keys(keyvals, matchings, my_index, groups, blocks_here):
    matches = matchings.shape[0]
    digits = groups.bit_length() - 1
    up = [(i, i + 1) for i in range(groups - 1)]
    down = [(i + 1, i) for i in range(groups - 1)]
    before = lax.ppermute(keyvals, "node", up)
    after = lax.ppermute(keyvals, "node", down)
    targets = jnp.bitwise_xor(matchings[:, 0] // blocks_here, my_index)
    received = [route_direct(keyvals, targets[match_pos], digits) for match_pos in range(matches)]
    return jnp.stack([before, after] + received)


def switched_send(payload, shift_val, groups):
    def branch(shift):
        def moved(current):
            return lax.ppermute(current, "node", [(i, i ^ shift) for i in range(groups)])

        return moved

    branches = [branch(shift) for shift in range(1, groups)]
    return lax.switch(jnp.clip(shift_val - 1, 0, groups - 2), branches, payload)


def quarter_keys(node_states, w_kv, w_parts, matchings, my_index, groups, blocks_here):
    total_rows, model_width = node_states.shape
    matches = matchings.shape[0]
    heads_axis = lax.axis_size("head")
    sub_rows = ROWS // heads_axis
    me = lax.axis_index("head")
    mine = node_states.reshape(blocks_here, heads_axis, sub_rows, model_width)
    mine = lax.dynamic_index_in_dim(mine, me, axis=1, keepdims=False)
    mine = mine.reshape(blocks_here * sub_rows, model_width)
    targets = jnp.bitwise_xor(matchings[:, 0] // blocks_here, my_index)
    if groups <= STATIC_GROUPS:
        return static_keys(mine, w_kv, w_parts, targets, my_index, groups, blocks_here, sub_rows)
    up = [(i, i + 1) for i in range(groups - 1)]
    down = [(i + 1, i) for i in range(groups - 1)]
    before = lax.ppermute(mine, "node", up)
    after = lax.ppermute(mine, "node", down)
    matched = [switched_send(mine, targets[match_pos], groups) for match_pos in range(matches)]
    w_parts, matched[0] = lax.optimization_barrier((w_parts, matched[0]))
    spread = [spread_stack(piece, heads_axis) for piece in [before, after] + matched]
    return kv_of_spread(spread, w_kv, blocks_here, sub_rows), w_parts


def static_keys(mine, w_kv, w_parts, targets, my_index, groups, blocks_here, sub_rows):
    heads_axis = lax.axis_size("head")
    matches = targets.shape[0]
    far = [(j, j + 1) for j in range(1, groups - 1, 2)] + [(j, j - 1) for j in range(2, groups, 2)]
    other = spread_stack(lax.ppermute(mine, "node", far), heads_axis)
    every = jnp.stack(
        [
            spread_stack(
                lax.ppermute(mine, "node", [(i, i ^ shift) for i in range(groups)]), heads_axis
            )
            for shift in range(1, groups)
        ]
    )
    odd = (my_index % 2) == 1
    before = jnp.where(odd, every[0], other)
    after = jnp.where(odd, other, every[0])
    matched = [
        lax.dynamic_index_in_dim(
            every, jnp.clip(targets[match_pos] - 1, 0, groups - 2), 0, keepdims=False
        )
        for match_pos in range(matches)
    ]
    w_parts, matched[0] = lax.optimization_barrier((w_parts, matched[0]))
    return kv_of_spread([before, after] + matched, w_kv, blocks_here, sub_rows), w_parts


def spread_stack(piece, heads_axis):
    slots = spread_slots(piece, heads_axis)
    return jnp.stack([slots[k] for k in range(heads_axis)])


def kv_of_spread(spread, w_kv, blocks_here, sub_rows):
    heads_axis, _, model_width = spread[0].shape
    rows = jnp.stack(
        [
            jnp.transpose(one.reshape(heads_axis, blocks_here, sub_rows, model_width), (1, 0, 2, 3))
            for one in spread
        ]
    )
    count = len(spread)
    total_rows = blocks_here * heads_axis * sub_rows
    rows = rows.reshape(count * total_rows, model_width)
    partner_kv = jnp.dot(rows, w_kv, preferred_element_type=jnp.float32).astype(jnp.bfloat16)
    return partner_kv.reshape(count, total_rows, w_kv.shape[1])


def attention_kernel(
    live_ref, pick_ref, q_ref, own_ref, part_ref, out_ref, score_ref, high_ref, total_ref, sum_ref
):
    blocks_here = q_ref.shape[0]
    head_feats = q_ref.shape[2]
    pairs = head_feats // LANES
    per_pair = LANES // HEAD_DIM
    window = 2 * REACH + 1
    matches = part_ref.shape[0] - 2
    key_blocks = window + matches
    inv_root = 1.0 / math.sqrt(HEAD_DIM)
    lane = lax.broadcasted_iota(jnp.int32, (ROWS, LANES), 1)
    for j in range(blocks_here):

        def key_block(t, cols, j=j):
            if t < window:
                pos = j + t - REACH
                if pos < 0:
                    return part_ref[0, pos + blocks_here, :, cols]
                if pos < blocks_here:
                    return own_ref[pos, :, cols]
                return part_ref[1, pos - blocks_here, :, cols]
            match_pos = t - window
            return part_ref[2 + match_pos, pick_ref[match_pos, j], :, cols]

        def when_live(t, body, j=j):
            if t < window:
                pl.when(live_ref[j, t] != 0)(body)
            else:
                body()

        for pair in range(pairs):
            kcols = pl.ds(pair * LANES, LANES)
            vcols = pl.ds(head_feats + pair * LANES, LANES)
            both = q_ref[j, :, kcols]
            merged = jnp.zeros((ROWS, LANES), jnp.float32)
            for half in range(per_pair):
                mine = (lane >= half * HEAD_DIM) & (lane < (half + 1) * HEAD_DIM)
                query = jnp.where(mine, both, jnp.zeros_like(both))
                high_ref[...] = jnp.full((ROWS, ROWS), -jnp.inf, jnp.float32)
                for t in range(key_blocks):

                    def first(t=t, query=query, kcols=kcols):
                        scores = lax.dot_general(
                            query, key_block(t, kcols), (((1,), (1,)), ((), ())),
                            preferred_element_type=jnp.float32,
                        ) * inv_root
                        score_ref[t] = scores
                        high_ref[...] = jnp.maximum(high_ref[...], scores)

                    when_live(t, first)
                highest = jnp.max(high_ref[...], axis=1, keepdims=True)
                total_ref[...] = jnp.zeros((ROWS, ROWS), jnp.float32)
                for t in range(key_blocks):

                    def second(t=t, highest=highest):
                        weights = jnp.exp(score_ref[t] - highest)
                        score_ref[t] = weights
                        total_ref[...] = total_ref[...] + weights

                    when_live(t, second)
                total = jnp.sum(total_ref[...], axis=1, keepdims=True)
                sum_ref[...] = jnp.zeros((ROWS, LANES), jnp.float32)
                for t in range(key_blocks):

                    def third(t=t, total=total, vcols=vcols):
                        probs = (score_ref[t] / total).astype(jnp.bfloat16)
                        sum_ref[...] = sum_ref[...] + jnp.dot(
                            probs, key_block(t, vcols), preferred_element_type=jnp.float32
                        )

                    when_live(t, third)
                merged = jnp.where(mine, sum_ref[...], merged)
            out_ref[j, :, kcols] = merged.astype(jnp.bfloat16)


def attention(live, pick, query, own, part):
    blocks_here, rows, head_feats = query.shape
    key_blocks = live.shape[1]
    vmem = pltpu.VMEM
    flops = 8 * blocks_here * rows * key_blocks * rows * head_feats
    moved = 2 * (query.size * 2 + own.size + part.size)
    return pl.pallas_call(
        attention_kernel,
        out_shape=jax.ShapeDtypeStruct(query.shape, jnp.bfloat16),
        in_specs=[pl.BlockSpec(memory_space=pltpu.SMEM), pl.BlockSpec(memory_space=pltpu.SMEM),
                  pl.BlockSpec(memory_space=vmem), pl.BlockSpec(memory_space=vmem), pl.BlockSpec(memory_space=vmem)],
        out_specs=pl.BlockSpec(memory_space=vmem),
        scratch_shapes=[
            pltpu.VMEM((key_blocks, ROWS, ROWS), jnp.float32),
            pltpu.VMEM((ROWS, ROWS), jnp.float32),
            pltpu.VMEM((ROWS, ROWS), jnp.float32),
            pltpu.VMEM((ROWS, LANES), jnp.float32),
        ],
        cost_estimate=pl.CostEstimate(
            flops=flops, transcendentals=blocks_here * rows * key_blocks * rows * 4, bytes_accessed=moved
        ),
    )(live, pick, query, own, part)

def local(node_states, w_qkv, w_out, ln_gain, ln_bias, local_mask, matchings):
    total_rows, model_width = node_states.shape
    blocks_here = total_rows // ROWS
    head_feats = w_qkv.shape[2]
    heads_here = head_feats // HEAD_DIM
    window = 2 * REACH + 1
    matches = matchings.shape[0]
    inv_root = 1.0 / math.sqrt(HEAD_DIM)
    my_index = lax.axis_index("node")
    groups = lax.axis_size("node")
    all_blocks = groups * blocks_here
    heads_axis = lax.axis_size("head")
    head_index = lax.axis_index("head")
    out_cols = ln_gain.shape[0]
    w_parts = [lax.dynamic_slice_in_dim(w_out, head_index * out_cols, out_cols, 1)] + [
        flip_heads(
            lax.dynamic_slice_in_dim(w_out, (head_index ^ flip) * out_cols, out_cols, 1),
            flip,
            heads_axis,
        )
        for flip in range(1, heads_axis)
    ]
    projected = jnp.einsum(
        "nd,dtf->ntf", node_states, w_qkv, preferred_element_type=jnp.float32
    ).astype(jnp.bfloat16)
    queries = projected[:, 0]
    keyvals = projected[:, 1:].reshape(total_rows, 2 * head_feats)
    global_blocks = my_index * blocks_here + jnp.arange(blocks_here, dtype=jnp.int32)
    offsets = jnp.arange(window, dtype=jnp.int32) - REACH
    neighbour = global_blocks[:, None] + offsets[None, :]
    if groups <= GATHER_GROUPS:
        w_kv = w_qkv[:, 1:].reshape(model_width, 2 * head_feats)
        part, w_parts = quarter_keys(
            node_states, w_kv, w_parts, matchings, my_index, groups, blocks_here
        )
    else:
        part = routed_keys(keyvals, matchings, my_index, groups, blocks_here)
    local_ok = (
        (neighbour >= 0) & (neighbour < all_blocks) & ((offsets[None, :] == 0) | (local_mask == 1))
    )
    block_ok = jnp.concatenate([local_ok, jnp.ones((blocks_here, matches), dtype=bool)], axis=1)
    context = attention(
        block_ok.astype(jnp.int32),
        (matchings % blocks_here).astype(jnp.int32),
        queries.reshape(blocks_here, ROWS, head_feats),
        keyvals.reshape(blocks_here, ROWS, 2 * head_feats),
        part.reshape(part.shape[0], blocks_here, ROWS, 2 * head_feats),
    ).reshape(total_rows, head_feats)
    context_slots = spread_slots(context, heads_axis)
    own_cols = lax.dynamic_slice_in_dim(node_states, head_index * out_cols, out_cols, 1)
    mixed_rows = own_cols.astype(jnp.float32) + jnp.einsum(
        "srf,sfo->ro",
        jnp.stack([context_slots[flip] for flip in range(heads_axis)]),
        jnp.stack(w_parts),
        preferred_element_type=jnp.float32,
    )
    part_mean = jnp.mean(mixed_rows, axis=1, keepdims=True)
    part_square = jnp.sum(jnp.square(mixed_rows - part_mean), axis=1, keepdims=True)
    stats = jnp.concatenate([part_mean, part_square], axis=1)
    all_stats = jnp.stack(
        [stats] + [flip_heads(stats, flip, heads_axis) for flip in range(1, heads_axis)]
    )
    centre = jnp.mean(all_stats[:, :, 0:1], axis=0)
    spread = (
        jnp.sum(all_stats[:, :, 1:2], axis=0)
        + out_cols * jnp.sum(jnp.square(all_stats[:, :, 0:1] - centre), axis=0)
    ) / (heads_axis * out_cols)
    normed = (mixed_rows - centre) * lax.rsqrt(spread + NORM_EPS)
    return (normed * ln_gain + ln_bias).astype(jnp.bfloat16)


def solution(mesh):
    placed = (
        P("node", None),
        P(None, None, "head"),
        P("head", None),
        P("head"),
        P("head"),
        P("node", None),
        P(None, "node"),
    )
    return jax.shard_map(
        local, mesh=mesh, in_specs=placed, out_specs=P("node", "head"), check_vma=False
    )
```

```python
import functools
import math

import jax
import jax.numpy as jnp
from jax import lax
from jax.experimental import pallas as pl
from jax.experimental.pallas import tpu as pltpu
from jax.sharding import PartitionSpec as P

HEAD_DIM = 64
ROWS = 128
REACH = 3
LANES = 128
GATHER_GROUPS = 16
STATIC_GROUPS = 8


NORM_EPS = 1e-05


def partner(array, axis, bit):
    return lax.ppermute(array, axis, [(i, i ^ 1 << bit) for i in range(lax.axis_size(axis))])


def flip_heads(array, flip, devices):
    return lax.ppermute(array, "head", [(i, i ^ flip) for i in range(devices)])


def spread_slots(piece, heads_axis):
    slots = {0: piece}
    for bit in reversed(range(heads_axis.bit_length() - 1)):
        flip = 1 << bit
        held = sorted(slots)
        other = flip_heads(jnp.stack([slots[k] for k in held]), flip, heads_axis)
        for pos, k in enumerate(held):
            slots[k ^ flip] = other[pos]
    return slots


def keep_same(current):
    return current


def route_direct(payload, shift_val, digits):
    for bit_pos in range(digits):

        def moved(current, bit_pos=bit_pos):
            return partner(current, "node", bit_pos)

        taken = jnp.bitwise_and(jnp.right_shift(shift_val, bit_pos), 1) == 1
        payload = lax.cond(taken, moved, keep_same, payload)
    return payload


def routed_keys(keyvals, matchings, my_index, groups, blocks_here):
    matches = matchings.shape[0]
    digits = groups.bit_length() - 1
    up = [(i, i + 1) for i in range(groups - 1)]
    down = [(i + 1, i) for i in range(groups - 1)]
    before = lax.ppermute(keyvals, "node", up)
    after = lax.ppermute(keyvals, "node", down)
    targets = jnp.bitwise_xor(matchings[:, 0] // blocks_here, my_index)
    received = [route_direct(keyvals, targets[match_pos], digits) for match_pos in range(matches)]
    return jnp.stack([before, after] + received)


def switched_send(payload, shift_val, groups):
    def branch(shift):
        def moved(current):
            return lax.ppermute(current, "node", [(i, i ^ shift) for i in range(groups)])

        return moved

    branches = [branch(shift) for shift in range(1, groups)]
    return lax.switch(jnp.clip(shift_val - 1, 0, groups - 2), branches, payload)


def quarter_keys(node_states, w_kv, w_parts, matchings, my_index, groups, blocks_here):
    total_rows, model_width = node_states.shape
    matches = matchings.shape[0]
    heads_axis = lax.axis_size("head")
    sub_rows = ROWS // heads_axis
    me = lax.axis_index("head")
    mine = node_states.reshape(blocks_here, heads_axis, sub_rows, model_width)
    mine = lax.dynamic_index_in_dim(mine, me, axis=1, keepdims=False)
    mine = mine.reshape(blocks_here * sub_rows, model_width)
    targets = jnp.bitwise_xor(matchings[:, 0] // blocks_here, my_index)
    if groups <= STATIC_GROUPS:
        return static_keys(mine, w_kv, w_parts, targets, my_index, groups, blocks_here, sub_rows)
    up = [(i, i + 1) for i in range(groups - 1)]
    down = [(i + 1, i) for i in range(groups - 1)]
    before = lax.ppermute(mine, "node", up)
    after = lax.ppermute(mine, "node", down)
    matched = [switched_send(mine, targets[match_pos], groups) for match_pos in range(matches)]
    w_parts, matched[0] = lax.optimization_barrier((w_parts, matched[0]))
    spread = [spread_stack(piece, heads_axis) for piece in [before, after] + matched]
    return kv_of_spread(spread, w_kv, blocks_here, sub_rows), w_parts


def static_keys(mine, w_kv, w_parts, targets, my_index, groups, blocks_here, sub_rows):
    heads_axis = lax.axis_size("head")
    matches = targets.shape[0]
    far = [(j, j + 1) for j in range(1, groups - 1, 2)] + [(j, j - 1) for j in range(2, groups, 2)]
    other = spread_stack(lax.ppermute(mine, "node", far), heads_axis)
    every = jnp.stack(
        [
            spread_stack(
                lax.ppermute(mine, "node", [(i, i ^ shift) for i in range(groups)]), heads_axis
            )
            for shift in range(1, groups)
        ]
    )
    odd = (my_index % 2) == 1
    before = jnp.where(odd, every[0], other)
    after = jnp.where(odd, other, every[0])
    matched = [
        lax.dynamic_index_in_dim(
            every, jnp.clip(targets[match_pos] - 1, 0, groups - 2), 0, keepdims=False
        )
        for match_pos in range(matches)
    ]
    w_parts, matched[0] = lax.optimization_barrier((w_parts, matched[0]))
    return kv_of_spread([before, after] + matched, w_kv, blocks_here, sub_rows), w_parts


def spread_stack(piece, heads_axis):
    slots = spread_slots(piece, heads_axis)
    return jnp.stack([slots[k] for k in range(heads_axis)])


def kv_of_spread(spread, w_kv, blocks_here, sub_rows):
    heads_axis, _, model_width = spread[0].shape
    rows = jnp.stack(
        [
            jnp.transpose(one.reshape(heads_axis, blocks_here, sub_rows, model_width), (1, 0, 2, 3))
            for one in spread
        ]
    )
    count = len(spread)
    total_rows = blocks_here * heads_axis * sub_rows
    rows = rows.reshape(count * total_rows, model_width)
    partner_kv = jnp.dot(rows, w_kv, preferred_element_type=jnp.float32).astype(jnp.bfloat16)
    return partner_kv.reshape(count, total_rows, w_kv.shape[1])


def attention_kernel(pair, live_ref, pick_ref, q_ref, own_ref, part_ref, out_ref, score_ref):
    blocks_here = q_ref.shape[0]
    head_feats = q_ref.shape[2]
    per_pair = LANES // HEAD_DIM
    window = 2 * REACH + 1
    matches = part_ref.shape[0] - 2
    key_blocks = window + matches
    inv_root = 1.0 / math.sqrt(HEAD_DIM)
    lane = lax.broadcasted_iota(jnp.int32, (ROWS, LANES), 1)
    for j in range(blocks_here):

        def key_block(t, cols, j=j):
            if t < window:
                pos = j + t - REACH
                if pos < 0:
                    return part_ref[0, pos + blocks_here, :, cols]
                if pos < blocks_here:
                    return own_ref[pos, :, cols]
                return part_ref[1, pos - blocks_here, :, cols]
            match_pos = t - window
            return part_ref[2 + match_pos, pick_ref[match_pos, j], :, cols]

        for pair in [pair]:
            kcols = pl.ds(pair * LANES, LANES)
            vcols = pl.ds(head_feats + pair * LANES, LANES)
            both = q_ref[j, :, kcols]
            merged = jnp.zeros((ROWS, LANES), jnp.float32)
            for half in range(per_pair):
                mine = (lane >= half * HEAD_DIM) & (lane < (half + 1) * HEAD_DIM)
                query = jnp.where(mine, both, jnp.zeros_like(both))
                highest = jnp.full((ROWS, ROWS), -jnp.inf, jnp.float32)
                for t in range(key_blocks):
                    scores = lax.dot_general(
                        query, key_block(t, kcols), (((1,), (1,)), ((), ())),
                        preferred_element_type=jnp.float32,
                    ) * inv_root
                    scores = jnp.where(live_ref[j, t] != 0, scores, -jnp.inf)
                    score_ref[t] = scores
                    highest = jnp.maximum(highest, scores)
                highest = jnp.max(highest, axis=1, keepdims=True)
                total = jnp.zeros((ROWS, ROWS), jnp.float32)
                for t in range(key_blocks):
                    weights = jnp.exp(score_ref[t] - highest)
                    score_ref[t] = weights
                    total = total + weights
                total = jnp.sum(total, axis=1, keepdims=True)
                context = jnp.zeros((ROWS, LANES), jnp.float32)
                for t in range(key_blocks):
                    probs = (score_ref[t] / total).astype(jnp.bfloat16)
                    context = context + jnp.dot(
                        probs, key_block(t, vcols), preferred_element_type=jnp.float32
                    )
                merged = jnp.where(mine, context, merged)
            out_ref[j] = merged.astype(jnp.bfloat16)


def attention(live, pick, query, own, part, pair):
    blocks_here, rows, head_feats = query.shape
    key_blocks = live.shape[1]
    vmem = pltpu.VMEM
    flops = 8 * blocks_here * rows * key_blocks * rows * LANES
    moved = 2 * (query.size + own.size + part.size) // 2
    return pl.pallas_call(
        functools.partial(attention_kernel, pair),
        out_shape=jax.ShapeDtypeStruct((blocks_here, rows, LANES), jnp.bfloat16),
        in_specs=[pl.BlockSpec(memory_space=pltpu.SMEM), pl.BlockSpec(memory_space=pltpu.SMEM),
                  pl.BlockSpec(memory_space=vmem), pl.BlockSpec(memory_space=vmem), pl.BlockSpec(memory_space=vmem)],
        out_specs=pl.BlockSpec(memory_space=vmem),
        scratch_shapes=[pltpu.VMEM((key_blocks, ROWS, ROWS), jnp.float32)],
        cost_estimate=pl.CostEstimate(
            flops=flops, transcendentals=blocks_here * rows * key_blocks * rows * 4, bytes_accessed=moved
        ),
    )(live, pick, query, own, part)

def local(node_states, w_qkv, w_out, ln_gain, ln_bias, local_mask, matchings):
    total_rows, model_width = node_states.shape
    blocks_here = total_rows // ROWS
    head_feats = w_qkv.shape[2]
    heads_here = head_feats // HEAD_DIM
    window = 2 * REACH + 1
    matches = matchings.shape[0]
    inv_root = 1.0 / math.sqrt(HEAD_DIM)
    my_index = lax.axis_index("node")
    groups = lax.axis_size("node")
    all_blocks = groups * blocks_here
    heads_axis = lax.axis_size("head")
    head_index = lax.axis_index("head")
    out_cols = ln_gain.shape[0]
    w_parts = [lax.dynamic_slice_in_dim(w_out, head_index * out_cols, out_cols, 1)] + [
        flip_heads(
            lax.dynamic_slice_in_dim(w_out, (head_index ^ flip) * out_cols, out_cols, 1),
            flip,
            heads_axis,
        )
        for flip in range(1, heads_axis)
    ]
    projected = jnp.einsum(
        "nd,dtf->ntf", node_states, w_qkv, preferred_element_type=jnp.float32
    ).astype(jnp.bfloat16)
    queries = projected[:, 0]
    keyvals = projected[:, 1:].reshape(total_rows, 2 * head_feats)
    global_blocks = my_index * blocks_here + jnp.arange(blocks_here, dtype=jnp.int32)
    offsets = jnp.arange(window, dtype=jnp.int32) - REACH
    neighbour = global_blocks[:, None] + offsets[None, :]
    if groups <= GATHER_GROUPS:
        w_kv = w_qkv[:, 1:].reshape(model_width, 2 * head_feats)
        part, w_parts = quarter_keys(
            node_states, w_kv, w_parts, matchings, my_index, groups, blocks_here
        )
    else:
        part = routed_keys(keyvals, matchings, my_index, groups, blocks_here)
    local_ok = (
        (neighbour >= 0) & (neighbour < all_blocks) & ((offsets[None, :] == 0) | (local_mask == 1))
    )
    block_ok = jnp.concatenate([local_ok, jnp.ones((blocks_here, matches), dtype=bool)], axis=1)
    per_pair = []
    for pair in range(head_feats // LANES):
        pair_context = attention(
            block_ok.astype(jnp.int32),
            (matchings % blocks_here).astype(jnp.int32),
            queries.reshape(blocks_here, ROWS, head_feats),
            keyvals.reshape(blocks_here, ROWS, 2 * head_feats),
            part.reshape(part.shape[0], blocks_here, ROWS, 2 * head_feats),
            pair,
        ).reshape(total_rows, LANES)
        per_pair.append(spread_slots(pair_context, heads_axis))
    context_slots = {
        flip: jnp.concatenate([slots[flip] for slots in per_pair], axis=1)
        for flip in range(heads_axis)
    }
    own_cols = lax.dynamic_slice_in_dim(node_states, head_index * out_cols, out_cols, 1)
    mixed_rows = own_cols.astype(jnp.float32) + jnp.einsum(
        "srf,sfo->ro",
        jnp.stack([context_slots[flip] for flip in range(heads_axis)]),
        jnp.stack(w_parts),
        preferred_element_type=jnp.float32,
    )
    part_mean = jnp.mean(mixed_rows, axis=1, keepdims=True)
    part_square = jnp.sum(jnp.square(mixed_rows - part_mean), axis=1, keepdims=True)
    stats = jnp.concatenate([part_mean, part_square], axis=1)
    all_stats = jnp.stack(
        [stats] + [flip_heads(stats, flip, heads_axis) for flip in range(1, heads_axis)]
    )
    centre = jnp.mean(all_stats[:, :, 0:1], axis=0)
    spread = (
        jnp.sum(all_stats[:, :, 1:2], axis=0)
        + out_cols * jnp.sum(jnp.square(all_stats[:, :, 0:1] - centre), axis=0)
    ) / (heads_axis * out_cols)
    normed = (mixed_rows - centre) * lax.rsqrt(spread + NORM_EPS)
    return (normed * ln_gain + ln_bias).astype(jnp.bfloat16)


def solution(mesh):
    placed = (
        P("node", None),
        P(None, None, "head"),
        P("head", None),
        P("head"),
        P("head"),
        P("node", None),
        P(None, "node"),
    )
    return jax.shard_map(
        local, mesh=mesh, in_specs=placed, out_specs=P("node", "head"), check_vma=False
    )
```

```python
import math

import jax
import jax.numpy as jnp
from jax import lax
from jax.experimental import pallas as pl
from jax.experimental.pallas import tpu as pltpu
from jax.sharding import PartitionSpec as P

HEAD_DIM = 64
ROWS = 128
REACH = 3
LANES = 128
GATHER_GROUPS = 16
STATIC_GROUPS = 8
NEAR_SHIFTS = 4


NORM_EPS = 1e-05


def partner(array, axis, bit):
    return lax.ppermute(array, axis, [(i, i ^ 1 << bit) for i in range(lax.axis_size(axis))])


def flip_heads(array, flip, devices):
    return lax.ppermute(array, "head", [(i, i ^ flip) for i in range(devices)])


def spread_slots(piece, heads_axis):
    slots = {0: piece}
    for bit in reversed(range(heads_axis.bit_length() - 1)):
        flip = 1 << bit
        held = sorted(slots)
        other = flip_heads(jnp.stack([slots[k] for k in held]), flip, heads_axis)
        for pos, k in enumerate(held):
            slots[k ^ flip] = other[pos]
    return slots


def keep_same(current):
    return current


def route_direct(payload, shift_val, digits):
    for bit_pos in range(digits):

        def moved(current, bit_pos=bit_pos):
            return partner(current, "node", bit_pos)

        taken = jnp.bitwise_and(jnp.right_shift(shift_val, bit_pos), 1) == 1
        payload = lax.cond(taken, moved, keep_same, payload)
    return payload


def routed_keys(keyvals, matchings, my_index, groups, blocks_here):
    matches = matchings.shape[0]
    digits = groups.bit_length() - 1
    up = [(i, i + 1) for i in range(groups - 1)]
    down = [(i + 1, i) for i in range(groups - 1)]
    before = lax.ppermute(keyvals, "node", up)
    after = lax.ppermute(keyvals, "node", down)
    targets = jnp.bitwise_xor(matchings[:, 0] // blocks_here, my_index)
    received = [route_direct(keyvals, targets[match_pos], digits) for match_pos in range(matches)]
    return jnp.stack([before, after] + received)


def switched_send(payload, shift_val, groups):
    def branch(shift):
        def moved(current):
            return lax.ppermute(current, "node", [(i, i ^ shift) for i in range(groups)])

        return moved

    branches = [branch(shift) for shift in range(1, groups)]
    return lax.switch(jnp.clip(shift_val - 1, 0, groups - 2), branches, payload)


def quarter_keys(node_states, w_kv, w_parts, matchings, my_index, groups, blocks_here):
    total_rows, model_width = node_states.shape
    matches = matchings.shape[0]
    heads_axis = lax.axis_size("head")
    sub_rows = ROWS // heads_axis
    me = lax.axis_index("head")
    mine = node_states.reshape(blocks_here, heads_axis, sub_rows, model_width)
    mine = lax.dynamic_index_in_dim(mine, me, axis=1, keepdims=False)
    mine = mine.reshape(blocks_here * sub_rows, model_width)
    targets = jnp.bitwise_xor(matchings[:, 0] // blocks_here, my_index)
    if groups <= STATIC_GROUPS:
        return static_keys(
            node_states, mine, w_kv, w_parts, targets, my_index, groups, blocks_here, sub_rows
        )
    up = [(i, i + 1) for i in range(groups - 1)]
    down = [(i + 1, i) for i in range(groups - 1)]
    before = lax.ppermute(mine, "node", up)
    after = lax.ppermute(mine, "node", down)
    matched = [switched_send(mine, targets[match_pos], groups) for match_pos in range(matches)]
    w_parts, matched[0] = lax.optimization_barrier((w_parts, matched[0]))
    spread = [spread_stack(piece, heads_axis) for piece in [before, after] + matched]
    return kv_of_spread(spread, w_kv, blocks_here, sub_rows), w_parts


def static_keys(
    node_states, mine, w_kv, w_parts, targets, my_index, groups, blocks_here, sub_rows
):
    heads_axis = lax.axis_size("head")
    matches = targets.shape[0]
    far = [(j, j + 1) for j in range(1, groups - 1, 2)] + [(j, j - 1) for j in range(2, groups, 2)]
    other = spread_stack(lax.ppermute(mine, "node", far), heads_axis)
    near = near_rows(node_states, blocks_here, sub_rows)
    every = jnp.stack(
        [
            pair_stack(
                lax.ppermute(near, "node", [(i, i ^ shift) for i in range(groups)]), heads_axis
            )
            if shift < NEAR_SHIFTS and heads_axis == 4
            else spread_stack(
                lax.ppermute(mine, "node", [(i, i ^ shift) for i in range(groups)]), heads_axis
            )
            for shift in range(1, groups)
        ]
    )
    odd = (my_index % 2) == 1
    before = jnp.where(odd, every[0], other)
    after = jnp.where(odd, other, every[0])
    matched = [
        lax.dynamic_index_in_dim(
            every, jnp.clip(targets[match_pos] - 1, 0, groups - 2), 0, keepdims=False
        )
        for match_pos in range(matches)
    ]
    w_parts, matched[0] = lax.optimization_barrier((w_parts, matched[0]))
    return kv_of_spread([before, after] + matched, w_kv, blocks_here, sub_rows), w_parts


def near_rows(node_states, blocks_here, sub_rows):
    model_width = node_states.shape[1]
    me = lax.axis_index("head")
    parts = node_states.reshape(blocks_here, 4, sub_rows, model_width)
    return jnp.stack(
        [
            lax.dynamic_index_in_dim(parts, me ^ flip, axis=1, keepdims=False).reshape(
                blocks_here * sub_rows, model_width
            )
            for flip in (0, 2)
        ]
    )


def pair_stack(received, heads_axis):
    beside = flip_heads(received, 1, heads_axis)
    return jnp.stack([received[0], beside[0], received[1], beside[1]])


def spread_stack(piece, heads_axis):
    slots = spread_slots(piece, heads_axis)
    return jnp.stack([slots[k] for k in range(heads_axis)])


def kv_of_spread(spread, w_kv, blocks_here, sub_rows):
    heads_axis, _, model_width = spread[0].shape
    rows = jnp.stack(
        [
            jnp.transpose(one.reshape(heads_axis, blocks_here, sub_rows, model_width), (1, 0, 2, 3))
            for one in spread
        ]
    )
    count = len(spread)
    total_rows = blocks_here * heads_axis * sub_rows
    rows = rows.reshape(count * total_rows, model_width)
    partner_kv = jnp.dot(rows, w_kv, preferred_element_type=jnp.float32).astype(jnp.bfloat16)
    return partner_kv.reshape(count, total_rows, w_kv.shape[1])


def attention_kernel(live_ref, pick_ref, q_ref, own_ref, part_ref, out_ref, score_ref):
    blocks_here = q_ref.shape[0]
    head_feats = q_ref.shape[2]
    pairs = head_feats // LANES
    per_pair = LANES // HEAD_DIM
    window = 2 * REACH + 1
    matches = part_ref.shape[0] - 2
    key_blocks = window + matches
    inv_root = 1.0 / math.sqrt(HEAD_DIM)
    lane = lax.broadcasted_iota(jnp.int32, (ROWS, LANES), 1)
    for j in range(blocks_here):

        def key_block(t, cols, j=j):
            if t < window:
                pos = j + t - REACH
                if pos < 0:
                    return part_ref[0, pos + blocks_here, :, cols]
                if pos < blocks_here:
                    return own_ref[pos, :, cols]
                return part_ref[1, pos - blocks_here, :, cols]
            match_pos = t - window
            return part_ref[2 + match_pos, pick_ref[match_pos, j], :, cols]

        for pair in range(pairs):
            kcols = pl.ds(pair * LANES, LANES)
            vcols = pl.ds(head_feats + pair * LANES, LANES)
            both = q_ref[j, :, kcols]
            merged = jnp.zeros((ROWS, LANES), jnp.float32)
            for half in range(per_pair):
                mine = (lane >= half * HEAD_DIM) & (lane < (half + 1) * HEAD_DIM)
                query = jnp.where(mine, both, jnp.zeros_like(both))
                highest = jnp.full((ROWS, ROWS), -jnp.inf, jnp.float32)
                for t in range(key_blocks):
                    scores = lax.dot_general(
                        query, key_block(t, kcols), (((1,), (1,)), ((), ())),
                        preferred_element_type=jnp.float32,
                    ) * inv_root
                    scores = jnp.where(live_ref[j, t] != 0, scores, -jnp.inf)
                    score_ref[t] = scores
                    highest = jnp.maximum(highest, scores)
                highest = jnp.max(highest, axis=1, keepdims=True)
                total = jnp.zeros((ROWS, ROWS), jnp.float32)
                for t in range(key_blocks):
                    weights = jnp.exp(score_ref[t] - highest)
                    score_ref[t] = weights
                    total = total + weights
                total = jnp.sum(total, axis=1, keepdims=True)
                context = jnp.zeros((ROWS, LANES), jnp.float32)
                for t in range(key_blocks):
                    probs = (score_ref[t] / total).astype(jnp.bfloat16)
                    context = context + jnp.dot(
                        probs, key_block(t, vcols), preferred_element_type=jnp.float32
                    )
                merged = jnp.where(mine, context, merged)
            out_ref[j, :, kcols] = merged.astype(jnp.bfloat16)


def attention(live, pick, query, own, part):
    blocks_here, rows, head_feats = query.shape
    key_blocks = live.shape[1]
    vmem = pltpu.VMEM
    flops = 8 * blocks_here * rows * key_blocks * rows * head_feats
    moved = 2 * (query.size * 2 + own.size + part.size)
    return pl.pallas_call(
        attention_kernel,
        out_shape=jax.ShapeDtypeStruct(query.shape, jnp.bfloat16),
        in_specs=[pl.BlockSpec(memory_space=pltpu.SMEM), pl.BlockSpec(memory_space=pltpu.SMEM),
                  pl.BlockSpec(memory_space=vmem), pl.BlockSpec(memory_space=vmem), pl.BlockSpec(memory_space=vmem)],
        out_specs=pl.BlockSpec(memory_space=vmem),
        scratch_shapes=[pltpu.VMEM((key_blocks, ROWS, ROWS), jnp.float32)],
        cost_estimate=pl.CostEstimate(
            flops=flops, transcendentals=blocks_here * rows * key_blocks * rows * 4, bytes_accessed=moved
        ),
    )(live, pick, query, own, part)

def local(node_states, w_qkv, w_out, ln_gain, ln_bias, local_mask, matchings):
    total_rows, model_width = node_states.shape
    blocks_here = total_rows // ROWS
    head_feats = w_qkv.shape[2]
    heads_here = head_feats // HEAD_DIM
    window = 2 * REACH + 1
    matches = matchings.shape[0]
    inv_root = 1.0 / math.sqrt(HEAD_DIM)
    my_index = lax.axis_index("node")
    groups = lax.axis_size("node")
    all_blocks = groups * blocks_here
    heads_axis = lax.axis_size("head")
    head_index = lax.axis_index("head")
    out_cols = ln_gain.shape[0]
    w_parts = [lax.dynamic_slice_in_dim(w_out, head_index * out_cols, out_cols, 1)] + [
        flip_heads(
            lax.dynamic_slice_in_dim(w_out, (head_index ^ flip) * out_cols, out_cols, 1),
            flip,
            heads_axis,
        )
        for flip in range(1, heads_axis)
    ]
    projected = jnp.einsum(
        "nd,dtf->ntf", node_states, w_qkv, preferred_element_type=jnp.float32
    ).astype(jnp.bfloat16)
    queries = projected[:, 0]
    keyvals = projected[:, 1:].reshape(total_rows, 2 * head_feats)
    global_blocks = my_index * blocks_here + jnp.arange(blocks_here, dtype=jnp.int32)
    offsets = jnp.arange(window, dtype=jnp.int32) - REACH
    neighbour = global_blocks[:, None] + offsets[None, :]
    if groups <= GATHER_GROUPS:
        w_kv = w_qkv[:, 1:].reshape(model_width, 2 * head_feats)
        part, w_parts = quarter_keys(
            node_states, w_kv, w_parts, matchings, my_index, groups, blocks_here
        )
    else:
        part = routed_keys(keyvals, matchings, my_index, groups, blocks_here)
    local_ok = (
        (neighbour >= 0) & (neighbour < all_blocks) & ((offsets[None, :] == 0) | (local_mask == 1))
    )
    block_ok = jnp.concatenate([local_ok, jnp.ones((blocks_here, matches), dtype=bool)], axis=1)
    context = attention(
        block_ok.astype(jnp.int32),
        (matchings % blocks_here).astype(jnp.int32),
        queries.reshape(blocks_here, ROWS, head_feats),
        keyvals.reshape(blocks_here, ROWS, 2 * head_feats),
        part.reshape(part.shape[0], blocks_here, ROWS, 2 * head_feats),
    ).reshape(total_rows, head_feats)
    context_slots = spread_slots(context, heads_axis)
    own_cols = lax.dynamic_slice_in_dim(node_states, head_index * out_cols, out_cols, 1)
    mixed_rows = own_cols.astype(jnp.float32) + jnp.einsum(
        "srf,sfo->ro",
        jnp.stack([context_slots[flip] for flip in range(heads_axis)]),
        jnp.stack(w_parts),
        preferred_element_type=jnp.float32,
    )
    part_mean = jnp.mean(mixed_rows, axis=1, keepdims=True)
    part_square = jnp.sum(jnp.square(mixed_rows - part_mean), axis=1, keepdims=True)
    stats = jnp.concatenate([part_mean, part_square], axis=1)
    all_stats = jnp.stack(
        [stats] + [flip_heads(stats, flip, heads_axis) for flip in range(1, heads_axis)]
    )
    centre = jnp.mean(all_stats[:, :, 0:1], axis=0)
    spread = (
        jnp.sum(all_stats[:, :, 1:2], axis=0)
        + out_cols * jnp.sum(jnp.square(all_stats[:, :, 0:1] - centre), axis=0)
    ) / (heads_axis * out_cols)
    normed = (mixed_rows - centre) * lax.rsqrt(spread + NORM_EPS)
    return (normed * ln_gain + ln_bias).astype(jnp.bfloat16)


def solution(mesh):
    placed = (
        P("node", None),
        P(None, None, "head"),
        P("head", None),
        P("head"),
        P("head"),
        P("node", None),
        P(None, "node"),
    )
    return jax.shard_map(
        local, mesh=mesh, in_specs=placed, out_specs=P("node", "head"), check_vma=False
    )
```

```python
import math

import jax
import jax.numpy as jnp
from jax import lax
from jax.experimental import pallas as pl
from jax.experimental.pallas import tpu as pltpu
from jax.sharding import PartitionSpec as P

HEAD_DIM = 64
ROWS = 128
REACH = 3
LANES = 128
GATHER_GROUPS = 16
STATIC_GROUPS = 8
NEAR_SHIFTS = 4


NORM_EPS = 1e-05


def partner(array, axis, bit):
    return lax.ppermute(array, axis, [(i, i ^ 1 << bit) for i in range(lax.axis_size(axis))])


def flip_heads(array, flip, devices):
    return lax.ppermute(array, "head", [(i, i ^ flip) for i in range(devices)])


def spread_slots(piece, heads_axis):
    slots = {0: piece}
    for bit in reversed(range(heads_axis.bit_length() - 1)):
        flip = 1 << bit
        held = sorted(slots)
        other = flip_heads(jnp.stack([slots[k] for k in held]), flip, heads_axis)
        for pos, k in enumerate(held):
            slots[k ^ flip] = other[pos]
    return slots


def keep_same(current):
    return current


def route_direct(payload, shift_val, digits):
    for bit_pos in range(digits):

        def moved(current, bit_pos=bit_pos):
            return partner(current, "node", bit_pos)

        taken = jnp.bitwise_and(jnp.right_shift(shift_val, bit_pos), 1) == 1
        payload = lax.cond(taken, moved, keep_same, payload)
    return payload


def routed_keys(keyvals, matchings, my_index, groups, blocks_here):
    matches = matchings.shape[0]
    digits = groups.bit_length() - 1
    up = [(i, i + 1) for i in range(groups - 1)]
    down = [(i + 1, i) for i in range(groups - 1)]
    before = lax.ppermute(keyvals, "node", up)
    after = lax.ppermute(keyvals, "node", down)
    targets = jnp.bitwise_xor(matchings[:, 0] // blocks_here, my_index)
    received = [route_direct(keyvals, targets[match_pos], digits) for match_pos in range(matches)]
    return jnp.stack([before, after] + received)


def switched_send(payload, shift_val, groups):
    def branch(shift):
        def moved(current):
            return lax.ppermute(current, "node", [(i, i ^ shift) for i in range(groups)])

        return moved

    branches = [branch(shift) for shift in range(1, groups)]
    return lax.switch(jnp.clip(shift_val - 1, 0, groups - 2), branches, payload)


def quarter_keys(node_states, w_kv, w_parts, matchings, my_index, groups, blocks_here):
    total_rows, model_width = node_states.shape
    matches = matchings.shape[0]
    heads_axis = lax.axis_size("head")
    sub_rows = ROWS // heads_axis
    me = lax.axis_index("head")
    mine = node_states.reshape(blocks_here, heads_axis, sub_rows, model_width)
    mine = lax.dynamic_index_in_dim(mine, me, axis=1, keepdims=False)
    mine = mine.reshape(blocks_here * sub_rows, model_width)
    targets = jnp.bitwise_xor(matchings[:, 0] // blocks_here, my_index)
    if groups <= STATIC_GROUPS:
        return static_keys(
            node_states, mine, w_kv, w_parts, targets, my_index, groups, blocks_here, sub_rows
        )
    up = [(i, i + 1) for i in range(groups - 1)]
    down = [(i + 1, i) for i in range(groups - 1)]
    before = lax.ppermute(mine, "node", up)
    after = lax.ppermute(mine, "node", down)
    matched = [switched_send(mine, targets[match_pos], groups) for match_pos in range(matches)]
    w_parts, matched[0] = lax.optimization_barrier((w_parts, matched[0]))
    spread = [spread_stack(piece, heads_axis) for piece in [before, after] + matched]
    return kv_of_spread(spread, w_kv, blocks_here, sub_rows), w_parts


def static_keys(
    node_states, mine, w_kv, w_parts, targets, my_index, groups, blocks_here, sub_rows
):
    heads_axis = lax.axis_size("head")
    matches = targets.shape[0]
    far = [(j, j + 1) for j in range(1, groups - 1, 2)] + [(j, j - 1) for j in range(2, groups, 2)]
    near = near_rows(node_states, blocks_here, sub_rows)
    if heads_axis == 4:
        other = pair_stack(lax.ppermute(near, "node", far), heads_axis)
    else:
        other = spread_stack(lax.ppermute(mine, "node", far), heads_axis)
    every = jnp.stack(
        [
            pair_stack(
                lax.ppermute(near, "node", [(i, i ^ shift) for i in range(groups)]), heads_axis
            )
            if shift < NEAR_SHIFTS and heads_axis == 4
            else spread_stack(
                lax.ppermute(mine, "node", [(i, i ^ shift) for i in range(groups)]), heads_axis
            )
            for shift in range(1, groups)
        ]
    )
    odd = (my_index % 2) == 1
    before = jnp.where(odd, every[0], other)
    after = jnp.where(odd, other, every[0])
    matched = [
        lax.dynamic_index_in_dim(
            every, jnp.clip(targets[match_pos] - 1, 0, groups - 2), 0, keepdims=False
        )
        for match_pos in range(matches)
    ]
    w_parts, matched[0] = lax.optimization_barrier((w_parts, matched[0]))
    return kv_of_spread([before, after] + matched, w_kv, blocks_here, sub_rows), w_parts


def near_rows(node_states, blocks_here, sub_rows):
    model_width = node_states.shape[1]
    me = lax.axis_index("head")
    parts = node_states.reshape(blocks_here, 4, sub_rows, model_width)
    return jnp.stack(
        [
            lax.dynamic_index_in_dim(parts, me ^ flip, axis=1, keepdims=False).reshape(
                blocks_here * sub_rows, model_width
            )
            for flip in (0, 2)
        ]
    )


def pair_stack(received, heads_axis):
    beside = flip_heads(received, 1, heads_axis)
    return jnp.stack([received[0], beside[0], received[1], beside[1]])


def spread_stack(piece, heads_axis):
    slots = spread_slots(piece, heads_axis)
    return jnp.stack([slots[k] for k in range(heads_axis)])


def kv_of_spread(spread, w_kv, blocks_here, sub_rows):
    heads_axis, _, model_width = spread[0].shape
    rows = jnp.stack(
        [
            jnp.transpose(one.reshape(heads_axis, blocks_here, sub_rows, model_width), (1, 0, 2, 3))
            for one in spread
        ]
    )
    count = len(spread)
    total_rows = blocks_here * heads_axis * sub_rows
    rows = rows.reshape(count * total_rows, model_width)
    partner_kv = jnp.dot(rows, w_kv, preferred_element_type=jnp.float32).astype(jnp.bfloat16)
    return partner_kv.reshape(count, total_rows, w_kv.shape[1])


def attention_kernel(live_ref, pick_ref, q_ref, own_ref, part_ref, out_ref, score_ref):
    blocks_here = q_ref.shape[0]
    head_feats = q_ref.shape[2]
    pairs = head_feats // LANES
    per_pair = LANES // HEAD_DIM
    window = 2 * REACH + 1
    matches = part_ref.shape[0] - 2
    key_blocks = window + matches
    inv_root = 1.0 / math.sqrt(HEAD_DIM)
    lane = lax.broadcasted_iota(jnp.int32, (ROWS, LANES), 1)
    for j in range(blocks_here):

        def key_block(t, cols, j=j):
            if t < window:
                pos = j + t - REACH
                if pos < 0:
                    return part_ref[0, pos + blocks_here, :, cols]
                if pos < blocks_here:
                    return own_ref[pos, :, cols]
                return part_ref[1, pos - blocks_here, :, cols]
            match_pos = t - window
            return part_ref[2 + match_pos, pick_ref[match_pos, j], :, cols]

        for pair in range(pairs):
            kcols = pl.ds(pair * LANES, LANES)
            vcols = pl.ds(head_feats + pair * LANES, LANES)
            both = q_ref[j, :, kcols]
            merged = jnp.zeros((ROWS, LANES), jnp.float32)
            for half in range(per_pair):
                mine = (lane >= half * HEAD_DIM) & (lane < (half + 1) * HEAD_DIM)
                query = jnp.where(mine, both, jnp.zeros_like(both))
                highest = jnp.full((ROWS, ROWS), -jnp.inf, jnp.float32)
                for t in range(key_blocks):
                    scores = lax.dot_general(
                        query, key_block(t, kcols), (((1,), (1,)), ((), ())),
                        preferred_element_type=jnp.float32,
                    ) * inv_root
                    scores = jnp.where(live_ref[j, t] != 0, scores, -jnp.inf)
                    score_ref[t] = scores
                    highest = jnp.maximum(highest, scores)
                highest = jnp.max(highest, axis=1, keepdims=True)
                total = jnp.zeros((ROWS, ROWS), jnp.float32)
                for t in range(key_blocks):
                    weights = jnp.exp(score_ref[t] - highest)
                    score_ref[t] = weights
                    total = total + weights
                total = jnp.sum(total, axis=1, keepdims=True)
                context = jnp.zeros((ROWS, LANES), jnp.float32)
                for t in range(key_blocks):
                    probs = (score_ref[t] / total).astype(jnp.bfloat16)
                    context = context + jnp.dot(
                        probs, key_block(t, vcols), preferred_element_type=jnp.float32
                    )
                merged = jnp.where(mine, context, merged)
            out_ref[j, :, kcols] = merged.astype(jnp.bfloat16)


def attention(live, pick, query, own, part):
    blocks_here, rows, head_feats = query.shape
    key_blocks = live.shape[1]
    vmem = pltpu.VMEM
    flops = 8 * blocks_here * rows * key_blocks * rows * head_feats
    moved = 2 * (query.size * 2 + own.size + part.size)
    return pl.pallas_call(
        attention_kernel,
        out_shape=jax.ShapeDtypeStruct(query.shape, jnp.bfloat16),
        in_specs=[pl.BlockSpec(memory_space=pltpu.SMEM), pl.BlockSpec(memory_space=pltpu.SMEM),
                  pl.BlockSpec(memory_space=vmem), pl.BlockSpec(memory_space=vmem), pl.BlockSpec(memory_space=vmem)],
        out_specs=pl.BlockSpec(memory_space=vmem),
        scratch_shapes=[pltpu.VMEM((key_blocks, ROWS, ROWS), jnp.float32)],
        cost_estimate=pl.CostEstimate(
            flops=flops, transcendentals=blocks_here * rows * key_blocks * rows * 4, bytes_accessed=moved
        ),
    )(live, pick, query, own, part)

def local(node_states, w_qkv, w_out, ln_gain, ln_bias, local_mask, matchings):
    total_rows, model_width = node_states.shape
    blocks_here = total_rows // ROWS
    head_feats = w_qkv.shape[2]
    heads_here = head_feats // HEAD_DIM
    window = 2 * REACH + 1
    matches = matchings.shape[0]
    inv_root = 1.0 / math.sqrt(HEAD_DIM)
    my_index = lax.axis_index("node")
    groups = lax.axis_size("node")
    all_blocks = groups * blocks_here
    heads_axis = lax.axis_size("head")
    head_index = lax.axis_index("head")
    out_cols = ln_gain.shape[0]
    w_parts = [lax.dynamic_slice_in_dim(w_out, head_index * out_cols, out_cols, 1)] + [
        flip_heads(
            lax.dynamic_slice_in_dim(w_out, (head_index ^ flip) * out_cols, out_cols, 1),
            flip,
            heads_axis,
        )
        for flip in range(1, heads_axis)
    ]
    projected = jnp.einsum(
        "nd,dtf->ntf", node_states, w_qkv, preferred_element_type=jnp.float32
    ).astype(jnp.bfloat16)
    queries = projected[:, 0]
    keyvals = projected[:, 1:].reshape(total_rows, 2 * head_feats)
    global_blocks = my_index * blocks_here + jnp.arange(blocks_here, dtype=jnp.int32)
    offsets = jnp.arange(window, dtype=jnp.int32) - REACH
    neighbour = global_blocks[:, None] + offsets[None, :]
    if groups <= GATHER_GROUPS:
        w_kv = w_qkv[:, 1:].reshape(model_width, 2 * head_feats)
        part, w_parts = quarter_keys(
            node_states, w_kv, w_parts, matchings, my_index, groups, blocks_here
        )
    else:
        part = routed_keys(keyvals, matchings, my_index, groups, blocks_here)
    local_ok = (
        (neighbour >= 0) & (neighbour < all_blocks) & ((offsets[None, :] == 0) | (local_mask == 1))
    )
    block_ok = jnp.concatenate([local_ok, jnp.ones((blocks_here, matches), dtype=bool)], axis=1)
    context = attention(
        block_ok.astype(jnp.int32),
        (matchings % blocks_here).astype(jnp.int32),
        queries.reshape(blocks_here, ROWS, head_feats),
        keyvals.reshape(blocks_here, ROWS, 2 * head_feats),
        part.reshape(part.shape[0], blocks_here, ROWS, 2 * head_feats),
    ).reshape(total_rows, head_feats)
    context_slots = spread_slots(context, heads_axis)
    own_cols = lax.dynamic_slice_in_dim(node_states, head_index * out_cols, out_cols, 1)
    mixed_rows = own_cols.astype(jnp.float32) + jnp.einsum(
        "srf,sfo->ro",
        jnp.stack([context_slots[flip] for flip in range(heads_axis)]),
        jnp.stack(w_parts),
        preferred_element_type=jnp.float32,
    )
    part_mean = jnp.mean(mixed_rows, axis=1, keepdims=True)
    part_square = jnp.sum(jnp.square(mixed_rows - part_mean), axis=1, keepdims=True)
    stats = jnp.concatenate([part_mean, part_square], axis=1)
    all_stats = jnp.stack(
        [stats] + [flip_heads(stats, flip, heads_axis) for flip in range(1, heads_axis)]
    )
    centre = jnp.mean(all_stats[:, :, 0:1], axis=0)
    spread = (
        jnp.sum(all_stats[:, :, 1:2], axis=0)
        + out_cols * jnp.sum(jnp.square(all_stats[:, :, 0:1] - centre), axis=0)
    ) / (heads_axis * out_cols)
    normed = (mixed_rows - centre) * lax.rsqrt(spread + NORM_EPS)
    return (normed * ln_gain + ln_bias).astype(jnp.bfloat16)


def solution(mesh):
    placed = (
        P("node", None),
        P(None, None, "head"),
        P("head", None),
        P("head"),
        P("head"),
        P("node", None),
        P(None, "node"),
    )
    return jax.shard_map(
        local, mesh=mesh, in_specs=placed, out_specs=P("node", "head"), check_vma=False
    )
```

```python
import math

import jax
import jax.numpy as jnp
from jax import lax
from jax.experimental import pallas as pl
from jax.experimental.pallas import tpu as pltpu
from jax.sharding import PartitionSpec as P

HEAD_DIM = 64
ROWS = 128
REACH = 3
LANES = 128
GATHER_GROUPS = 16
STATIC_GROUPS = 8
NEAR_SHIFTS = 4


NORM_EPS = 1e-05


def partner(array, axis, bit):
    return lax.ppermute(array, axis, [(i, i ^ 1 << bit) for i in range(lax.axis_size(axis))])


def flip_heads(array, flip, devices):
    return lax.ppermute(array, "head", [(i, i ^ flip) for i in range(devices)])


def spread_slots(piece, heads_axis):
    if heads_axis == 4:
        across = flip_heads(piece, 2, heads_axis)
        return {
            0: piece,
            1: flip_heads(piece, 1, heads_axis),
            2: across,
            3: flip_heads(across, 1, heads_axis),
        }
    slots = {0: piece}
    for bit in reversed(range(heads_axis.bit_length() - 1)):
        flip = 1 << bit
        held = sorted(slots)
        other = flip_heads(jnp.stack([slots[k] for k in held]), flip, heads_axis)
        for pos, k in enumerate(held):
            slots[k ^ flip] = other[pos]
    return slots


def keep_same(current):
    return current


def route_direct(payload, shift_val, digits):
    for bit_pos in range(digits):

        def moved(current, bit_pos=bit_pos):
            return partner(current, "node", bit_pos)

        taken = jnp.bitwise_and(jnp.right_shift(shift_val, bit_pos), 1) == 1
        payload = lax.cond(taken, moved, keep_same, payload)
    return payload


def routed_keys(keyvals, matchings, my_index, groups, blocks_here):
    matches = matchings.shape[0]
    digits = groups.bit_length() - 1
    up = [(i, i + 1) for i in range(groups - 1)]
    down = [(i + 1, i) for i in range(groups - 1)]
    before = lax.ppermute(keyvals, "node", up)
    after = lax.ppermute(keyvals, "node", down)
    targets = jnp.bitwise_xor(matchings[:, 0] // blocks_here, my_index)
    received = [route_direct(keyvals, targets[match_pos], digits) for match_pos in range(matches)]
    return jnp.stack([before, after] + received)


def switched_send(payload, shift_val, groups):
    def branch(shift):
        def moved(current):
            return lax.ppermute(current, "node", [(i, i ^ shift) for i in range(groups)])

        return moved

    branches = [branch(shift) for shift in range(1, groups)]
    return lax.switch(jnp.clip(shift_val - 1, 0, groups - 2), branches, payload)


def quarter_keys(node_states, w_kv, w_parts, matchings, my_index, groups, blocks_here):
    total_rows, model_width = node_states.shape
    matches = matchings.shape[0]
    heads_axis = lax.axis_size("head")
    sub_rows = ROWS // heads_axis
    me = lax.axis_index("head")
    mine = node_states.reshape(blocks_here, heads_axis, sub_rows, model_width)
    mine = lax.dynamic_index_in_dim(mine, me, axis=1, keepdims=False)
    mine = mine.reshape(blocks_here * sub_rows, model_width)
    targets = jnp.bitwise_xor(matchings[:, 0] // blocks_here, my_index)
    if groups <= STATIC_GROUPS:
        return static_keys(
            node_states, mine, w_kv, w_parts, targets, my_index, groups, blocks_here, sub_rows
        )
    up = [(i, i + 1) for i in range(groups - 1)]
    down = [(i + 1, i) for i in range(groups - 1)]
    before = lax.ppermute(mine, "node", up)
    after = lax.ppermute(mine, "node", down)
    matched = [switched_send(mine, targets[match_pos], groups) for match_pos in range(matches)]
    w_parts, matched[0] = lax.optimization_barrier((w_parts, matched[0]))
    spread = [spread_stack(piece, heads_axis) for piece in [before, after] + matched]
    return kv_of_spread(spread, w_kv, blocks_here, sub_rows), w_parts


def static_keys(
    node_states, mine, w_kv, w_parts, targets, my_index, groups, blocks_here, sub_rows
):
    heads_axis = lax.axis_size("head")
    matches = targets.shape[0]
    far = [(j, j + 1) for j in range(1, groups - 1, 2)] + [(j, j - 1) for j in range(2, groups, 2)]
    other = spread_stack(lax.ppermute(mine, "node", far), heads_axis)
    near = near_rows(node_states, blocks_here, sub_rows)
    every = jnp.stack(
        [
            pair_stack(
                lax.ppermute(near, "node", [(i, i ^ shift) for i in range(groups)]), heads_axis
            )
            if shift < NEAR_SHIFTS and heads_axis == 4
            else spread_stack(
                lax.ppermute(mine, "node", [(i, i ^ shift) for i in range(groups)]), heads_axis
            )
            for shift in range(1, groups)
        ]
    )
    odd = (my_index % 2) == 1
    before = jnp.where(odd, every[0], other)
    after = jnp.where(odd, other, every[0])
    matched = [
        lax.dynamic_index_in_dim(
            every, jnp.clip(targets[match_pos] - 1, 0, groups - 2), 0, keepdims=False
        )
        for match_pos in range(matches)
    ]
    w_parts, matched[0] = lax.optimization_barrier((w_parts, matched[0]))
    return kv_of_spread([before, after] + matched, w_kv, blocks_here, sub_rows), w_parts


def near_rows(node_states, blocks_here, sub_rows):
    model_width = node_states.shape[1]
    me = lax.axis_index("head")
    parts = node_states.reshape(blocks_here, 4, sub_rows, model_width)
    return jnp.stack(
        [
            lax.dynamic_index_in_dim(parts, me ^ flip, axis=1, keepdims=False).reshape(
                blocks_here * sub_rows, model_width
            )
            for flip in (0, 2)
        ]
    )


def pair_stack(received, heads_axis):
    beside = flip_heads(received, 1, heads_axis)
    return jnp.stack([received[0], beside[0], received[1], beside[1]])


def spread_stack(piece, heads_axis):
    slots = spread_slots(piece, heads_axis)
    return jnp.stack([slots[k] for k in range(heads_axis)])


def kv_of_spread(spread, w_kv, blocks_here, sub_rows):
    heads_axis, _, model_width = spread[0].shape
    rows = jnp.stack(
        [
            jnp.transpose(one.reshape(heads_axis, blocks_here, sub_rows, model_width), (1, 0, 2, 3))
            for one in spread
        ]
    )
    count = len(spread)
    total_rows = blocks_here * heads_axis * sub_rows
    rows = rows.reshape(count * total_rows, model_width)
    partner_kv = jnp.dot(rows, w_kv, preferred_element_type=jnp.float32).astype(jnp.bfloat16)
    return partner_kv.reshape(count, total_rows, w_kv.shape[1])


def attention_kernel(live_ref, pick_ref, q_ref, own_ref, part_ref, out_ref, score_ref):
    blocks_here = q_ref.shape[0]
    head_feats = q_ref.shape[2]
    pairs = head_feats // LANES
    per_pair = LANES // HEAD_DIM
    window = 2 * REACH + 1
    matches = part_ref.shape[0] - 2
    key_blocks = window + matches
    inv_root = 1.0 / math.sqrt(HEAD_DIM)
    lane = lax.broadcasted_iota(jnp.int32, (ROWS, LANES), 1)
    for j in range(blocks_here):

        def key_block(t, cols, j=j):
            if t < window:
                pos = j + t - REACH
                if pos < 0:
                    return part_ref[0, pos + blocks_here, :, cols]
                if pos < blocks_here:
                    return own_ref[pos, :, cols]
                return part_ref[1, pos - blocks_here, :, cols]
            match_pos = t - window
            return part_ref[2 + match_pos, pick_ref[match_pos, j], :, cols]

        for pair in range(pairs):
            kcols = pl.ds(pair * LANES, LANES)
            vcols = pl.ds(head_feats + pair * LANES, LANES)
            both = q_ref[j, :, kcols]
            merged = jnp.zeros((ROWS, LANES), jnp.float32)
            for half in range(per_pair):
                mine = (lane >= half * HEAD_DIM) & (lane < (half + 1) * HEAD_DIM)
                query = jnp.where(mine, both, jnp.zeros_like(both))
                highest = jnp.full((ROWS, ROWS), -jnp.inf, jnp.float32)
                for t in range(key_blocks):
                    scores = lax.dot_general(
                        query, key_block(t, kcols), (((1,), (1,)), ((), ())),
                        preferred_element_type=jnp.float32,
                    ) * inv_root
                    scores = jnp.where(live_ref[j, t] != 0, scores, -jnp.inf)
                    score_ref[t] = scores
                    highest = jnp.maximum(highest, scores)
                highest = jnp.max(highest, axis=1, keepdims=True)
                total = jnp.zeros((ROWS, ROWS), jnp.float32)
                for t in range(key_blocks):
                    weights = jnp.exp(score_ref[t] - highest)
                    score_ref[t] = weights
                    total = total + weights
                total = jnp.sum(total, axis=1, keepdims=True)
                context = jnp.zeros((ROWS, LANES), jnp.float32)
                for t in range(key_blocks):
                    probs = (score_ref[t] / total).astype(jnp.bfloat16)
                    context = context + jnp.dot(
                        probs, key_block(t, vcols), preferred_element_type=jnp.float32
                    )
                merged = jnp.where(mine, context, merged)
            out_ref[j, :, kcols] = merged.astype(jnp.bfloat16)


def attention(live, pick, query, own, part):
    blocks_here, rows, head_feats = query.shape
    key_blocks = live.shape[1]
    vmem = pltpu.VMEM
    flops = 8 * blocks_here * rows * key_blocks * rows * head_feats
    moved = 2 * (query.size * 2 + own.size + part.size)
    return pl.pallas_call(
        attention_kernel,
        out_shape=jax.ShapeDtypeStruct(query.shape, jnp.bfloat16),
        in_specs=[pl.BlockSpec(memory_space=pltpu.SMEM), pl.BlockSpec(memory_space=pltpu.SMEM),
                  pl.BlockSpec(memory_space=vmem), pl.BlockSpec(memory_space=vmem), pl.BlockSpec(memory_space=vmem)],
        out_specs=pl.BlockSpec(memory_space=vmem),
        scratch_shapes=[pltpu.VMEM((key_blocks, ROWS, ROWS), jnp.float32)],
        cost_estimate=pl.CostEstimate(
            flops=flops, transcendentals=blocks_here * rows * key_blocks * rows * 4, bytes_accessed=moved
        ),
    )(live, pick, query, own, part)

def local(node_states, w_qkv, w_out, ln_gain, ln_bias, local_mask, matchings):
    total_rows, model_width = node_states.shape
    blocks_here = total_rows // ROWS
    head_feats = w_qkv.shape[2]
    heads_here = head_feats // HEAD_DIM
    window = 2 * REACH + 1
    matches = matchings.shape[0]
    inv_root = 1.0 / math.sqrt(HEAD_DIM)
    my_index = lax.axis_index("node")
    groups = lax.axis_size("node")
    all_blocks = groups * blocks_here
    heads_axis = lax.axis_size("head")
    head_index = lax.axis_index("head")
    out_cols = ln_gain.shape[0]
    w_parts = [lax.dynamic_slice_in_dim(w_out, head_index * out_cols, out_cols, 1)] + [
        flip_heads(
            lax.dynamic_slice_in_dim(w_out, (head_index ^ flip) * out_cols, out_cols, 1),
            flip,
            heads_axis,
        )
        for flip in range(1, heads_axis)
    ]
    projected = jnp.einsum(
        "nd,dtf->ntf", node_states, w_qkv, preferred_element_type=jnp.float32
    ).astype(jnp.bfloat16)
    queries = projected[:, 0]
    keyvals = projected[:, 1:].reshape(total_rows, 2 * head_feats)
    global_blocks = my_index * blocks_here + jnp.arange(blocks_here, dtype=jnp.int32)
    offsets = jnp.arange(window, dtype=jnp.int32) - REACH
    neighbour = global_blocks[:, None] + offsets[None, :]
    if groups <= GATHER_GROUPS:
        w_kv = w_qkv[:, 1:].reshape(model_width, 2 * head_feats)
        part, w_parts = quarter_keys(
            node_states, w_kv, w_parts, matchings, my_index, groups, blocks_here
        )
    else:
        part = routed_keys(keyvals, matchings, my_index, groups, blocks_here)
    local_ok = (
        (neighbour >= 0) & (neighbour < all_blocks) & ((offsets[None, :] == 0) | (local_mask == 1))
    )
    block_ok = jnp.concatenate([local_ok, jnp.ones((blocks_here, matches), dtype=bool)], axis=1)
    context = attention(
        block_ok.astype(jnp.int32),
        (matchings % blocks_here).astype(jnp.int32),
        queries.reshape(blocks_here, ROWS, head_feats),
        keyvals.reshape(blocks_here, ROWS, 2 * head_feats),
        part.reshape(part.shape[0], blocks_here, ROWS, 2 * head_feats),
    ).reshape(total_rows, head_feats)
    context_slots = spread_slots(context, heads_axis)
    own_cols = lax.dynamic_slice_in_dim(node_states, head_index * out_cols, out_cols, 1)
    mixed_rows = own_cols.astype(jnp.float32) + jnp.einsum(
        "srf,sfo->ro",
        jnp.stack([context_slots[flip] for flip in range(heads_axis)]),
        jnp.stack(w_parts),
        preferred_element_type=jnp.float32,
    )
    part_mean = jnp.mean(mixed_rows, axis=1, keepdims=True)
    part_square = jnp.sum(jnp.square(mixed_rows - part_mean), axis=1, keepdims=True)
    stats = jnp.concatenate([part_mean, part_square], axis=1)
    all_stats = jnp.stack(
        [stats] + [flip_heads(stats, flip, heads_axis) for flip in range(1, heads_axis)]
    )
    centre = jnp.mean(all_stats[:, :, 0:1], axis=0)
    spread = (
        jnp.sum(all_stats[:, :, 1:2], axis=0)
        + out_cols * jnp.sum(jnp.square(all_stats[:, :, 0:1] - centre), axis=0)
    ) / (heads_axis * out_cols)
    normed = (mixed_rows - centre) * lax.rsqrt(spread + NORM_EPS)
    return (normed * ln_gain + ln_bias).astype(jnp.bfloat16)


def solution(mesh):
    placed = (
        P("node", None),
        P(None, None, "head"),
        P("head", None),
        P("head"),
        P("head"),
        P("node", None),
        P(None, "node"),
    )
    return jax.shard_map(
        local, mesh=mesh, in_specs=placed, out_specs=P("node", "head"), check_vma=False
    )
```

```python
import math

import jax
import jax.numpy as jnp
from jax import lax
from jax.experimental import pallas as pl
from jax.experimental.pallas import tpu as pltpu
from jax.sharding import PartitionSpec as P

HEAD_DIM = 64
ROWS = 128
REACH = 3
LANES = 128
GATHER_GROUPS = 16
STATIC_GROUPS = 8
NEAR_SHIFTS = 2


NORM_EPS = 1e-05


def partner(array, axis, bit):
    return lax.ppermute(array, axis, [(i, i ^ 1 << bit) for i in range(lax.axis_size(axis))])


def flip_heads(array, flip, devices):
    return lax.ppermute(array, "head", [(i, i ^ flip) for i in range(devices)])


def spread_slots(piece, heads_axis):
    slots = {0: piece}
    for bit in reversed(range(heads_axis.bit_length() - 1)):
        flip = 1 << bit
        held = sorted(slots)
        other = flip_heads(jnp.stack([slots[k] for k in held]), flip, heads_axis)
        for pos, k in enumerate(held):
            slots[k ^ flip] = other[pos]
    return slots


def keep_same(current):
    return current


def route_direct(payload, shift_val, digits):
    for bit_pos in range(digits):

        def moved(current, bit_pos=bit_pos):
            return partner(current, "node", bit_pos)

        taken = jnp.bitwise_and(jnp.right_shift(shift_val, bit_pos), 1) == 1
        payload = lax.cond(taken, moved, keep_same, payload)
    return payload


def routed_keys(keyvals, matchings, my_index, groups, blocks_here):
    matches = matchings.shape[0]
    digits = groups.bit_length() - 1
    up = [(i, i + 1) for i in range(groups - 1)]
    down = [(i + 1, i) for i in range(groups - 1)]
    before = lax.ppermute(keyvals, "node", up)
    after = lax.ppermute(keyvals, "node", down)
    targets = jnp.bitwise_xor(matchings[:, 0] // blocks_here, my_index)
    received = [route_direct(keyvals, targets[match_pos], digits) for match_pos in range(matches)]
    return jnp.stack([before, after] + received)


def switched_send(payload, shift_val, groups):
    def branch(shift):
        def moved(current):
            return lax.ppermute(current, "node", [(i, i ^ shift) for i in range(groups)])

        return moved

    branches = [branch(shift) for shift in range(1, groups)]
    return lax.switch(jnp.clip(shift_val - 1, 0, groups - 2), branches, payload)


def quarter_keys(node_states, w_kv, w_parts, matchings, my_index, groups, blocks_here):
    total_rows, model_width = node_states.shape
    matches = matchings.shape[0]
    heads_axis = lax.axis_size("head")
    sub_rows = ROWS // heads_axis
    me = lax.axis_index("head")
    mine = node_states.reshape(blocks_here, heads_axis, sub_rows, model_width)
    mine = lax.dynamic_index_in_dim(mine, me, axis=1, keepdims=False)
    mine = mine.reshape(blocks_here * sub_rows, model_width)
    targets = jnp.bitwise_xor(matchings[:, 0] // blocks_here, my_index)
    if groups <= STATIC_GROUPS:
        return static_keys(
            node_states, mine, w_kv, w_parts, targets, my_index, groups, blocks_here, sub_rows
        )
    up = [(i, i + 1) for i in range(groups - 1)]
    down = [(i + 1, i) for i in range(groups - 1)]
    before = lax.ppermute(mine, "node", up)
    after = lax.ppermute(mine, "node", down)
    matched = [switched_send(mine, targets[match_pos], groups) for match_pos in range(matches)]
    w_parts, matched[0] = lax.optimization_barrier((w_parts, matched[0]))
    spread = [spread_stack(piece, heads_axis) for piece in [before, after] + matched]
    return kv_of_spread(spread, w_kv, blocks_here, sub_rows), w_parts


def static_keys(
    node_states, mine, w_kv, w_parts, targets, my_index, groups, blocks_here, sub_rows
):
    heads_axis = lax.axis_size("head")
    matches = targets.shape[0]
    far = [(j, j + 1) for j in range(1, groups - 1, 2)] + [(j, j - 1) for j in range(2, groups, 2)]
    other = spread_stack(lax.ppermute(mine, "node", far), heads_axis)
    near = near_rows(node_states, blocks_here, sub_rows)
    every = jnp.stack(
        [
            pair_stack(
                lax.ppermute(near, "node", [(i, i ^ shift) for i in range(groups)]), heads_axis
            )
            if shift < NEAR_SHIFTS and heads_axis == 4
            else spread_stack(
                lax.ppermute(mine, "node", [(i, i ^ shift) for i in range(groups)]), heads_axis
            )
            for shift in range(1, groups)
        ]
    )
    odd = (my_index % 2) == 1
    before = jnp.where(odd, every[0], other)
    after = jnp.where(odd, other, every[0])
    matched = [
        lax.dynamic_index_in_dim(
            every, jnp.clip(targets[match_pos] - 1, 0, groups - 2), 0, keepdims=False
        )
        for match_pos in range(matches)
    ]
    w_parts, matched[0] = lax.optimization_barrier((w_parts, matched[0]))
    return kv_of_spread([before, after] + matched, w_kv, blocks_here, sub_rows), w_parts


def near_rows(node_states, blocks_here, sub_rows):
    model_width = node_states.shape[1]
    me = lax.axis_index("head")
    parts = node_states.reshape(blocks_here, 4, sub_rows, model_width)
    return jnp.stack(
        [
            lax.dynamic_index_in_dim(parts, me ^ flip, axis=1, keepdims=False).reshape(
                blocks_here * sub_rows, model_width
            )
            for flip in (0, 2)
        ]
    )


def pair_stack(received, heads_axis):
    beside = flip_heads(received, 1, heads_axis)
    return jnp.stack([received[0], beside[0], received[1], beside[1]])


def spread_stack(piece, heads_axis):
    slots = spread_slots(piece, heads_axis)
    return jnp.stack([slots[k] for k in range(heads_axis)])


def kv_of_spread(spread, w_kv, blocks_here, sub_rows):
    heads_axis, _, model_width = spread[0].shape
    rows = jnp.stack(
        [
            jnp.transpose(one.reshape(heads_axis, blocks_here, sub_rows, model_width), (1, 0, 2, 3))
            for one in spread
        ]
    )
    count = len(spread)
    total_rows = blocks_here * heads_axis * sub_rows
    rows = rows.reshape(count * total_rows, model_width)
    partner_kv = jnp.dot(rows, w_kv, preferred_element_type=jnp.float32).astype(jnp.bfloat16)
    return partner_kv.reshape(count, total_rows, w_kv.shape[1])


def attention_kernel(live_ref, pick_ref, q_ref, own_ref, part_ref, out_ref, score_ref):
    blocks_here = q_ref.shape[0]
    head_feats = q_ref.shape[2]
    pairs = head_feats // LANES
    per_pair = LANES // HEAD_DIM
    window = 2 * REACH + 1
    matches = part_ref.shape[0] - 2
    key_blocks = window + matches
    inv_root = 1.0 / math.sqrt(HEAD_DIM)
    lane = lax.broadcasted_iota(jnp.int32, (ROWS, LANES), 1)
    for j in range(blocks_here):

        def key_block(t, cols, j=j):
            if t < window:
                pos = j + t - REACH
                if pos < 0:
                    return part_ref[0, pos + blocks_here, :, cols]
                if pos < blocks_here:
                    return own_ref[pos, :, cols]
                return part_ref[1, pos - blocks_here, :, cols]
            match_pos = t - window
            return part_ref[2 + match_pos, pick_ref[match_pos, j], :, cols]

        for pair in range(pairs):
            kcols = pl.ds(pair * LANES, LANES)
            vcols = pl.ds(head_feats + pair * LANES, LANES)
            both = q_ref[j, :, kcols]
            merged = jnp.zeros((ROWS, LANES), jnp.float32)
            for half in range(per_pair):
                mine = (lane >= half * HEAD_DIM) & (lane < (half + 1) * HEAD_DIM)
                query = jnp.where(mine, both, jnp.zeros_like(both))
                highest = jnp.full((ROWS, ROWS), -jnp.inf, jnp.float32)
                for t in range(key_blocks):
                    scores = lax.dot_general(
                        query, key_block(t, kcols), (((1,), (1,)), ((), ())),
                        preferred_element_type=jnp.float32,
                    ) * inv_root
                    scores = jnp.where(live_ref[j, t] != 0, scores, -jnp.inf)
                    score_ref[t] = scores
                    highest = jnp.maximum(highest, scores)
                highest = jnp.max(highest, axis=1, keepdims=True)
                total = jnp.zeros((ROWS, ROWS), jnp.float32)
                for t in range(key_blocks):
                    weights = jnp.exp(score_ref[t] - highest)
                    score_ref[t] = weights
                    total = total + weights
                total = jnp.sum(total, axis=1, keepdims=True)
                context = jnp.zeros((ROWS, LANES), jnp.float32)
                for t in range(key_blocks):
                    probs = (score_ref[t] / total).astype(jnp.bfloat16)
                    context = context + jnp.dot(
                        probs, key_block(t, vcols), preferred_element_type=jnp.float32
                    )
                merged = jnp.where(mine, context, merged)
            out_ref[j, :, kcols] = merged.astype(jnp.bfloat16)


def attention(live, pick, query, own, part):
    blocks_here, rows, head_feats = query.shape
    key_blocks = live.shape[1]
    vmem = pltpu.VMEM
    flops = 8 * blocks_here * rows * key_blocks * rows * head_feats
    moved = 2 * (query.size * 2 + own.size + part.size)
    return pl.pallas_call(
        attention_kernel,
        out_shape=jax.ShapeDtypeStruct(query.shape, jnp.bfloat16),
        in_specs=[pl.BlockSpec(memory_space=pltpu.SMEM), pl.BlockSpec(memory_space=pltpu.SMEM),
                  pl.BlockSpec(memory_space=vmem), pl.BlockSpec(memory_space=vmem), pl.BlockSpec(memory_space=vmem)],
        out_specs=pl.BlockSpec(memory_space=vmem),
        scratch_shapes=[pltpu.VMEM((key_blocks, ROWS, ROWS), jnp.float32)],
        cost_estimate=pl.CostEstimate(
            flops=flops, transcendentals=blocks_here * rows * key_blocks * rows * 4, bytes_accessed=moved
        ),
    )(live, pick, query, own, part)

def local(node_states, w_qkv, w_out, ln_gain, ln_bias, local_mask, matchings):
    total_rows, model_width = node_states.shape
    blocks_here = total_rows // ROWS
    head_feats = w_qkv.shape[2]
    heads_here = head_feats // HEAD_DIM
    window = 2 * REACH + 1
    matches = matchings.shape[0]
    inv_root = 1.0 / math.sqrt(HEAD_DIM)
    my_index = lax.axis_index("node")
    groups = lax.axis_size("node")
    all_blocks = groups * blocks_here
    heads_axis = lax.axis_size("head")
    head_index = lax.axis_index("head")
    out_cols = ln_gain.shape[0]
    w_parts = [lax.dynamic_slice_in_dim(w_out, head_index * out_cols, out_cols, 1)] + [
        flip_heads(
            lax.dynamic_slice_in_dim(w_out, (head_index ^ flip) * out_cols, out_cols, 1),
            flip,
            heads_axis,
        )
        for flip in range(1, heads_axis)
    ]
    projected = jnp.einsum(
        "nd,dtf->ntf", node_states, w_qkv, preferred_element_type=jnp.float32
    ).astype(jnp.bfloat16)
    queries = projected[:, 0]
    keyvals = projected[:, 1:].reshape(total_rows, 2 * head_feats)
    global_blocks = my_index * blocks_here + jnp.arange(blocks_here, dtype=jnp.int32)
    offsets = jnp.arange(window, dtype=jnp.int32) - REACH
    neighbour = global_blocks[:, None] + offsets[None, :]
    if groups <= GATHER_GROUPS:
        w_kv = w_qkv[:, 1:].reshape(model_width, 2 * head_feats)
        part, w_parts = quarter_keys(
            node_states, w_kv, w_parts, matchings, my_index, groups, blocks_here
        )
    else:
        part = routed_keys(keyvals, matchings, my_index, groups, blocks_here)
    local_ok = (
        (neighbour >= 0) & (neighbour < all_blocks) & ((offsets[None, :] == 0) | (local_mask == 1))
    )
    block_ok = jnp.concatenate([local_ok, jnp.ones((blocks_here, matches), dtype=bool)], axis=1)
    context = attention(
        block_ok.astype(jnp.int32),
        (matchings % blocks_here).astype(jnp.int32),
        queries.reshape(blocks_here, ROWS, head_feats),
        keyvals.reshape(blocks_here, ROWS, 2 * head_feats),
        part.reshape(part.shape[0], blocks_here, ROWS, 2 * head_feats),
    ).reshape(total_rows, head_feats)
    context_slots = spread_slots(context, heads_axis)
    own_cols = lax.dynamic_slice_in_dim(node_states, head_index * out_cols, out_cols, 1)
    mixed_rows = own_cols.astype(jnp.float32) + jnp.einsum(
        "srf,sfo->ro",
        jnp.stack([context_slots[flip] for flip in range(heads_axis)]),
        jnp.stack(w_parts),
        preferred_element_type=jnp.float32,
    )
    part_mean = jnp.mean(mixed_rows, axis=1, keepdims=True)
    part_square = jnp.sum(jnp.square(mixed_rows - part_mean), axis=1, keepdims=True)
    stats = jnp.concatenate([part_mean, part_square], axis=1)
    all_stats = jnp.stack(
        [stats] + [flip_heads(stats, flip, heads_axis) for flip in range(1, heads_axis)]
    )
    centre = jnp.mean(all_stats[:, :, 0:1], axis=0)
    spread = (
        jnp.sum(all_stats[:, :, 1:2], axis=0)
        + out_cols * jnp.sum(jnp.square(all_stats[:, :, 0:1] - centre), axis=0)
    ) / (heads_axis * out_cols)
    normed = (mixed_rows - centre) * lax.rsqrt(spread + NORM_EPS)
    return (normed * ln_gain + ln_bias).astype(jnp.bfloat16)


def solution(mesh):
    placed = (
        P("node", None),
        P(None, None, "head"),
        P("head", None),
        P("head"),
        P("head"),
        P("node", None),
        P(None, "node"),
    )
    return jax.shard_map(
        local, mesh=mesh, in_specs=placed, out_specs=P("node", "head"), check_vma=False
    )
```

```python
import math

import jax
import jax.numpy as jnp
from jax import lax
from jax.experimental import pallas as pl
from jax.experimental.pallas import tpu as pltpu
from jax.sharding import PartitionSpec as P

HEAD_DIM = 64
ROWS = 128
REACH = 3
LANES = 128
GATHER_GROUPS = 16
STATIC_GROUPS = 8
NEAR_SHIFTS = 3


NORM_EPS = 1e-05


def partner(array, axis, bit):
    return lax.ppermute(array, axis, [(i, i ^ 1 << bit) for i in range(lax.axis_size(axis))])


def flip_heads(array, flip, devices):
    return lax.ppermute(array, "head", [(i, i ^ flip) for i in range(devices)])


def spread_slots(piece, heads_axis):
    slots = {0: piece}
    for bit in reversed(range(heads_axis.bit_length() - 1)):
        flip = 1 << bit
        held = sorted(slots)
        other = flip_heads(jnp.stack([slots[k] for k in held]), flip, heads_axis)
        for pos, k in enumerate(held):
            slots[k ^ flip] = other[pos]
    return slots


def keep_same(current):
    return current


def route_direct(payload, shift_val, digits):
    for bit_pos in range(digits):

        def moved(current, bit_pos=bit_pos):
            return partner(current, "node", bit_pos)

        taken = jnp.bitwise_and(jnp.right_shift(shift_val, bit_pos), 1) == 1
        payload = lax.cond(taken, moved, keep_same, payload)
    return payload


def routed_keys(keyvals, matchings, my_index, groups, blocks_here):
    matches = matchings.shape[0]
    digits = groups.bit_length() - 1
    up = [(i, i + 1) for i in range(groups - 1)]
    down = [(i + 1, i) for i in range(groups - 1)]
    before = lax.ppermute(keyvals, "node", up)
    after = lax.ppermute(keyvals, "node", down)
    targets = jnp.bitwise_xor(matchings[:, 0] // blocks_here, my_index)
    received = [route_direct(keyvals, targets[match_pos], digits) for match_pos in range(matches)]
    return jnp.stack([before, after] + received)


def switched_send(payload, shift_val, groups):
    def branch(shift):
        def moved(current):
            return lax.ppermute(current, "node", [(i, i ^ shift) for i in range(groups)])

        return moved

    branches = [branch(shift) for shift in range(1, groups)]
    return lax.switch(jnp.clip(shift_val - 1, 0, groups - 2), branches, payload)


def quarter_keys(node_states, w_kv, w_parts, matchings, my_index, groups, blocks_here):
    total_rows, model_width = node_states.shape
    matches = matchings.shape[0]
    heads_axis = lax.axis_size("head")
    sub_rows = ROWS // heads_axis
    me = lax.axis_index("head")
    mine = node_states.reshape(blocks_here, heads_axis, sub_rows, model_width)
    mine = lax.dynamic_index_in_dim(mine, me, axis=1, keepdims=False)
    mine = mine.reshape(blocks_here * sub_rows, model_width)
    targets = jnp.bitwise_xor(matchings[:, 0] // blocks_here, my_index)
    if groups <= STATIC_GROUPS:
        return static_keys(
            node_states, mine, w_kv, w_parts, targets, my_index, groups, blocks_here, sub_rows
        )
    up = [(i, i + 1) for i in range(groups - 1)]
    down = [(i + 1, i) for i in range(groups - 1)]
    before = lax.ppermute(mine, "node", up)
    after = lax.ppermute(mine, "node", down)
    matched = [switched_send(mine, targets[match_pos], groups) for match_pos in range(matches)]
    w_parts, matched[0] = lax.optimization_barrier((w_parts, matched[0]))
    spread = [spread_stack(piece, heads_axis) for piece in [before, after] + matched]
    return kv_of_spread(spread, w_kv, blocks_here, sub_rows), w_parts


def static_keys(
    node_states, mine, w_kv, w_parts, targets, my_index, groups, blocks_here, sub_rows
):
    heads_axis = lax.axis_size("head")
    matches = targets.shape[0]
    far = [(j, j + 1) for j in range(1, groups - 1, 2)] + [(j, j - 1) for j in range(2, groups, 2)]
    other = spread_stack(lax.ppermute(mine, "node", far), heads_axis)
    near = near_rows(node_states, blocks_here, sub_rows)
    every = jnp.stack(
        [
            pair_stack(
                lax.ppermute(near, "node", [(i, i ^ shift) for i in range(groups)]), heads_axis
            )
            if shift < NEAR_SHIFTS and heads_axis == 4
            else spread_stack(
                lax.ppermute(mine, "node", [(i, i ^ shift) for i in range(groups)]), heads_axis
            )
            for shift in range(1, groups)
        ]
    )
    odd = (my_index % 2) == 1
    before = jnp.where(odd, every[0], other)
    after = jnp.where(odd, other, every[0])
    matched = [
        lax.dynamic_index_in_dim(
            every, jnp.clip(targets[match_pos] - 1, 0, groups - 2), 0, keepdims=False
        )
        for match_pos in range(matches)
    ]
    w_parts, matched[0] = lax.optimization_barrier((w_parts, matched[0]))
    return kv_of_spread([before, after] + matched, w_kv, blocks_here, sub_rows), w_parts


def near_rows(node_states, blocks_here, sub_rows):
    model_width = node_states.shape[1]
    me = lax.axis_index("head")
    parts = node_states.reshape(blocks_here, 4, sub_rows, model_width)
    return jnp.stack(
        [
            lax.dynamic_index_in_dim(parts, me ^ flip, axis=1, keepdims=False).reshape(
                blocks_here * sub_rows, model_width
            )
            for flip in (0, 2)
        ]
    )


def pair_stack(received, heads_axis):
    beside = flip_heads(received, 1, heads_axis)
    return jnp.stack([received[0], beside[0], received[1], beside[1]])


def spread_stack(piece, heads_axis):
    slots = spread_slots(piece, heads_axis)
    return jnp.stack([slots[k] for k in range(heads_axis)])


def kv_of_spread(spread, w_kv, blocks_here, sub_rows):
    heads_axis, _, model_width = spread[0].shape
    rows = jnp.stack(
        [
            jnp.transpose(one.reshape(heads_axis, blocks_here, sub_rows, model_width), (1, 0, 2, 3))
            for one in spread
        ]
    )
    count = len(spread)
    total_rows = blocks_here * heads_axis * sub_rows
    rows = rows.reshape(count * total_rows, model_width)
    partner_kv = jnp.dot(rows, w_kv, preferred_element_type=jnp.float32).astype(jnp.bfloat16)
    return partner_kv.reshape(count, total_rows, w_kv.shape[1])


def attention_kernel(live_ref, pick_ref, q_ref, own_ref, part_ref, out_ref, score_ref):
    blocks_here = q_ref.shape[0]
    head_feats = q_ref.shape[2]
    pairs = head_feats // LANES
    per_pair = LANES // HEAD_DIM
    window = 2 * REACH + 1
    matches = part_ref.shape[0] - 2
    key_blocks = window + matches
    inv_root = 1.0 / math.sqrt(HEAD_DIM)
    lane = lax.broadcasted_iota(jnp.int32, (ROWS, LANES), 1)
    for j in range(blocks_here):

        def key_block(t, cols, j=j):
            if t < window:
                pos = j + t - REACH
                if pos < 0:
                    return part_ref[0, pos + blocks_here, :, cols]
                if pos < blocks_here:
                    return own_ref[pos, :, cols]
                return part_ref[1, pos - blocks_here, :, cols]
            match_pos = t - window
            return part_ref[2 + match_pos, pick_ref[match_pos, j], :, cols]

        for pair in range(pairs):
            kcols = pl.ds(pair * LANES, LANES)
            vcols = pl.ds(head_feats + pair * LANES, LANES)
            both = q_ref[j, :, kcols]
            merged = jnp.zeros((ROWS, LANES), jnp.float32)
            for half in range(per_pair):
                mine = (lane >= half * HEAD_DIM) & (lane < (half + 1) * HEAD_DIM)
                query = jnp.where(mine, both, jnp.zeros_like(both))
                highest = jnp.full((ROWS, ROWS), -jnp.inf, jnp.float32)
                for t in range(key_blocks):
                    scores = lax.dot_general(
                        query, key_block(t, kcols), (((1,), (1,)), ((), ())),
                        preferred_element_type=jnp.float32,
                    ) * inv_root
                    scores = jnp.where(live_ref[j, t] != 0, scores, -jnp.inf)
                    score_ref[t] = scores
                    highest = jnp.maximum(highest, scores)
                highest = jnp.max(highest, axis=1, keepdims=True)
                total = jnp.zeros((ROWS, ROWS), jnp.float32)
                for t in range(key_blocks):
                    weights = jnp.exp(score_ref[t] - highest)
                    score_ref[t] = weights
                    total = total + weights
                total = jnp.sum(total, axis=1, keepdims=True)
                context = jnp.zeros((ROWS, LANES), jnp.float32)
                for t in range(key_blocks):
                    probs = (score_ref[t] / total).astype(jnp.bfloat16)
                    context = context + jnp.dot(
                        probs, key_block(t, vcols), preferred_element_type=jnp.float32
                    )
                merged = jnp.where(mine, context, merged)
            out_ref[j, :, kcols] = merged.astype(jnp.bfloat16)


def attention(live, pick, query, own, part):
    blocks_here, rows, head_feats = query.shape
    key_blocks = live.shape[1]
    vmem = pltpu.VMEM
    flops = 8 * blocks_here * rows * key_blocks * rows * head_feats
    moved = 2 * (query.size * 2 + own.size + part.size)
    return pl.pallas_call(
        attention_kernel,
        out_shape=jax.ShapeDtypeStruct(query.shape, jnp.bfloat16),
        in_specs=[pl.BlockSpec(memory_space=pltpu.SMEM), pl.BlockSpec(memory_space=pltpu.SMEM),
                  pl.BlockSpec(memory_space=vmem), pl.BlockSpec(memory_space=vmem), pl.BlockSpec(memory_space=vmem)],
        out_specs=pl.BlockSpec(memory_space=vmem),
        scratch_shapes=[pltpu.VMEM((key_blocks, ROWS, ROWS), jnp.float32)],
        cost_estimate=pl.CostEstimate(
            flops=flops, transcendentals=blocks_here * rows * key_blocks * rows * 4, bytes_accessed=moved
        ),
    )(live, pick, query, own, part)

def local(node_states, w_qkv, w_out, ln_gain, ln_bias, local_mask, matchings):
    total_rows, model_width = node_states.shape
    blocks_here = total_rows // ROWS
    head_feats = w_qkv.shape[2]
    heads_here = head_feats // HEAD_DIM
    window = 2 * REACH + 1
    matches = matchings.shape[0]
    inv_root = 1.0 / math.sqrt(HEAD_DIM)
    my_index = lax.axis_index("node")
    groups = lax.axis_size("node")
    all_blocks = groups * blocks_here
    heads_axis = lax.axis_size("head")
    head_index = lax.axis_index("head")
    out_cols = ln_gain.shape[0]
    w_parts = [lax.dynamic_slice_in_dim(w_out, head_index * out_cols, out_cols, 1)] + [
        flip_heads(
            lax.dynamic_slice_in_dim(w_out, (head_index ^ flip) * out_cols, out_cols, 1),
            flip,
            heads_axis,
        )
        for flip in range(1, heads_axis)
    ]
    projected = jnp.einsum(
        "nd,dtf->ntf", node_states, w_qkv, preferred_element_type=jnp.float32
    ).astype(jnp.bfloat16)
    queries = projected[:, 0]
    keyvals = projected[:, 1:].reshape(total_rows, 2 * head_feats)
    global_blocks = my_index * blocks_here + jnp.arange(blocks_here, dtype=jnp.int32)
    offsets = jnp.arange(window, dtype=jnp.int32) - REACH
    neighbour = global_blocks[:, None] + offsets[None, :]
    if groups <= GATHER_GROUPS:
        w_kv = w_qkv[:, 1:].reshape(model_width, 2 * head_feats)
        part, w_parts = quarter_keys(
            node_states, w_kv, w_parts, matchings, my_index, groups, blocks_here
        )
    else:
        part = routed_keys(keyvals, matchings, my_index, groups, blocks_here)
    local_ok = (
        (neighbour >= 0) & (neighbour < all_blocks) & ((offsets[None, :] == 0) | (local_mask == 1))
    )
    block_ok = jnp.concatenate([local_ok, jnp.ones((blocks_here, matches), dtype=bool)], axis=1)
    context = attention(
        block_ok.astype(jnp.int32),
        (matchings % blocks_here).astype(jnp.int32),
        queries.reshape(blocks_here, ROWS, head_feats),
        keyvals.reshape(blocks_here, ROWS, 2 * head_feats),
        part.reshape(part.shape[0], blocks_here, ROWS, 2 * head_feats),
    ).reshape(total_rows, head_feats)
    context_slots = spread_slots(context, heads_axis)
    own_cols = lax.dynamic_slice_in_dim(node_states, head_index * out_cols, out_cols, 1)
    mixed_rows = own_cols.astype(jnp.float32) + jnp.einsum(
        "srf,sfo->ro",
        jnp.stack([context_slots[flip] for flip in range(heads_axis)]),
        jnp.stack(w_parts),
        preferred_element_type=jnp.float32,
    )
    part_mean = jnp.mean(mixed_rows, axis=1, keepdims=True)
    part_square = jnp.sum(jnp.square(mixed_rows - part_mean), axis=1, keepdims=True)
    stats = jnp.concatenate([part_mean, part_square], axis=1)
    all_stats = jnp.stack(
        [stats] + [flip_heads(stats, flip, heads_axis) for flip in range(1, heads_axis)]
    )
    centre = jnp.mean(all_stats[:, :, 0:1], axis=0)
    spread = (
        jnp.sum(all_stats[:, :, 1:2], axis=0)
        + out_cols * jnp.sum(jnp.square(all_stats[:, :, 0:1] - centre), axis=0)
    ) / (heads_axis * out_cols)
    normed = (mixed_rows - centre) * lax.rsqrt(spread + NORM_EPS)
    return (normed * ln_gain + ln_bias).astype(jnp.bfloat16)


def solution(mesh):
    placed = (
        P("node", None),
        P(None, None, "head"),
        P("head", None),
        P("head"),
        P("head"),
        P("node", None),
        P(None, "node"),
    )
    return jax.shard_map(
        local, mesh=mesh, in_specs=placed, out_specs=P("node", "head"), check_vma=False
    )
```

```python
import math

import jax
import jax.numpy as jnp
from jax import lax
from jax.experimental import pallas as pl
from jax.experimental.pallas import tpu as pltpu
from jax.sharding import PartitionSpec as P

HEAD_DIM = 64
ROWS = 128
REACH = 3
LANES = 128
GATHER_GROUPS = 16
STATIC_GROUPS = 8
NEAR_SHIFTS = 2


NORM_EPS = 1e-05


def partner(array, axis, bit):
    return lax.ppermute(array, axis, [(i, i ^ 1 << bit) for i in range(lax.axis_size(axis))])


def flip_heads(array, flip, devices):
    return lax.ppermute(array, "head", [(i, i ^ flip) for i in range(devices)])


def spread_slots(piece, heads_axis):
    slots = {0: piece}
    for bit in reversed(range(heads_axis.bit_length() - 1)):
        flip = 1 << bit
        held = sorted(slots)
        other = flip_heads(jnp.stack([slots[k] for k in held]), flip, heads_axis)
        for pos, k in enumerate(held):
            slots[k ^ flip] = other[pos]
    return slots


def keep_same(current):
    return current


def route_direct(payload, shift_val, digits):
    for bit_pos in range(digits):

        def moved(current, bit_pos=bit_pos):
            return partner(current, "node", bit_pos)

        taken = jnp.bitwise_and(jnp.right_shift(shift_val, bit_pos), 1) == 1
        payload = lax.cond(taken, moved, keep_same, payload)
    return payload


def routed_keys(keyvals, matchings, my_index, groups, blocks_here):
    matches = matchings.shape[0]
    digits = groups.bit_length() - 1
    up = [(i, i + 1) for i in range(groups - 1)]
    down = [(i + 1, i) for i in range(groups - 1)]
    before = lax.ppermute(keyvals, "node", up)
    after = lax.ppermute(keyvals, "node", down)
    targets = jnp.bitwise_xor(matchings[:, 0] // blocks_here, my_index)
    received = [route_direct(keyvals, targets[match_pos], digits) for match_pos in range(matches)]
    return jnp.stack([before, after] + received)


def switched_send(payload, shift_val, groups):
    def branch(shift):
        def moved(current):
            return lax.ppermute(current, "node", [(i, i ^ shift) for i in range(groups)])

        return moved

    branches = [branch(shift) for shift in range(1, groups)]
    return lax.switch(jnp.clip(shift_val - 1, 0, groups - 2), branches, payload)


def quarter_keys(node_states, w_kv, w_parts, matchings, my_index, groups, blocks_here):
    total_rows, model_width = node_states.shape
    matches = matchings.shape[0]
    heads_axis = lax.axis_size("head")
    sub_rows = ROWS // heads_axis
    me = lax.axis_index("head")
    mine = node_states.reshape(blocks_here, heads_axis, sub_rows, model_width)
    mine = lax.dynamic_index_in_dim(mine, me, axis=1, keepdims=False)
    mine = mine.reshape(blocks_here * sub_rows, model_width)
    targets = jnp.bitwise_xor(matchings[:, 0] // blocks_here, my_index)
    if groups <= STATIC_GROUPS:
        return static_keys(
            node_states, mine, w_kv, w_parts, targets, my_index, groups, blocks_here, sub_rows
        )
    up = [(i, i + 1) for i in range(groups - 1)]
    down = [(i + 1, i) for i in range(groups - 1)]
    before = lax.ppermute(mine, "node", up)
    after = lax.ppermute(mine, "node", down)
    matched = [switched_send(mine, targets[match_pos], groups) for match_pos in range(matches)]
    w_parts, matched[0] = lax.optimization_barrier((w_parts, matched[0]))
    spread = [spread_stack(piece, heads_axis) for piece in [before, after] + matched]
    return kv_of_spread(spread, w_kv, blocks_here, sub_rows), w_parts


def static_keys(
    node_states, mine, w_kv, w_parts, targets, my_index, groups, blocks_here, sub_rows
):
    heads_axis = lax.axis_size("head")
    matches = targets.shape[0]
    far = [(j, j + 1) for j in range(1, groups - 1, 2)] + [(j, j - 1) for j in range(2, groups, 2)]
    near = near_rows(node_states, blocks_here, sub_rows)
    if heads_axis == 4:
        other = pair_stack(lax.ppermute(near, "node", far), heads_axis)
    else:
        other = spread_stack(lax.ppermute(mine, "node", far), heads_axis)
    every = jnp.stack(
        [
            pair_stack(
                lax.ppermute(near, "node", [(i, i ^ shift) for i in range(groups)]), heads_axis
            )
            if shift < NEAR_SHIFTS and heads_axis == 4
            else spread_stack(
                lax.ppermute(mine, "node", [(i, i ^ shift) for i in range(groups)]), heads_axis
            )
            for shift in range(1, groups)
        ]
    )
    odd = (my_index % 2) == 1
    before = jnp.where(odd, every[0], other)
    after = jnp.where(odd, other, every[0])
    matched = [
        lax.dynamic_index_in_dim(
            every, jnp.clip(targets[match_pos] - 1, 0, groups - 2), 0, keepdims=False
        )
        for match_pos in range(matches)
    ]
    w_parts, matched[0] = lax.optimization_barrier((w_parts, matched[0]))
    return kv_of_spread([before, after] + matched, w_kv, blocks_here, sub_rows), w_parts


def near_rows(node_states, blocks_here, sub_rows):
    model_width = node_states.shape[1]
    me = lax.axis_index("head")
    parts = node_states.reshape(blocks_here, 4, sub_rows, model_width)
    return jnp.stack(
        [
            lax.dynamic_index_in_dim(parts, me ^ flip, axis=1, keepdims=False).reshape(
                blocks_here * sub_rows, model_width
            )
            for flip in (0, 2)
        ]
    )


def pair_stack(received, heads_axis):
    beside = flip_heads(received, 1, heads_axis)
    return jnp.stack([received[0], beside[0], received[1], beside[1]])


def spread_stack(piece, heads_axis):
    slots = spread_slots(piece, heads_axis)
    return jnp.stack([slots[k] for k in range(heads_axis)])


def kv_of_spread(spread, w_kv, blocks_here, sub_rows):
    heads_axis, _, model_width = spread[0].shape
    rows = jnp.stack(
        [
            jnp.transpose(one.reshape(heads_axis, blocks_here, sub_rows, model_width), (1, 0, 2, 3))
            for one in spread
        ]
    )
    count = len(spread)
    total_rows = blocks_here * heads_axis * sub_rows
    rows = rows.reshape(count * total_rows, model_width)
    partner_kv = jnp.dot(rows, w_kv, preferred_element_type=jnp.float32).astype(jnp.bfloat16)
    return partner_kv.reshape(count, total_rows, w_kv.shape[1])


def attention_kernel(live_ref, pick_ref, q_ref, own_ref, part_ref, out_ref, score_ref):
    blocks_here = q_ref.shape[0]
    head_feats = q_ref.shape[2]
    pairs = head_feats // LANES
    per_pair = LANES // HEAD_DIM
    window = 2 * REACH + 1
    matches = part_ref.shape[0] - 2
    key_blocks = window + matches
    inv_root = 1.0 / math.sqrt(HEAD_DIM)
    lane = lax.broadcasted_iota(jnp.int32, (ROWS, LANES), 1)
    for j in range(blocks_here):

        def key_block(t, cols, j=j):
            if t < window:
                pos = j + t - REACH
                if pos < 0:
                    return part_ref[0, pos + blocks_here, :, cols]
                if pos < blocks_here:
                    return own_ref[pos, :, cols]
                return part_ref[1, pos - blocks_here, :, cols]
            match_pos = t - window
            return part_ref[2 + match_pos, pick_ref[match_pos, j], :, cols]

        for pair in range(pairs):
            kcols = pl.ds(pair * LANES, LANES)
            vcols = pl.ds(head_feats + pair * LANES, LANES)
            both = q_ref[j, :, kcols]
            merged = jnp.zeros((ROWS, LANES), jnp.float32)
            for half in range(per_pair):
                mine = (lane >= half * HEAD_DIM) & (lane < (half + 1) * HEAD_DIM)
                query = jnp.where(mine, both, jnp.zeros_like(both))
                highest = jnp.full((ROWS, ROWS), -jnp.inf, jnp.float32)
                for t in range(key_blocks):
                    scores = lax.dot_general(
                        query, key_block(t, kcols), (((1,), (1,)), ((), ())),
                        preferred_element_type=jnp.float32,
                    ) * inv_root
                    scores = jnp.where(live_ref[j, t] != 0, scores, -jnp.inf)
                    score_ref[t] = scores
                    highest = jnp.maximum(highest, scores)
                highest = jnp.max(highest, axis=1, keepdims=True)
                total = jnp.zeros((ROWS, ROWS), jnp.float32)
                for t in range(key_blocks):
                    weights = jnp.exp(score_ref[t] - highest)
                    score_ref[t] = weights
                    total = total + weights
                total = jnp.sum(total, axis=1, keepdims=True)
                context = jnp.zeros((ROWS, LANES), jnp.float32)
                for t in range(key_blocks):
                    probs = (score_ref[t] / total).astype(jnp.bfloat16)
                    context = context + jnp.dot(
                        probs, key_block(t, vcols), preferred_element_type=jnp.float32
                    )
                merged = jnp.where(mine, context, merged)
            out_ref[j, :, kcols] = merged.astype(jnp.bfloat16)


def attention(live, pick, query, own, part):
    blocks_here, rows, head_feats = query.shape
    key_blocks = live.shape[1]
    vmem = pltpu.VMEM
    flops = 8 * blocks_here * rows * key_blocks * rows * head_feats
    moved = 2 * (query.size * 2 + own.size + part.size)
    return pl.pallas_call(
        attention_kernel,
        out_shape=jax.ShapeDtypeStruct(query.shape, jnp.bfloat16),
        in_specs=[pl.BlockSpec(memory_space=pltpu.SMEM), pl.BlockSpec(memory_space=pltpu.SMEM),
                  pl.BlockSpec(memory_space=vmem), pl.BlockSpec(memory_space=vmem), pl.BlockSpec(memory_space=vmem)],
        out_specs=pl.BlockSpec(memory_space=vmem),
        scratch_shapes=[pltpu.VMEM((key_blocks, ROWS, ROWS), jnp.float32)],
        cost_estimate=pl.CostEstimate(
            flops=flops, transcendentals=blocks_here * rows * key_blocks * rows * 4, bytes_accessed=moved
        ),
    )(live, pick, query, own, part)

def local(node_states, w_qkv, w_out, ln_gain, ln_bias, local_mask, matchings):
    total_rows, model_width = node_states.shape
    blocks_here = total_rows // ROWS
    head_feats = w_qkv.shape[2]
    heads_here = head_feats // HEAD_DIM
    window = 2 * REACH + 1
    matches = matchings.shape[0]
    inv_root = 1.0 / math.sqrt(HEAD_DIM)
    my_index = lax.axis_index("node")
    groups = lax.axis_size("node")
    all_blocks = groups * blocks_here
    heads_axis = lax.axis_size("head")
    head_index = lax.axis_index("head")
    out_cols = ln_gain.shape[0]
    w_parts = [lax.dynamic_slice_in_dim(w_out, head_index * out_cols, out_cols, 1)] + [
        flip_heads(
            lax.dynamic_slice_in_dim(w_out, (head_index ^ flip) * out_cols, out_cols, 1),
            flip,
            heads_axis,
        )
        for flip in range(1, heads_axis)
    ]
    projected = jnp.einsum(
        "nd,dtf->ntf", node_states, w_qkv, preferred_element_type=jnp.float32
    ).astype(jnp.bfloat16)
    queries = projected[:, 0]
    keyvals = projected[:, 1:].reshape(total_rows, 2 * head_feats)
    global_blocks = my_index * blocks_here + jnp.arange(blocks_here, dtype=jnp.int32)
    offsets = jnp.arange(window, dtype=jnp.int32) - REACH
    neighbour = global_blocks[:, None] + offsets[None, :]
    if groups <= GATHER_GROUPS:
        w_kv = w_qkv[:, 1:].reshape(model_width, 2 * head_feats)
        part, w_parts = quarter_keys(
            node_states, w_kv, w_parts, matchings, my_index, groups, blocks_here
        )
    else:
        part = routed_keys(keyvals, matchings, my_index, groups, blocks_here)
    local_ok = (
        (neighbour >= 0) & (neighbour < all_blocks) & ((offsets[None, :] == 0) | (local_mask == 1))
    )
    block_ok = jnp.concatenate([local_ok, jnp.ones((blocks_here, matches), dtype=bool)], axis=1)
    context = attention(
        block_ok.astype(jnp.int32),
        (matchings % blocks_here).astype(jnp.int32),
        queries.reshape(blocks_here, ROWS, head_feats),
        keyvals.reshape(blocks_here, ROWS, 2 * head_feats),
        part.reshape(part.shape[0], blocks_here, ROWS, 2 * head_feats),
    ).reshape(total_rows, head_feats)
    context_slots = spread_slots(context, heads_axis)
    own_cols = lax.dynamic_slice_in_dim(node_states, head_index * out_cols, out_cols, 1)
    mixed_rows = own_cols.astype(jnp.float32) + jnp.einsum(
        "srf,sfo->ro",
        jnp.stack([context_slots[flip] for flip in range(heads_axis)]),
        jnp.stack(w_parts),
        preferred_element_type=jnp.float32,
    )
    part_mean = jnp.mean(mixed_rows, axis=1, keepdims=True)
    part_square = jnp.sum(jnp.square(mixed_rows - part_mean), axis=1, keepdims=True)
    stats = jnp.concatenate([part_mean, part_square], axis=1)
    all_stats = jnp.stack(
        [stats] + [flip_heads(stats, flip, heads_axis) for flip in range(1, heads_axis)]
    )
    centre = jnp.mean(all_stats[:, :, 0:1], axis=0)
    spread = (
        jnp.sum(all_stats[:, :, 1:2], axis=0)
        + out_cols * jnp.sum(jnp.square(all_stats[:, :, 0:1] - centre), axis=0)
    ) / (heads_axis * out_cols)
    normed = (mixed_rows - centre) * lax.rsqrt(spread + NORM_EPS)
    return (normed * ln_gain + ln_bias).astype(jnp.bfloat16)


def solution(mesh):
    placed = (
        P("node", None),
        P(None, None, "head"),
        P("head", None),
        P("head"),
        P("head"),
        P("node", None),
        P(None, "node"),
    )
    return jax.shard_map(
        local, mesh=mesh, in_specs=placed, out_specs=P("node", "head"), check_vma=False
    )
```

```python
import math

import jax
import jax.numpy as jnp
from jax import lax
from jax.experimental import pallas as pl
from jax.experimental.pallas import tpu as pltpu
from jax.sharding import PartitionSpec as P

HEAD_DIM = 64
ROWS = 128
REACH = 3
LANES = 128
GATHER_GROUPS = 16
STATIC_GROUPS = 8
NEAR_SHIFTS = (1, 3)


NORM_EPS = 1e-05


def partner(array, axis, bit):
    return lax.ppermute(array, axis, [(i, i ^ 1 << bit) for i in range(lax.axis_size(axis))])


def flip_heads(array, flip, devices):
    return lax.ppermute(array, "head", [(i, i ^ flip) for i in range(devices)])


def spread_slots(piece, heads_axis):
    slots = {0: piece}
    for bit in reversed(range(heads_axis.bit_length() - 1)):
        flip = 1 << bit
        held = sorted(slots)
        other = flip_heads(jnp.stack([slots[k] for k in held]), flip, heads_axis)
        for pos, k in enumerate(held):
            slots[k ^ flip] = other[pos]
    return slots


def keep_same(current):
    return current


def route_direct(payload, shift_val, digits):
    for bit_pos in range(digits):

        def moved(current, bit_pos=bit_pos):
            return partner(current, "node", bit_pos)

        taken = jnp.bitwise_and(jnp.right_shift(shift_val, bit_pos), 1) == 1
        payload = lax.cond(taken, moved, keep_same, payload)
    return payload


def routed_keys(keyvals, matchings, my_index, groups, blocks_here):
    matches = matchings.shape[0]
    digits = groups.bit_length() - 1
    up = [(i, i + 1) for i in range(groups - 1)]
    down = [(i + 1, i) for i in range(groups - 1)]
    before = lax.ppermute(keyvals, "node", up)
    after = lax.ppermute(keyvals, "node", down)
    targets = jnp.bitwise_xor(matchings[:, 0] // blocks_here, my_index)
    received = [route_direct(keyvals, targets[match_pos], digits) for match_pos in range(matches)]
    return jnp.stack([before, after] + received)


def switched_send(payload, shift_val, groups):
    def branch(shift):
        def moved(current):
            return lax.ppermute(current, "node", [(i, i ^ shift) for i in range(groups)])

        return moved

    branches = [branch(shift) for shift in range(1, groups)]
    return lax.switch(jnp.clip(shift_val - 1, 0, groups - 2), branches, payload)


def quarter_keys(node_states, w_kv, w_parts, matchings, my_index, groups, blocks_here):
    total_rows, model_width = node_states.shape
    matches = matchings.shape[0]
    heads_axis = lax.axis_size("head")
    sub_rows = ROWS // heads_axis
    me = lax.axis_index("head")
    mine = node_states.reshape(blocks_here, heads_axis, sub_rows, model_width)
    mine = lax.dynamic_index_in_dim(mine, me, axis=1, keepdims=False)
    mine = mine.reshape(blocks_here * sub_rows, model_width)
    targets = jnp.bitwise_xor(matchings[:, 0] // blocks_here, my_index)
    if groups <= STATIC_GROUPS:
        return static_keys(
            node_states, mine, w_kv, w_parts, targets, my_index, groups, blocks_here, sub_rows
        )
    up = [(i, i + 1) for i in range(groups - 1)]
    down = [(i + 1, i) for i in range(groups - 1)]
    before = lax.ppermute(mine, "node", up)
    after = lax.ppermute(mine, "node", down)
    matched = [switched_send(mine, targets[match_pos], groups) for match_pos in range(matches)]
    w_parts, matched[0] = lax.optimization_barrier((w_parts, matched[0]))
    spread = [spread_stack(piece, heads_axis) for piece in [before, after] + matched]
    return kv_of_spread(spread, w_kv, blocks_here, sub_rows), w_parts


def static_keys(
    node_states, mine, w_kv, w_parts, targets, my_index, groups, blocks_here, sub_rows
):
    heads_axis = lax.axis_size("head")
    matches = targets.shape[0]
    far = [(j, j + 1) for j in range(1, groups - 1, 2)] + [(j, j - 1) for j in range(2, groups, 2)]
    other = spread_stack(lax.ppermute(mine, "node", far), heads_axis)
    near = near_rows(node_states, blocks_here, sub_rows)
    every = jnp.stack(
        [
            pair_stack(
                lax.ppermute(near, "node", [(i, i ^ shift) for i in range(groups)]), heads_axis
            )
            if shift in NEAR_SHIFTS and heads_axis == 4
            else spread_stack(
                lax.ppermute(mine, "node", [(i, i ^ shift) for i in range(groups)]), heads_axis
            )
            for shift in range(1, groups)
        ]
    )
    odd = (my_index % 2) == 1
    before = jnp.where(odd, every[0], other)
    after = jnp.where(odd, other, every[0])
    matched = [
        lax.dynamic_index_in_dim(
            every, jnp.clip(targets[match_pos] - 1, 0, groups - 2), 0, keepdims=False
        )
        for match_pos in range(matches)
    ]
    w_parts, matched[0] = lax.optimization_barrier((w_parts, matched[0]))
    return kv_of_spread([before, after] + matched, w_kv, blocks_here, sub_rows), w_parts


def near_rows(node_states, blocks_here, sub_rows):
    model_width = node_states.shape[1]
    me = lax.axis_index("head")
    parts = node_states.reshape(blocks_here, 4, sub_rows, model_width)
    return jnp.stack(
        [
            lax.dynamic_index_in_dim(parts, me ^ flip, axis=1, keepdims=False).reshape(
                blocks_here * sub_rows, model_width
            )
            for flip in (0, 2)
        ]
    )


def pair_stack(received, heads_axis):
    beside = flip_heads(received, 1, heads_axis)
    return jnp.stack([received[0], beside[0], received[1], beside[1]])


def spread_stack(piece, heads_axis):
    slots = spread_slots(piece, heads_axis)
    return jnp.stack([slots[k] for k in range(heads_axis)])


def kv_of_spread(spread, w_kv, blocks_here, sub_rows):
    heads_axis, _, model_width = spread[0].shape
    rows = jnp.stack(
        [
            jnp.transpose(one.reshape(heads_axis, blocks_here, sub_rows, model_width), (1, 0, 2, 3))
            for one in spread
        ]
    )
    count = len(spread)
    total_rows = blocks_here * heads_axis * sub_rows
    rows = rows.reshape(count * total_rows, model_width)
    partner_kv = jnp.dot(rows, w_kv, preferred_element_type=jnp.float32).astype(jnp.bfloat16)
    return partner_kv.reshape(count, total_rows, w_kv.shape[1])


def attention_kernel(live_ref, pick_ref, q_ref, own_ref, part_ref, out_ref, score_ref):
    blocks_here = q_ref.shape[0]
    head_feats = q_ref.shape[2]
    pairs = head_feats // LANES
    per_pair = LANES // HEAD_DIM
    window = 2 * REACH + 1
    matches = part_ref.shape[0] - 2
    key_blocks = window + matches
    inv_root = 1.0 / math.sqrt(HEAD_DIM)
    lane = lax.broadcasted_iota(jnp.int32, (ROWS, LANES), 1)
    for j in range(blocks_here):

        def key_block(t, cols, j=j):
            if t < window:
                pos = j + t - REACH
                if pos < 0:
                    return part_ref[0, pos + blocks_here, :, cols]
                if pos < blocks_here:
                    return own_ref[pos, :, cols]
                return part_ref[1, pos - blocks_here, :, cols]
            match_pos = t - window
            return part_ref[2 + match_pos, pick_ref[match_pos, j], :, cols]

        for pair in range(pairs):
            kcols = pl.ds(pair * LANES, LANES)
            vcols = pl.ds(head_feats + pair * LANES, LANES)
            both = q_ref[j, :, kcols]
            merged = jnp.zeros((ROWS, LANES), jnp.float32)
            for half in range(per_pair):
                mine = (lane >= half * HEAD_DIM) & (lane < (half + 1) * HEAD_DIM)
                query = jnp.where(mine, both, jnp.zeros_like(both))
                highest = jnp.full((ROWS, ROWS), -jnp.inf, jnp.float32)
                for t in range(key_blocks):
                    scores = lax.dot_general(
                        query, key_block(t, kcols), (((1,), (1,)), ((), ())),
                        preferred_element_type=jnp.float32,
                    ) * inv_root
                    scores = jnp.where(live_ref[j, t] != 0, scores, -jnp.inf)
                    score_ref[t] = scores
                    highest = jnp.maximum(highest, scores)
                highest = jnp.max(highest, axis=1, keepdims=True)
                total = jnp.zeros((ROWS, ROWS), jnp.float32)
                for t in range(key_blocks):
                    weights = jnp.exp(score_ref[t] - highest)
                    score_ref[t] = weights
                    total = total + weights
                total = jnp.sum(total, axis=1, keepdims=True)
                context = jnp.zeros((ROWS, LANES), jnp.float32)
                for t in range(key_blocks):
                    probs = (score_ref[t] / total).astype(jnp.bfloat16)
                    context = context + jnp.dot(
                        probs, key_block(t, vcols), preferred_element_type=jnp.float32
                    )
                merged = jnp.where(mine, context, merged)
            out_ref[j, :, kcols] = merged.astype(jnp.bfloat16)


def attention(live, pick, query, own, part):
    blocks_here, rows, head_feats = query.shape
    key_blocks = live.shape[1]
    vmem = pltpu.VMEM
    flops = 8 * blocks_here * rows * key_blocks * rows * head_feats
    moved = 2 * (query.size * 2 + own.size + part.size)
    return pl.pallas_call(
        attention_kernel,
        out_shape=jax.ShapeDtypeStruct(query.shape, jnp.bfloat16),
        in_specs=[pl.BlockSpec(memory_space=pltpu.SMEM), pl.BlockSpec(memory_space=pltpu.SMEM),
                  pl.BlockSpec(memory_space=vmem), pl.BlockSpec(memory_space=vmem), pl.BlockSpec(memory_space=vmem)],
        out_specs=pl.BlockSpec(memory_space=vmem),
        scratch_shapes=[pltpu.VMEM((key_blocks, ROWS, ROWS), jnp.float32)],
        cost_estimate=pl.CostEstimate(
            flops=flops, transcendentals=blocks_here * rows * key_blocks * rows * 4, bytes_accessed=moved
        ),
    )(live, pick, query, own, part)

def local(node_states, w_qkv, w_out, ln_gain, ln_bias, local_mask, matchings):
    total_rows, model_width = node_states.shape
    blocks_here = total_rows // ROWS
    head_feats = w_qkv.shape[2]
    heads_here = head_feats // HEAD_DIM
    window = 2 * REACH + 1
    matches = matchings.shape[0]
    inv_root = 1.0 / math.sqrt(HEAD_DIM)
    my_index = lax.axis_index("node")
    groups = lax.axis_size("node")
    all_blocks = groups * blocks_here
    heads_axis = lax.axis_size("head")
    head_index = lax.axis_index("head")
    out_cols = ln_gain.shape[0]
    w_parts = [lax.dynamic_slice_in_dim(w_out, head_index * out_cols, out_cols, 1)] + [
        flip_heads(
            lax.dynamic_slice_in_dim(w_out, (head_index ^ flip) * out_cols, out_cols, 1),
            flip,
            heads_axis,
        )
        for flip in range(1, heads_axis)
    ]
    projected = jnp.einsum(
        "nd,dtf->ntf", node_states, w_qkv, preferred_element_type=jnp.float32
    ).astype(jnp.bfloat16)
    queries = projected[:, 0]
    keyvals = projected[:, 1:].reshape(total_rows, 2 * head_feats)
    global_blocks = my_index * blocks_here + jnp.arange(blocks_here, dtype=jnp.int32)
    offsets = jnp.arange(window, dtype=jnp.int32) - REACH
    neighbour = global_blocks[:, None] + offsets[None, :]
    if groups <= GATHER_GROUPS:
        w_kv = w_qkv[:, 1:].reshape(model_width, 2 * head_feats)
        part, w_parts = quarter_keys(
            node_states, w_kv, w_parts, matchings, my_index, groups, blocks_here
        )
    else:
        part = routed_keys(keyvals, matchings, my_index, groups, blocks_here)
    local_ok = (
        (neighbour >= 0) & (neighbour < all_blocks) & ((offsets[None, :] == 0) | (local_mask == 1))
    )
    block_ok = jnp.concatenate([local_ok, jnp.ones((blocks_here, matches), dtype=bool)], axis=1)
    context = attention(
        block_ok.astype(jnp.int32),
        (matchings % blocks_here).astype(jnp.int32),
        queries.reshape(blocks_here, ROWS, head_feats),
        keyvals.reshape(blocks_here, ROWS, 2 * head_feats),
        part.reshape(part.shape[0], blocks_here, ROWS, 2 * head_feats),
    ).reshape(total_rows, head_feats)
    context_slots = spread_slots(context, heads_axis)
    own_cols = lax.dynamic_slice_in_dim(node_states, head_index * out_cols, out_cols, 1)
    mixed_rows = own_cols.astype(jnp.float32) + jnp.einsum(
        "srf,sfo->ro",
        jnp.stack([context_slots[flip] for flip in range(heads_axis)]),
        jnp.stack(w_parts),
        preferred_element_type=jnp.float32,
    )
    part_mean = jnp.mean(mixed_rows, axis=1, keepdims=True)
    part_square = jnp.sum(jnp.square(mixed_rows - part_mean), axis=1, keepdims=True)
    stats = jnp.concatenate([part_mean, part_square], axis=1)
    all_stats = jnp.stack(
        [stats] + [flip_heads(stats, flip, heads_axis) for flip in range(1, heads_axis)]
    )
    centre = jnp.mean(all_stats[:, :, 0:1], axis=0)
    spread = (
        jnp.sum(all_stats[:, :, 1:2], axis=0)
        + out_cols * jnp.sum(jnp.square(all_stats[:, :, 0:1] - centre), axis=0)
    ) / (heads_axis * out_cols)
    normed = (mixed_rows - centre) * lax.rsqrt(spread + NORM_EPS)
    return (normed * ln_gain + ln_bias).astype(jnp.bfloat16)


def solution(mesh):
    placed = (
        P("node", None),
        P(None, None, "head"),
        P("head", None),
        P("head"),
        P("head"),
        P("node", None),
        P(None, "node"),
    )
    return jax.shard_map(
        local, mesh=mesh, in_specs=placed, out_specs=P("node", "head"), check_vma=False
    )
```
